32 devices in a mesh: leaf: 8 (over z, x), couple: 4 (over y, core).
Axes of the slice: x: 2, y: 2, z: 4, core: 2. Of those that a mesh axis runs over, the one named last changes fastest.
Arguments:
- charges: bfloat16 [2048, 64, 128], P(('leaf', 'couple')), may hold values from -6 to 6
- leaf_basis: bfloat16 [131072, 64], P(('leaf', 'couple')), may hold values from -0.75 to 0.75
- transfer: bfloat16 [131072, 64], P(('leaf', 'couple')), may hold values from -0.75 to 0.75
- near_blocks: bfloat16 [131072, 768], P(('leaf', 'couple')), may hold values from -0.21875 to 0.21875
- near_source: int32 [24576], P(('leaf', 'couple')), may hold values from 0 to 71, as said below
- couple_fine: bfloat16 [131072, 1024], P(('leaf', 'couple')), may hold values from -0.1875 to 0.1875
- source_fine: int32 [32768], P(('leaf', 'couple')), may hold values from 0 to 255, as said below
- couple_coarse: bfloat16 [65536, 1024], P(('leaf', 'couple')), may hold values from -0.1875 to 0.1875
- source_coarse: int32 [16384], P(('leaf', 'couple')), may hold values from 0 to 127, as said below
- send_fine: int32 [32, 192], P(('leaf', 'couple')), may hold values from 0 to 63
- send_coarse: int32 [32, 96], P(('leaf', 'couple')), may hold values from 0 to 31
Outputs:
- product: bfloat16 [2048, 64, 128], P(('leaf', 'couple'))
The draws below stay inside these ranges and needn't reach their ends.
Inputs may be any that keep to these rules, and one draw needn't show every extreme that they name: `source_fine`: entry k of a device's part belongs to leaf cluster k // 16 of that device. A value 64 + q * 32 + m appears only where the owner d - o_q exists, and on every device each such value appears at least once. `source_coarse`: entry k of a device's part belongs to parent cluster k // 16 of that device. A value 64 / 2 + q * 16 + m appears only where the owner d - o_q exists, and on every device each such value appears at least once. `near_source`: entry k of a device's part belongs to leaf k // 12 of that device and names a place in the device's leaves extended by 4 leaves on each side (own leaf t at place t + 4), at most 4 places from its own leaf; the first three entries of each leaf name the leaf itself and the leaves 4 before and 4 after it.
All inputs are finite; a program needn't handle non-finite values.
Results may differ from the reference program's by a relative error of at most 0.0063.
Values may be sent and summed in bfloat16 or wider, within the bound.
No kernel may reach another device: no remote copies, remote signals or barrier semaphores. Data moves between devices by JAX's collectives and lax.ppermute only.
A program may use at most 128 MiB of HBM per device.

```python
import jax
import jax.numpy as jnp
from jax import lax

LEAF = 64
RANK = 64
RHS = 128
LEAF_DEV = 64
CPL = 16
NEAR = 12
HALO = 4
REACH = 3
SEND_FINE = 32
SEND_COARSE = 16
DEVS = 32
NLEAF = 2048


def coupling_sources(key, local, each):
    count = local * CPL
    slots = 2 * REACH * each
    subkeys = jax.random.split(key, DEVS)
    devices = jnp.arange(DEVS, dtype=jnp.int32)

    def per_device(subkey, device):
        first, second, third = jax.random.split(subkey, 3)
        slot = jnp.arange(slots, dtype=jnp.int32)
        which = slot // each
        offset = jnp.where(which % 2 == 0, which // 2 + 1, -(which // 2 + 1))
        owner = device - offset
        valid = jnp.logical_and(owner >= 0, owner < DEVS)
        order = jax.random.permutation(first, count).astype(jnp.int32)
        spread = jax.random.randint(second, (count,), 0, local + slots).astype(jnp.int32)
        fallback = jax.random.randint(third, (count,), 0, local).astype(jnp.int32)
        spread_ok = jnp.logical_or(spread < local, valid[jnp.clip(spread - local, 0, slots - 1)])
        spread = jnp.where(spread_ok, spread, fallback)
        order_ok = valid[jnp.clip(order, 0, slots - 1)]
        planted = jnp.logical_and(order < slots, order_ok)
        return jnp.where(planted, local + order, spread).astype(jnp.int32)
    return jax.vmap(per_device)(subkeys, devices).reshape(-1)


def draw_source_fine(key, part):
    return coupling_sources(jax.random.fold_in(key, 11), LEAF_DEV, SEND_FINE)


def draw_source_coarse(key, part):
    return coupling_sources(jax.random.fold_in(key, 23), LEAF_DEV // 2, SEND_COARSE)


def draw_near_source(key, part):
    positions = jnp.arange(LEAF_DEV * NEAR, dtype=jnp.int32)
    target = positions // NEAR
    column = positions % NEAR
    offsets = jax.random.randint(jax.random.fold_in(key, 37), (DEVS, LEAF_DEV * NEAR), -HALO, HALO + 1)
    offsets = jnp.where(column == 0, 0, jnp.where(column == 1, -HALO, jnp.where(column == 2, HALO, offsets)))
    return (target + HALO + offsets).astype(jnp.int32).reshape(-1)


def with_ends(drawn, stream_key, least, top_value):
    dims = drawn.shape
    place = [jax.random.randint(jax.random.fold_in(stream_key, axis), (), 0, dims[axis]) for axis in range(len(dims))]
    drawn = drawn.at[tuple(place)].set(least)
    longest = dims.index(max(dims))
    place[longest] = (place[longest] + 1) % dims[longest]
    return drawn.at[tuple(place)].set(top_value)


def block_scale(stream_key, dims, shards, least, high):
    def one(axis_at, blocks):
        heights = jax.random.uniform(jax.random.fold_in(jax.random.fold_in(stream_key, 6), axis_at), (blocks,), jnp.float32, least / len(shards), high / len(shards))
        return jnp.repeat(jnp.exp(heights), dims[axis_at] // blocks).reshape((-1,) + (1,) * (len(dims) - axis_at - 1))

    level = one(*shards[0])
    for cut in shards[1:]:
        level = level * one(*cut)
    return level


def noise(own_key, dims, scale, most, cuts=(), kind=jnp.bfloat16):
    drawn = jax.random.normal(own_key, dims, jnp.float32) * scale
    if len(cuts) > 0:
        drawn = block_scale(own_key, dims, cuts, -0.22, 0.18) * drawn
    return jnp.clip(drawn, min=-most, max=most).astype(kind)


def setup_inputs(seed: int = 0) -> dict:
    key_list = jax.random.split(jax.random.key(seed), 12)
    return {
        "charges": noise(key_list[0], (NLEAF, LEAF, RHS), 1.0, 6.0, ((0, 32),)),
        "leaf_basis": noise(key_list[1], (NLEAF * LEAF, RANK), LEAF ** -0.5, 0.75, ((0, 32),)),
        "transfer": noise(key_list[2], (NLEAF * RANK, RANK), RANK ** -0.5, 0.75, ((0, 32),)),
        "near_blocks": noise(key_list[3], (NLEAF * LEAF, NEAR * LEAF), (LEAF * NEAR) ** -0.5, 0.21875, ((0, 32),)),
        "near_source": draw_near_source(jax.random.fold_in(key_list[11], 71), 0),
        "couple_fine": noise(key_list[5], (NLEAF * RANK, CPL * RANK), (RANK * CPL) ** -0.5, 0.1875, ((0, 32),)),
        "source_fine": draw_source_fine(jax.random.fold_in(key_list[11], 71), 0),
        "couple_coarse": noise(key_list[7], (NLEAF // 2 * RANK, CPL * RANK), (RANK * CPL) ** -0.5, 0.1875, ((0, 32),)),
        "source_coarse": draw_source_coarse(jax.random.fold_in(key_list[11], 71), 0),
        "send_fine": with_ends(jax.random.randint(key_list[9], (DEVS, 2 * REACH * SEND_FINE), 0, LEAF_DEV), jax.random.fold_in(key_list[9], 1), 0, LEAF_DEV - 1).astype(jnp.int32),
        "send_coarse": with_ends(jax.random.randint(key_list[10], (DEVS, 2 * REACH * SEND_COARSE), 0, LEAF_DEV // 2), jax.random.fold_in(key_list[10], 1), 0, (LEAF_DEV // 2) - 1).astype(jnp.int32),
    }


def offset_list():
    values = []
    for step in range(REACH):
        values.append(step + 1)
        values.append(-(step + 1))
    return values


def reference(charges, leaf_basis, transfer, near_blocks, near_source, couple_fine, source_fine, couple_coarse, source_coarse, send_fine, send_coarse):
    leaves = LEAF_DEV * DEVS
    points = charges.astype(jnp.float32)
    leaf_bases = leaf_basis.reshape(leaves, LEAF, RANK).astype(jnp.float32)
    fine_coeffs = jnp.einsum("nlr,nlc->nrc", leaf_bases, points).astype(jnp.bfloat16)
    stacked = transfer.reshape(leaves // 2, 2 * RANK, RANK).astype(jnp.float32)
    pairs_view = fine_coeffs.reshape(leaves // 2, 2 * RANK, RHS).astype(jnp.float32)
    coarse_coeffs = jnp.einsum("pab,par->pbr", stacked, pairs_view).astype(jnp.bfloat16)
    padded = jnp.pad(charges, ((HALO, HALO), (0, 0), (0, 0)))

    def pooled(coeffs, sends, device, local, each):
        parts = [lax.dynamic_slice_in_dim(coeffs, device * local, local, 0)]
        for slot, offset in enumerate(offset_list()):
            owner = device - offset
            valid = jnp.logical_and(owner >= 0, owner < DEVS)
            safe = jnp.clip(owner, 0, DEVS - 1).astype(jnp.int32)
            row = lax.dynamic_index_in_dim(sends, safe, 0, keepdims=False)
            picks = row[slot * each:(slot + 1) * each].astype(jnp.int32)
            got = coeffs[(safe * local + picks).astype(jnp.int32)]
            parts.append(jnp.where(valid, got, jnp.zeros_like(got)))
        return jnp.concatenate(parts, 0)

    def coupled(blocks, sources, source_pool, clusters, device):
        matrices = lax.dynamic_slice_in_dim(blocks, device * clusters * RANK, clusters * RANK, 0).reshape(clusters, RANK, CPL * RANK).astype(jnp.float32)
        chosen = lax.dynamic_slice_in_dim(sources, device * clusters * CPL, clusters * CPL, 0).astype(jnp.int32)
        picked = source_pool[chosen].reshape(clusters, CPL * RANK, RHS).astype(jnp.float32)
        return jnp.einsum("tak,tkr->tar", matrices, picked)

    def one_device(device):
        half = LEAF_DEV // 2
        fine_target = coupled(couple_fine, source_fine, pooled(fine_coeffs, send_fine, device, LEAF_DEV, SEND_FINE), LEAF_DEV, device)
        coarse_target = coupled(couple_coarse, source_coarse, pooled(coarse_coeffs, send_coarse, device, half, SEND_COARSE), half, device)
        coarse_round = lax.optimization_barrier(coarse_target.astype(jnp.bfloat16)).astype(jnp.float32)
        local_stack = lax.dynamic_slice_in_dim(stacked, device * half, half, 0)
        fine_total = fine_target + jnp.einsum("pab,pbr->par", local_stack, coarse_round).reshape(LEAF_DEV, RANK, RHS)
        fine_round = lax.optimization_barrier(fine_total.astype(jnp.bfloat16)).astype(jnp.float32)
        local_bases = lax.dynamic_slice_in_dim(leaf_bases, device * LEAF_DEV, LEAF_DEV, 0)
        far_field = jnp.einsum("nlr,nrc->nlc", local_bases, fine_round)
        window = lax.dynamic_slice_in_dim(padded, device * LEAF_DEV, LEAF_DEV + 2 * HALO, 0)
        count = LEAF_DEV * NEAR
        chosen = lax.dynamic_slice_in_dim(near_source, device * count, count, 0).astype(jnp.int32)
        nearby = window[chosen].reshape(LEAF_DEV, NEAR * LEAF, RHS).astype(jnp.float32)
        near_mats = lax.dynamic_slice_in_dim(near_blocks, device * LEAF_DEV * LEAF, LEAF_DEV * LEAF, 0).reshape(LEAF_DEV, LEAF, NEAR * LEAF).astype(jnp.float32)
        near_field = jnp.einsum("nik,nkr->nir", near_mats, nearby)
        return (far_field + near_field).astype(jnp.bfloat16)

    result = lax.map(one_device, jnp.arange(DEVS, dtype=jnp.int32))
    return result.reshape(leaves, LEAF, RHS)
```

```python
import functools

import jax
import jax.numpy as jnp
from jax import lax
from jax.experimental import pallas as pl
from jax.experimental.pallas import tpu as pltpu
from jax.sharding import PartitionSpec as P

LEAF = 64
RANK = 64
RHS = 128
HALO = 4
REACH = 3
BLOCK_TARGETS = 8


def from_behind(value, axis, steps):
    count = lax.axis_size(axis)
    first, last = (max(0, -steps), min(count, count - steps))
    return lax.ppermute(value, axis, [(source, source + steps) for source in range(first, last)])


def halo_pieces(block, axis, width):
    count = lax.axis_size(axis)
    forward = [(i, i + 1) for i in range(count - 1)]
    backward = [(target, source) for source, target in forward]
    low = lax.ppermute(lax.slice_in_dim(block, block.shape[0] - width, None, axis=0), axis, forward)
    high = lax.ppermute(lax.slice_in_dim(block, 0, width, axis=0), axis, backward)
    return low, high


def offset_list():
    values = []
    for step in range(REACH):
        values.append(step + 1)
        values.append(-(step + 1))
    return values


def gather_dot(idx, mats, segments, pairs, epilogue=None):
    rows = mats.shape[0]
    width = mats.shape[1] // pairs
    targets = rows // LEAF
    tb = min(BLOCK_TARGETS, targets)
    steps = targets // tb
    n_seg = len(segments)
    seg_arrays = [s[0] for s in segments]
    seg_meta = [(s[1], s[2], s[3]) for s in segments]

    in_specs = [pl.BlockSpec((tb * LEAF, pairs * width), lambda i, ix: (i, 0))]
    for arr in seg_arrays:
        in_specs.append(pl.BlockSpec(arr.shape, lambda i, ix: (0, 0, 0)))
    extra = []
    if epilogue is not None:
        extra, extra_specs, _, out_dtype = epilogue
        in_specs.extend(extra_specs)
    else:
        out_dtype = jnp.float32

    def kernel(idx_ref, mats_ref, *refs):
        seg_refs = refs[:n_seg]
        extra_refs = refs[n_seg:len(refs) - 2]
        out_ref = refs[len(refs) - 2]
        g_ref = refs[len(refs) - 1]
        blk = pl.program_id(0)

        def per_target(tt, carry):
            base = (blk * tb + tt) * pairs

            def per_pair(k, c):
                s = idx_ref[base + k]
                dst = pl.multiple_of(k * width, width)
                for ref, (lo, cnt, row) in zip(seg_refs, seg_meta):
                    @pl.when(jnp.logical_and(s >= lo, s < lo + cnt))
                    def _():
                        at = jnp.clip(s - lo, 0, cnt - 1) + row
                        g_ref[pl.ds(dst, width), :] = ref[at]
                return c

            lax.fori_loop(0, pairs, per_pair, 0)
            r0 = pl.multiple_of(tt * LEAF, LEAF)
            acc = jnp.dot(mats_ref[pl.ds(r0, LEAF), :], g_ref[...], preferred_element_type=jnp.float32)
            if epilogue is None:
                out_ref[tt] = acc
            else:
                out_ref[tt] = epilogue[2](tt, acc, extra_refs)
            return carry

        lax.fori_loop(0, tb, per_target, 0)

    grid_spec = pltpu.PrefetchScalarGridSpec(
        num_scalar_prefetch=1,
        grid=(steps,),
        in_specs=in_specs,
        out_specs=pl.BlockSpec((tb, LEAF, RHS), lambda i, ix: (i, 0, 0)),
        scratch_shapes=[pltpu.VMEM((pairs * width, RHS), jnp.bfloat16)],
    )
    flops = 2 * rows * pairs * width * RHS
    bytes_accessed = mats.size * 2 + sum(a.size * 2 for a in seg_arrays) + targets * LEAF * RHS * 4
    return pl.pallas_call(
        kernel,
        grid_spec=grid_spec,
        out_shape=jax.ShapeDtypeStruct((targets, LEAF, RHS), out_dtype),
        compiler_params=pltpu.CompilerParams(dimension_semantics=("arbitrary",)),
        cost_estimate=pl.CostEstimate(flops=flops, transcendentals=0, bytes_accessed=bytes_accessed),
    )(idx, mats, *seg_arrays, *extra)


def on_device(
    charges,
    leaf_basis,
    transfer,
    near_blocks,
    near_source,
    couple_fine,
    source_fine,
    couple_coarse,
    source_coarse,
    send_fine,
    send_coarse,
):
    leaves = charges.shape[0]
    parents = leaves // 2
    fine_each = send_fine.shape[1] // (2 * REACH)
    coarse_each = send_coarse.shape[1] // (2 * REACH)
    axis = ("leaf", "couple")
    leaf_bases = leaf_basis.reshape(leaves, LEAF, RANK)
    fine_coeffs = jnp.einsum(
        "nlr,nlc->nrc", leaf_bases, charges, preferred_element_type=jnp.float32
    ).astype(jnp.bfloat16)
    stacked = transfer.reshape(parents, 2 * RANK, RANK)
    coarse_coeffs = jnp.einsum(
        "pab,par->pbr",
        stacked,
        fine_coeffs.reshape(parents, 2 * RANK, RHS),
        preferred_element_type=jnp.float32,
    ).astype(jnp.bfloat16)
    fine_out = fine_coeffs[send_fine[0]].reshape(2 * REACH, fine_each, RANK, RHS)
    coarse_out = coarse_coeffs[send_coarse[0]].reshape(2 * REACH, coarse_each, RANK, RHS)
    packets = jnp.concatenate([fine_out, coarse_out], 1)
    incoming = []
    for slot, offset in enumerate(offset_list()):
        incoming.append(from_behind(packets[slot], axis, offset))

    low, high = halo_pieces(charges, axis, HALO)
    near_field = gather_dot(
        near_source,
        near_blocks,
        [(low, 0, HALO, 0), (charges, HALO, leaves, 0), (high, HALO + leaves, HALO, 0)],
        near_source.shape[0] // leaves,
    )

    coarse_segments = [(coarse_coeffs, 0, parents, 0)]
    for slot in range(2 * REACH):
        coarse_segments.append((incoming[slot], parents + slot * coarse_each, coarse_each, fine_each))
    coarse_target = gather_dot(
        source_coarse, couple_coarse, coarse_segments, source_coarse.shape[0] // parents
    )
    coarse_round = coarse_target.astype(jnp.bfloat16)

    fine_segments = [(fine_coeffs, 0, leaves, 0)]
    for slot in range(2 * REACH):
        fine_segments.append((incoming[slot], leaves + slot * fine_each, fine_each, 0))

    tb = min(BLOCK_TARGETS, leaves)

    def finish(tt, acc, refs):
        cr_ref, e_ref, v_ref, near_ref = refs
        r0 = pl.multiple_of(tt * LEAF, LEAF)
        down = jnp.dot(e_ref[pl.ds(r0, RANK), :], cr_ref[tt // 2], preferred_element_type=jnp.float32)
        fine_round = (acc + down).astype(jnp.bfloat16)
        far = jnp.dot(v_ref[pl.ds(r0, LEAF), :], fine_round, preferred_element_type=jnp.float32)
        return (far + near_ref[tt]).astype(jnp.bfloat16)

    epilogue = (
        [coarse_round, transfer, leaf_basis, near_field],
        [
            pl.BlockSpec((tb // 2, RANK, RHS), lambda i, ix: (i, 0, 0)),
            pl.BlockSpec((tb * RANK, RANK), lambda i, ix: (i, 0)),
            pl.BlockSpec((tb * LEAF, RANK), lambda i, ix: (i, 0)),
            pl.BlockSpec((tb, LEAF, RHS), lambda i, ix: (i, 0, 0)),
        ],
        finish,
        jnp.bfloat16,
    )
    return gather_dot(
        source_fine, couple_fine, fine_segments, source_fine.shape[0] // leaves, epilogue
    )


def solution(mesh):
    return jax.shard_map(
        on_device,
        mesh=mesh,
        in_specs=(
            P(("leaf", "couple"), None, None),
            P(("leaf", "couple"), None),
            P(("leaf", "couple"), None),
            P(("leaf", "couple"), None),
            P(("leaf", "couple")),
            P(("leaf", "couple"), None),
            P(("leaf", "couple")),
            P(("leaf", "couple"), None),
            P(("leaf", "couple")),
            P(("leaf", "couple"), None),
            P(("leaf", "couple"), None),
        ),
        out_specs=P(("leaf", "couple"), None, None),
        check_vma=False,
    )
```

```python
import functools

import jax
import jax.numpy as jnp
from jax import lax
from jax.experimental import pallas as pl
from jax.experimental.pallas import tpu as pltpu
from jax.sharding import PartitionSpec as P

LEAF = 64
RANK = 64
RHS = 128
HALO = 4
REACH = 3
BLOCK_TARGETS = 8


def from_behind(value, axis, steps):
    count = lax.axis_size(axis)
    first, last = (max(0, -steps), min(count, count - steps))
    return lax.ppermute(value, axis, [(source, source + steps) for source in range(first, last)])


def halo_pieces(block, axis, width):
    count = lax.axis_size(axis)
    forward = [(i, i + 1) for i in range(count - 1)]
    backward = [(target, source) for source, target in forward]
    low = lax.ppermute(lax.slice_in_dim(block, block.shape[0] - width, None, axis=0), axis, forward)
    high = lax.ppermute(lax.slice_in_dim(block, 0, width, axis=0), axis, backward)
    return low, high


def offset_list():
    values = []
    for step in range(REACH):
        values.append(step + 1)
        values.append(-(step + 1))
    return values


def gather_dot(idx, mats, segments, pairs, epilogue=None):
    rows = mats.shape[0]
    width = mats.shape[1] // pairs
    targets = rows // LEAF
    tb = min(BLOCK_TARGETS, targets)
    steps = targets // tb
    n_seg = len(segments)
    seg_arrays = [s[0] for s in segments]
    seg_meta = [(s[1], s[2], s[3]) for s in segments]
    total = sum(s[2] for s in segments)

    in_specs = [pl.BlockSpec((tb * LEAF, pairs * width), lambda i, ix: (i, 0))]
    for arr in seg_arrays:
        in_specs.append(pl.BlockSpec(memory_space=pl.ANY))
    extra = []
    if epilogue is not None:
        extra, extra_specs, _, out_dtype = epilogue
        in_specs.extend(extra_specs)
    else:
        out_dtype = jnp.float32

    def kernel(idx_ref, mats_ref, *refs):
        seg_refs = refs[:n_seg]
        extra_refs = refs[n_seg:len(refs) - 4]
        out_ref, g_ref, pool_ref, sem = refs[len(refs) - 4:]
        blk = pl.program_id(0)

        @pl.when(blk == 0)
        def _():
            copies = []
            for j, (ref, (lo, cnt, row)) in enumerate(zip(seg_refs, seg_meta)):
                cp = pltpu.make_async_copy(ref.at[pl.ds(row, cnt)], pool_ref.at[pl.ds(lo, cnt)], sem.at[j])
                cp.start()
                copies.append(cp)
            for cp in copies:
                cp.wait()

        def per_target(tt, carry):
            base = (blk * tb + tt) * pairs
            for k in range(pairs):
                s = jnp.clip(idx_ref[base + k], 0, total - 1)
                g_ref[k * width:(k + 1) * width, :] = pool_ref[s]
            r0 = pl.multiple_of(tt * LEAF, LEAF)
            acc = jnp.dot(mats_ref[pl.ds(r0, LEAF), :], g_ref[...], preferred_element_type=jnp.float32)
            if epilogue is None:
                out_ref[tt] = acc
            else:
                out_ref[tt] = epilogue[2](tt, acc, extra_refs)
            return carry

        lax.fori_loop(0, tb, per_target, 0)

    grid_spec = pltpu.PrefetchScalarGridSpec(
        num_scalar_prefetch=1,
        grid=(steps,),
        in_specs=in_specs,
        out_specs=pl.BlockSpec((tb, LEAF, RHS), lambda i, ix: (i, 0, 0)),
        scratch_shapes=[
            pltpu.VMEM((pairs * width, RHS), jnp.bfloat16),
            pltpu.VMEM((total, width, RHS), jnp.bfloat16),
            pltpu.SemaphoreType.DMA((n_seg,)),
        ],
    )
    flops = 2 * rows * pairs * width * RHS
    bytes_accessed = mats.size * 2 + total * width * RHS * 2 + targets * LEAF * RHS * 4
    return pl.pallas_call(
        kernel,
        grid_spec=grid_spec,
        out_shape=jax.ShapeDtypeStruct((targets, LEAF, RHS), out_dtype),
        compiler_params=pltpu.CompilerParams(dimension_semantics=("arbitrary",)),
        cost_estimate=pl.CostEstimate(flops=flops, transcendentals=0, bytes_accessed=bytes_accessed),
    )(idx, mats, *seg_arrays, *extra)


def on_device(
    charges,
    leaf_basis,
    transfer,
    near_blocks,
    near_source,
    couple_fine,
    source_fine,
    couple_coarse,
    source_coarse,
    send_fine,
    send_coarse,
):
    leaves = charges.shape[0]
    parents = leaves // 2
    fine_each = send_fine.shape[1] // (2 * REACH)
    coarse_each = send_coarse.shape[1] // (2 * REACH)
    axis = ("leaf", "couple")
    leaf_bases = leaf_basis.reshape(leaves, LEAF, RANK)
    fine_coeffs = jnp.einsum(
        "nlr,nlc->nrc", leaf_bases, charges, preferred_element_type=jnp.float32
    ).astype(jnp.bfloat16)
    stacked = transfer.reshape(parents, 2 * RANK, RANK)
    coarse_coeffs = jnp.einsum(
        "pab,par->pbr",
        stacked,
        fine_coeffs.reshape(parents, 2 * RANK, RHS),
        preferred_element_type=jnp.float32,
    ).astype(jnp.bfloat16)
    fine_out = fine_coeffs[send_fine[0]].reshape(2 * REACH, fine_each, RANK, RHS)
    coarse_out = coarse_coeffs[send_coarse[0]].reshape(2 * REACH, coarse_each, RANK, RHS)
    packets = jnp.concatenate([fine_out, coarse_out], 1)
    incoming = []
    for slot, offset in enumerate(offset_list()):
        incoming.append(from_behind(packets[slot], axis, offset))

    low, high = halo_pieces(charges, axis, HALO)
    near_field = gather_dot(
        near_source,
        near_blocks,
        [(low, 0, HALO, 0), (charges, HALO, leaves, 0), (high, HALO + leaves, HALO, 0)],
        near_source.shape[0] // leaves,
    )

    coarse_segments = [(coarse_coeffs, 0, parents, 0)]
    for slot in range(2 * REACH):
        coarse_segments.append((incoming[slot], parents + slot * coarse_each, coarse_each, fine_each))
    coarse_target = gather_dot(
        source_coarse, couple_coarse, coarse_segments, source_coarse.shape[0] // parents
    )
    coarse_round = coarse_target.astype(jnp.bfloat16)

    fine_segments = [(fine_coeffs, 0, leaves, 0)]
    for slot in range(2 * REACH):
        fine_segments.append((incoming[slot], leaves + slot * fine_each, fine_each, 0))

    tb = min(BLOCK_TARGETS, leaves)

    def finish(tt, acc, refs):
        cr_ref, e_ref, v_ref, near_ref = refs
        r0 = pl.multiple_of(tt * LEAF, LEAF)
        down = jnp.dot(e_ref[pl.ds(r0, RANK), :], cr_ref[tt // 2], preferred_element_type=jnp.float32)
        fine_round = (acc + down).astype(jnp.bfloat16)
        far = jnp.dot(v_ref[pl.ds(r0, LEAF), :], fine_round, preferred_element_type=jnp.float32)
        return (far + near_ref[tt]).astype(jnp.bfloat16)

    epilogue = (
        [coarse_round, transfer, leaf_basis, near_field],
        [
            pl.BlockSpec((tb // 2, RANK, RHS), lambda i, ix: (i, 0, 0)),
            pl.BlockSpec((tb * RANK, RANK), lambda i, ix: (i, 0)),
            pl.BlockSpec((tb * LEAF, RANK), lambda i, ix: (i, 0)),
            pl.BlockSpec((tb, LEAF, RHS), lambda i, ix: (i, 0, 0)),
        ],
        finish,
        jnp.bfloat16,
    )
    return gather_dot(
        source_fine, couple_fine, fine_segments, source_fine.shape[0] // leaves, epilogue
    )


def solution(mesh):
    return jax.shard_map(
        on_device,
        mesh=mesh,
        in_specs=(
            P(("leaf", "couple"), None, None),
            P(("leaf", "couple"), None),
            P(("leaf", "couple"), None),
            P(("leaf", "couple"), None),
            P(("leaf", "couple")),
            P(("leaf", "couple"), None),
            P(("leaf", "couple")),
            P(("leaf", "couple"), None),
            P(("leaf", "couple")),
            P(("leaf", "couple"), None),
            P(("leaf", "couple"), None),
        ),
        out_specs=P(("leaf", "couple"), None, None),
        check_vma=False,
    )
```

```python
import functools

import jax
import jax.numpy as jnp
from jax import lax
from jax.experimental import pallas as pl
from jax.experimental.pallas import tpu as pltpu
from jax.sharding import PartitionSpec as P

LEAF = 64
RANK = 64
RHS = 128
HALO = 4
REACH = 3
BLOCK_TARGETS = 8


def from_behind(value, axis, steps):
    count = lax.axis_size(axis)
    first, last = (max(0, -steps), min(count, count - steps))
    return lax.ppermute(value, axis, [(source, source + steps) for source in range(first, last)])


def halo_pieces(block, axis, width):
    count = lax.axis_size(axis)
    forward = [(i, i + 1) for i in range(count - 1)]
    backward = [(target, source) for source, target in forward]
    low = lax.ppermute(lax.slice_in_dim(block, block.shape[0] - width, None, axis=0), axis, forward)
    high = lax.ppermute(lax.slice_in_dim(block, 0, width, axis=0), axis, backward)
    return low, high


def offset_list():
    values = []
    for step in range(REACH):
        values.append(step + 1)
        values.append(-(step + 1))
    return values


def gather_dot(idx, mats, segments, pairs, epilogue=None):
    rows = mats.shape[0]
    width = mats.shape[1] // pairs
    targets = rows // LEAF
    tb = min(BLOCK_TARGETS, targets)
    steps = targets // tb
    n_seg = len(segments)
    seg_arrays = [s[0] for s in segments]
    seg_meta = [(s[1], s[2], s[3]) for s in segments]
    total = sum(s[2] for s in segments)

    in_specs = [pl.BlockSpec((tb * LEAF, pairs * width), lambda i, ix: (i, 0))]
    for arr in seg_arrays:
        in_specs.append(pl.BlockSpec(memory_space=pl.ANY))
    extra = []
    if epilogue is not None:
        extra, extra_specs, _, out_dtype = epilogue
        in_specs.extend(extra_specs)
    else:
        out_dtype = jnp.float32

    def kernel(idx_ref, mats_ref, *refs):
        seg_refs = refs[:n_seg]
        extra_refs = refs[n_seg:len(refs) - 4]
        out_ref, g_ref, pool_ref, sem = refs[len(refs) - 4:]
        blk = pl.program_id(0)

        @pl.when(blk == 0)
        def _():
            copies = []
            for j, (ref, (lo, cnt, row)) in enumerate(zip(seg_refs, seg_meta)):
                cp = pltpu.make_async_copy(ref.at[pl.ds(row, cnt)], pool_ref.at[pl.ds(lo, cnt)], sem.at[j])
                cp.start()
                copies.append(cp)
            for cp in copies:
                cp.wait()

        for tt in range(tb):
            base = (blk * tb + tt) * pairs
            for k in range(pairs):
                s = jnp.clip(idx_ref[base + k], 0, total - 1)
                g_ref[tt, k * width:(k + 1) * width, :] = pool_ref[s]
            acc = jnp.dot(mats_ref[tt * LEAF:(tt + 1) * LEAF, :], g_ref[tt], preferred_element_type=jnp.float32)
            if epilogue is None:
                out_ref[tt] = acc
            else:
                out_ref[tt] = epilogue[2](tt, acc, extra_refs)

    grid_spec = pltpu.PrefetchScalarGridSpec(
        num_scalar_prefetch=1,
        grid=(steps,),
        in_specs=in_specs,
        out_specs=pl.BlockSpec((tb, LEAF, RHS), lambda i, ix: (i, 0, 0)),
        scratch_shapes=[
            pltpu.VMEM((tb, pairs * width, RHS), jnp.bfloat16),
            pltpu.VMEM((total, width, RHS), jnp.bfloat16),
            pltpu.SemaphoreType.DMA((n_seg,)),
        ],
    )
    flops = 2 * rows * pairs * width * RHS
    bytes_accessed = mats.size * 2 + total * width * RHS * 2 + targets * LEAF * RHS * 4
    return pl.pallas_call(
        kernel,
        grid_spec=grid_spec,
        out_shape=jax.ShapeDtypeStruct((targets, LEAF, RHS), out_dtype),
        compiler_params=pltpu.CompilerParams(dimension_semantics=("arbitrary",)),
        cost_estimate=pl.CostEstimate(flops=flops, transcendentals=0, bytes_accessed=bytes_accessed),
    )(idx, mats, *seg_arrays, *extra)


def upward(charges, basis_t, transfer_t, send_fine, send_coarse, fine_each, coarse_each):
    leaves = charges.shape[0]
    parents = leaves // 2
    slots = 2 * REACH
    each = fine_each + coarse_each

    def kernel(sf_ref, sc_ref, x_ref, v_ref, e_ref, fine_ref, coarse_ref, *packet_refs):
        def per_parent(j, c):
            col = pl.multiple_of(j * 2 * RANK, 2 * RANK)
            v = v_ref[:, pl.ds(col, 2 * RANK)]
            f0 = jnp.dot(v[:, :RANK], x_ref[2 * j], preferred_element_type=jnp.float32).astype(jnp.bfloat16)
            f1 = jnp.dot(v[:, RANK:], x_ref[2 * j + 1], preferred_element_type=jnp.float32).astype(jnp.bfloat16)
            fine_ref[2 * j] = f0
            fine_ref[2 * j + 1] = f1
            e = e_ref[:, pl.ds(col, 2 * RANK)]
            pair = jnp.concatenate([f0, f1], axis=0)
            coarse_ref[j] = jnp.dot(e, pair, preferred_element_type=jnp.float32).astype(jnp.bfloat16)
            return c

        lax.fori_loop(0, parents, per_parent, 0)

        for q in range(slots):
            out = packet_refs[q]

            def fine_pick(m, c):
                out[m] = fine_ref[jnp.clip(sf_ref[q * fine_each + m], 0, leaves - 1)]
                return c

            def coarse_pick(m, c):
                out[fine_each + m] = coarse_ref[jnp.clip(sc_ref[q * coarse_each + m], 0, parents - 1)]
                return c

            lax.fori_loop(0, fine_each, fine_pick, 0)
            lax.fori_loop(0, coarse_each, coarse_pick, 0)

    smem = pl.BlockSpec(memory_space=pltpu.SMEM)
    vmem = pl.BlockSpec(memory_space=pltpu.VMEM)
    block = jax.ShapeDtypeStruct
    outs = pl.pallas_call(
        kernel,
        in_specs=[smem, smem, vmem, vmem, vmem],
        out_specs=[vmem] * (2 + slots),
        out_shape=[block((leaves, RANK, RHS), jnp.bfloat16), block((parents, RANK, RHS), jnp.bfloat16)]
        + [block((each, RANK, RHS), jnp.bfloat16)] * slots,
        cost_estimate=pl.CostEstimate(
            flops=2 * leaves * LEAF * RANK * RHS * 2, transcendentals=0, bytes_accessed=16 * 2 ** 20
        ),
    )(send_fine, send_coarse, charges, basis_t, transfer_t)
    return outs[0], outs[1], outs[2:]


def on_device(
    charges,
    leaf_basis,
    transfer,
    near_blocks,
    near_source,
    couple_fine,
    source_fine,
    couple_coarse,
    source_coarse,
    send_fine,
    send_coarse,
):
    leaves = charges.shape[0]
    parents = leaves // 2
    fine_each = send_fine.shape[1] // (2 * REACH)
    coarse_each = send_coarse.shape[1] // (2 * REACH)
    axis = ("leaf", "couple")
    basis_t = leaf_basis.T
    transfer_t = transfer.T
    fine_coeffs, coarse_coeffs, packets = upward(
        charges, basis_t, transfer_t, send_fine[0], send_coarse[0], fine_each, coarse_each
    )
    incoming = []
    for slot, offset in enumerate(offset_list()):
        incoming.append(from_behind(packets[slot], axis, offset))

    low, high = halo_pieces(charges, axis, HALO)
    near_field = gather_dot(
        near_source,
        near_blocks,
        [(low, 0, HALO, 0), (charges, HALO, leaves, 0), (high, HALO + leaves, HALO, 0)],
        near_source.shape[0] // leaves,
    )

    coarse_segments = [(coarse_coeffs, 0, parents, 0)]
    for slot in range(2 * REACH):
        coarse_segments.append((incoming[slot], parents + slot * coarse_each, coarse_each, fine_each))
    coarse_target = gather_dot(
        source_coarse, couple_coarse, coarse_segments, source_coarse.shape[0] // parents
    )
    coarse_round = coarse_target.astype(jnp.bfloat16)

    fine_segments = [(fine_coeffs, 0, leaves, 0)]
    for slot in range(2 * REACH):
        fine_segments.append((incoming[slot], leaves + slot * fine_each, fine_each, 0))

    tb = min(BLOCK_TARGETS, leaves)

    def finish(tt, acc, refs):
        cr_ref, e_ref, v_ref, near_ref = refs
        lhs_t = (((0,), (0,)), ((), ()))
        e_t = e_ref[:, tt * RANK:(tt + 1) * RANK]
        down = lax.dot_general(e_t, cr_ref[tt // 2], lhs_t, preferred_element_type=jnp.float32)
        fine_round = (acc + down).astype(jnp.bfloat16)
        v_t = v_ref[:, tt * LEAF:(tt + 1) * LEAF]
        far = lax.dot_general(v_t, fine_round, lhs_t, preferred_element_type=jnp.float32)
        return (far + near_ref[tt]).astype(jnp.bfloat16)

    epilogue = (
        [coarse_round, transfer_t, basis_t, near_field],
        [
            pl.BlockSpec((tb // 2, RANK, RHS), lambda i, ix: (i, 0, 0)),
            pl.BlockSpec((RANK, tb * RANK), lambda i, ix: (0, i)),
            pl.BlockSpec((RANK, tb * LEAF), lambda i, ix: (0, i)),
            pl.BlockSpec((tb, LEAF, RHS), lambda i, ix: (i, 0, 0)),
        ],
        finish,
        jnp.bfloat16,
    )
    return gather_dot(
        source_fine, couple_fine, fine_segments, source_fine.shape[0] // leaves, epilogue
    )


def solution(mesh):
    return jax.shard_map(
        on_device,
        mesh=mesh,
        in_specs=(
            P(("leaf", "couple"), None, None),
            P(("leaf", "couple"), None),
            P(("leaf", "couple"), None),
            P(("leaf", "couple"), None),
            P(("leaf", "couple")),
            P(("leaf", "couple"), None),
            P(("leaf", "couple")),
            P(("leaf", "couple"), None),
            P(("leaf", "couple")),
            P(("leaf", "couple"), None),
            P(("leaf", "couple"), None),
        ),
        out_specs=P(("leaf", "couple"), None, None),
        check_vma=False,
    )
```

```python
import functools

import jax
import jax.numpy as jnp
from jax import lax
from jax.experimental import pallas as pl
from jax.experimental.pallas import tpu as pltpu
from jax.sharding import PartitionSpec as P

LEAF = 64
RANK = 64
RHS = 128
HALO = 4
REACH = 3
BLOCK_TARGETS = 8


def from_behind(value, axis, steps):
    count = lax.axis_size(axis)
    first, last = (max(0, -steps), min(count, count - steps))
    return lax.ppermute(value, axis, [(source, source + steps) for source in range(first, last)])


def halo_pieces(block, axis, width):
    count = lax.axis_size(axis)
    forward = [(i, i + 1) for i in range(count - 1)]
    backward = [(target, source) for source, target in forward]
    low = lax.ppermute(lax.slice_in_dim(block, block.shape[0] - width, None, axis=0), axis, forward)
    high = lax.ppermute(lax.slice_in_dim(block, 0, width, axis=0), axis, backward)
    return low, high


def offset_list():
    values = []
    for step in range(REACH):
        values.append(step + 1)
        values.append(-(step + 1))
    return values


def gather_dot(idx, mats, segments, pairs, epilogue=None, out_dtype=jnp.float32):
    rows = mats.shape[0]
    width = mats.shape[1] // pairs
    targets = rows // LEAF
    tb = min(BLOCK_TARGETS, targets)
    steps = targets // tb
    n_seg = len(segments)
    seg_arrays = [s[0] for s in segments]
    seg_meta = [(s[1], s[2], s[3]) for s in segments]
    total = sum(s[2] for s in segments)

    in_specs = [pl.BlockSpec((tb * LEAF, pairs * width), lambda i, ix: (i, 0))]
    for arr in seg_arrays:
        in_specs.append(pl.BlockSpec(memory_space=pl.ANY))
    extra = []
    if epilogue is not None:
        extra, extra_specs, _, out_dtype = epilogue
        in_specs.extend(extra_specs)

    def kernel(idx_ref, mats_ref, *refs):
        seg_refs = refs[:n_seg]
        extra_refs = refs[n_seg:len(refs) - 4]
        out_ref, g_ref, pool_ref, sem = refs[len(refs) - 4:]
        blk = pl.program_id(0)

        @pl.when(blk == 0)
        def _():
            copies = []
            for j, (ref, (lo, cnt, row)) in enumerate(zip(seg_refs, seg_meta)):
                cp = pltpu.make_async_copy(ref.at[pl.ds(row, cnt)], pool_ref.at[pl.ds(lo, cnt)], sem.at[j])
                cp.start()
                copies.append(cp)
            for cp in copies:
                cp.wait()

        for tt in range(tb):
            base = (blk * tb + tt) * pairs
            for k in range(pairs):
                s = jnp.clip(idx_ref[base + k], 0, total - 1)
                g_ref[tt, k * width:(k + 1) * width, :] = pool_ref[s]
            acc = jnp.dot(mats_ref[tt * LEAF:(tt + 1) * LEAF, :], g_ref[tt], preferred_element_type=jnp.float32)
            if epilogue is None:
                out_ref[tt] = acc.astype(out_dtype)
            else:
                out_ref[tt] = epilogue[2](tt, acc, extra_refs)

    grid_spec = pltpu.PrefetchScalarGridSpec(
        num_scalar_prefetch=1,
        grid=(steps,),
        in_specs=in_specs,
        out_specs=pl.BlockSpec((tb, LEAF, RHS), lambda i, ix: (i, 0, 0)),
        scratch_shapes=[
            pltpu.VMEM((tb, pairs * width, RHS), jnp.bfloat16),
            pltpu.VMEM((total, width, RHS), jnp.bfloat16),
            pltpu.SemaphoreType.DMA((n_seg,)),
        ],
    )
    flops = 2 * rows * pairs * width * RHS
    bytes_accessed = mats.size * 2 + total * width * RHS * 2 + targets * LEAF * RHS * 4
    return pl.pallas_call(
        kernel,
        grid_spec=grid_spec,
        out_shape=jax.ShapeDtypeStruct((targets, LEAF, RHS), out_dtype),
        compiler_params=pltpu.CompilerParams(dimension_semantics=("arbitrary",)),
        cost_estimate=pl.CostEstimate(flops=flops, transcendentals=0, bytes_accessed=bytes_accessed),
    )(idx, mats, *seg_arrays, *extra)


def upward(charges, basis_t, transfer_t, send_fine, send_coarse, fine_each, coarse_each):
    leaves = charges.shape[0]
    parents = leaves // 2
    slots = 2 * REACH
    each = fine_each + coarse_each

    def kernel(sf_ref, sc_ref, x_ref, v_ref, e_ref, fine_out, coarse_out, *rest):
        packet_refs = rest[:slots]
        fine_v, coarse_v, sem = rest[slots:]
        for j in range(parents):
            col = j * 2 * RANK
            f0 = jnp.dot(v_ref[:, col:col + RANK], x_ref[2 * j], preferred_element_type=jnp.float32)
            f1 = jnp.dot(v_ref[:, col + RANK:col + 2 * RANK], x_ref[2 * j + 1], preferred_element_type=jnp.float32)
            pair = jnp.concatenate([f0.astype(jnp.bfloat16), f1.astype(jnp.bfloat16)], axis=0)
            fine_v[2 * j] = pair[:RANK]
            fine_v[2 * j + 1] = pair[RANK:]
            e = e_ref[:, col:col + 2 * RANK]
            coarse_v[j] = jnp.dot(e, pair, preferred_element_type=jnp.float32).astype(jnp.bfloat16)

        whole = [
            pltpu.make_async_copy(fine_v, fine_out, sem.at[0]),
            pltpu.make_async_copy(coarse_v, coarse_out, sem.at[1]),
        ]
        for cp in whole:
            cp.start()

        def picks(q, m, start):
            base = 2 + q * each + m
            if start:
                if m < fine_each:
                    s = jnp.clip(sf_ref[q * fine_each + m], 0, leaves - 1)
                    src = fine_v.at[s]
                else:
                    s = jnp.clip(sc_ref[q * coarse_each + m - fine_each], 0, parents - 1)
                    src = coarse_v.at[s]
            else:
                src = fine_v.at[0]
            return pltpu.make_async_copy(src, packet_refs[q].at[m], sem.at[base])

        for q in range(slots):
            for m in range(each):
                picks(q, m, True).start()
        for cp in whole:
            cp.wait()
        for q in range(slots):
            for m in range(each):
                picks(q, m, False).wait()

    smem = pl.BlockSpec(memory_space=pltpu.SMEM)
    vmem = pl.BlockSpec(memory_space=pltpu.VMEM)
    hbm = pl.BlockSpec(memory_space=pl.ANY)
    block = jax.ShapeDtypeStruct
    outs = pl.pallas_call(
        kernel,
        in_specs=[smem, smem, vmem, vmem, vmem],
        out_specs=[hbm] * (2 + slots),
        out_shape=[block((leaves, RANK, RHS), jnp.bfloat16), block((parents, RANK, RHS), jnp.bfloat16)]
        + [block((each, RANK, RHS), jnp.bfloat16)] * slots,
        scratch_shapes=[
            pltpu.VMEM((leaves, RANK, RHS), jnp.bfloat16),
            pltpu.VMEM((parents, RANK, RHS), jnp.bfloat16),
            pltpu.SemaphoreType.DMA((2 + slots * each,)),
        ],
        cost_estimate=pl.CostEstimate(
            flops=2 * leaves * LEAF * RANK * RHS * 2, transcendentals=0, bytes_accessed=16 * 2 ** 20
        ),
    )(send_fine, send_coarse, charges, basis_t, transfer_t)
    return outs[0], outs[1], outs[2:]


def on_device(
    charges,
    leaf_basis,
    transfer,
    near_blocks,
    near_source,
    couple_fine,
    source_fine,
    couple_coarse,
    source_coarse,
    send_fine,
    send_coarse,
):
    leaves = charges.shape[0]
    parents = leaves // 2
    fine_each = send_fine.shape[1] // (2 * REACH)
    coarse_each = send_coarse.shape[1] // (2 * REACH)
    axis = ("leaf", "couple")
    basis_t = leaf_basis.T
    transfer_t = transfer.T
    fine_coeffs, coarse_coeffs, packets = upward(
        charges, basis_t, transfer_t, send_fine[0], send_coarse[0], fine_each, coarse_each
    )
    incoming = []
    for slot, offset in enumerate(offset_list()):
        incoming.append(from_behind(packets[slot], axis, offset))

    low, high = halo_pieces(charges, axis, HALO)
    near_field = gather_dot(
        near_source,
        near_blocks,
        [(low, 0, HALO, 0), (charges, HALO, leaves, 0), (high, HALO + leaves, HALO, 0)],
        near_source.shape[0] // leaves,
    )

    coarse_segments = [(coarse_coeffs, 0, parents, 0)]
    for slot in range(2 * REACH):
        coarse_segments.append((incoming[slot], parents + slot * coarse_each, coarse_each, fine_each))
    coarse_round = gather_dot(
        source_coarse, couple_coarse, coarse_segments, source_coarse.shape[0] // parents,
        out_dtype=jnp.bfloat16,
    )

    fine_segments = [(fine_coeffs, 0, leaves, 0)]
    for slot in range(2 * REACH):
        fine_segments.append((incoming[slot], leaves + slot * fine_each, fine_each, 0))

    tb = min(BLOCK_TARGETS, leaves)

    def finish(tt, acc, refs):
        cr_ref, e_ref, v_ref, near_ref = refs
        lhs_t = (((0,), (0,)), ((), ()))
        e_t = e_ref[:, tt * RANK:(tt + 1) * RANK]
        down = lax.dot_general(e_t, cr_ref[tt // 2], lhs_t, preferred_element_type=jnp.float32)
        fine_round = (acc + down).astype(jnp.bfloat16)
        v_t = v_ref[:, tt * LEAF:(tt + 1) * LEAF]
        far = lax.dot_general(v_t, fine_round, lhs_t, preferred_element_type=jnp.float32)
        return (far + near_ref[tt]).astype(jnp.bfloat16)

    epilogue = (
        [coarse_round, transfer_t, basis_t, near_field],
        [
            pl.BlockSpec((tb // 2, RANK, RHS), lambda i, ix: (i, 0, 0)),
            pl.BlockSpec((RANK, tb * RANK), lambda i, ix: (0, i)),
            pl.BlockSpec((RANK, tb * LEAF), lambda i, ix: (0, i)),
            pl.BlockSpec((tb, LEAF, RHS), lambda i, ix: (i, 0, 0)),
        ],
        finish,
        jnp.bfloat16,
    )
    return gather_dot(
        source_fine, couple_fine, fine_segments, source_fine.shape[0] // leaves, epilogue
    )


def solution(mesh):
    return jax.shard_map(
        on_device,
        mesh=mesh,
        in_specs=(
            P(("leaf", "couple"), None, None),
            P(("leaf", "couple"), None),
            P(("leaf", "couple"), None),
            P(("leaf", "couple"), None),
            P(("leaf", "couple")),
            P(("leaf", "couple"), None),
            P(("leaf", "couple")),
            P(("leaf", "couple"), None),
            P(("leaf", "couple")),
            P(("leaf", "couple"), None),
            P(("leaf", "couple"), None),
        ),
        out_specs=P(("leaf", "couple"), None, None),
        check_vma=False,
    )
```

```python
import functools

import jax
import jax.numpy as jnp
from jax import lax
from jax.experimental import pallas as pl
from jax.experimental.pallas import tpu as pltpu
from jax.sharding import PartitionSpec as P

LEAF = 64
RANK = 64
RHS = 128
HALO = 4
REACH = 3
BLOCK_TARGETS = 8


def from_behind(value, axis, steps):
    count = lax.axis_size(axis)
    first, last = (max(0, -steps), min(count, count - steps))
    return lax.ppermute(value, axis, [(source, source + steps) for source in range(first, last)])


def halo_pieces(block, axis, width):
    count = lax.axis_size(axis)
    forward = [(i, i + 1) for i in range(count - 1)]
    backward = [(target, source) for source, target in forward]
    low = lax.ppermute(lax.slice_in_dim(block, block.shape[0] - width, None, axis=0), axis, forward)
    high = lax.ppermute(lax.slice_in_dim(block, 0, width, axis=0), axis, backward)
    return low, high


def offset_list():
    values = []
    for step in range(REACH):
        values.append(step + 1)
        values.append(-(step + 1))
    return values


def gather_dot(idx, mats, segments, pairs, epilogue=None, out_dtype=jnp.float32):
    rows = mats.shape[0]
    width = mats.shape[1] // pairs
    targets = rows // LEAF
    tb = min(BLOCK_TARGETS, targets)
    steps = targets // tb
    n_seg = len(segments)
    seg_arrays = [s[0] for s in segments]
    seg_meta = [(s[1], s[2], s[3]) for s in segments]
    total = sum(s[2] for s in segments)

    in_specs = [pl.BlockSpec((tb * LEAF, pairs * width), lambda i, ix: (i, 0))]
    for arr in seg_arrays:
        in_specs.append(pl.BlockSpec(memory_space=pl.ANY))
    extra = []
    if epilogue is not None:
        extra, extra_specs, _, out_dtype = epilogue
        in_specs.extend(extra_specs)

    def kernel(idx_ref, mats_ref, *refs):
        seg_refs = refs[:n_seg]
        extra_refs = refs[n_seg:len(refs) - 3]
        out_ref, pool_ref, sem = refs[len(refs) - 3:]
        blk = pl.program_id(0)

        @pl.when(blk == 0)
        def _():
            copies = []
            for j, (ref, (lo, cnt, row)) in enumerate(zip(seg_refs, seg_meta)):
                cp = pltpu.make_async_copy(ref.at[pl.ds(row, cnt)], pool_ref.at[pl.ds(lo, cnt)], sem.at[j])
                cp.start()
                copies.append(cp)
            for cp in copies:
                cp.wait()

        for tt in range(tb):
            base = (blk * tb + tt) * pairs
            blocks = [pool_ref[jnp.clip(idx_ref[base + k], 0, total - 1)] for k in range(pairs)]
            rhs = jnp.concatenate(blocks, axis=0)
            acc = jnp.dot(mats_ref[tt * LEAF:(tt + 1) * LEAF, :], rhs, preferred_element_type=jnp.float32)
            if epilogue is None:
                out_ref[tt] = acc.astype(out_dtype)
            else:
                out_ref[tt] = epilogue[2](tt, acc, extra_refs)

    grid_spec = pltpu.PrefetchScalarGridSpec(
        num_scalar_prefetch=1,
        grid=(steps,),
        in_specs=in_specs,
        out_specs=pl.BlockSpec((tb, LEAF, RHS), lambda i, ix: (i, 0, 0)),
        scratch_shapes=[
            pltpu.VMEM((total, width, RHS), jnp.bfloat16),
            pltpu.SemaphoreType.DMA((n_seg,)),
        ],
    )
    flops = 2 * rows * pairs * width * RHS
    bytes_accessed = mats.size * 2 + total * width * RHS * 2 + targets * LEAF * RHS * 4
    return pl.pallas_call(
        kernel,
        grid_spec=grid_spec,
        out_shape=jax.ShapeDtypeStruct((targets, LEAF, RHS), out_dtype),
        compiler_params=pltpu.CompilerParams(dimension_semantics=("arbitrary",)),
        cost_estimate=pl.CostEstimate(flops=flops, transcendentals=0, bytes_accessed=bytes_accessed),
    )(idx, mats, *seg_arrays, *extra)


def upward(charges, basis_t, transfer_t, send_fine, send_coarse, fine_each, coarse_each):
    leaves = charges.shape[0]
    parents = leaves // 2
    slots = 2 * REACH
    each = fine_each + coarse_each

    def kernel(sf_ref, sc_ref, x_ref, v_ref, e_ref, fine_out, coarse_out, *rest):
        packet_refs = rest[:slots]
        fine_v, coarse_v, sem = rest[slots:]
        for j in range(parents):
            col = j * 2 * RANK
            f0 = jnp.dot(v_ref[:, col:col + RANK], x_ref[2 * j], preferred_element_type=jnp.float32)
            f1 = jnp.dot(v_ref[:, col + RANK:col + 2 * RANK], x_ref[2 * j + 1], preferred_element_type=jnp.float32)
            pair = jnp.concatenate([f0.astype(jnp.bfloat16), f1.astype(jnp.bfloat16)], axis=0)
            fine_v[2 * j] = pair[:RANK]
            fine_v[2 * j + 1] = pair[RANK:]
            e = e_ref[:, col:col + 2 * RANK]
            coarse_v[j] = jnp.dot(e, pair, preferred_element_type=jnp.float32).astype(jnp.bfloat16)

        whole = [
            pltpu.make_async_copy(fine_v, fine_out, sem.at[0]),
            pltpu.make_async_copy(coarse_v, coarse_out, sem.at[1]),
        ]
        for cp in whole:
            cp.start()

        def picks(q, m, start):
            base = 2 + q * each + m
            if start:
                if m < fine_each:
                    s = jnp.clip(sf_ref[q * fine_each + m], 0, leaves - 1)
                    src = fine_v.at[s]
                else:
                    s = jnp.clip(sc_ref[q * coarse_each + m - fine_each], 0, parents - 1)
                    src = coarse_v.at[s]
            else:
                src = fine_v.at[0]
            return pltpu.make_async_copy(src, packet_refs[q].at[m], sem.at[base])

        for q in range(slots):
            for m in range(each):
                picks(q, m, True).start()
        for cp in whole:
            cp.wait()
        for q in range(slots):
            for m in range(each):
                picks(q, m, False).wait()

    smem = pl.BlockSpec(memory_space=pltpu.SMEM)
    vmem = pl.BlockSpec(memory_space=pltpu.VMEM)
    hbm = pl.BlockSpec(memory_space=pl.ANY)
    block = jax.ShapeDtypeStruct
    outs = pl.pallas_call(
        kernel,
        in_specs=[smem, smem, vmem, vmem, vmem],
        out_specs=[hbm] * (2 + slots),
        out_shape=[block((leaves, RANK, RHS), jnp.bfloat16), block((parents, RANK, RHS), jnp.bfloat16)]
        + [block((each, RANK, RHS), jnp.bfloat16)] * slots,
        scratch_shapes=[
            pltpu.VMEM((leaves, RANK, RHS), jnp.bfloat16),
            pltpu.VMEM((parents, RANK, RHS), jnp.bfloat16),
            pltpu.SemaphoreType.DMA((2 + slots * each,)),
        ],
        cost_estimate=pl.CostEstimate(
            flops=2 * leaves * LEAF * RANK * RHS * 2, transcendentals=0, bytes_accessed=16 * 2 ** 20
        ),
    )(send_fine, send_coarse, charges, basis_t, transfer_t)
    return outs[0], outs[1], outs[2:]


def on_device(
    charges,
    leaf_basis,
    transfer,
    near_blocks,
    near_source,
    couple_fine,
    source_fine,
    couple_coarse,
    source_coarse,
    send_fine,
    send_coarse,
):
    leaves = charges.shape[0]
    parents = leaves // 2
    fine_each = send_fine.shape[1] // (2 * REACH)
    coarse_each = send_coarse.shape[1] // (2 * REACH)
    axis = ("leaf", "couple")
    basis_t = leaf_basis.T
    transfer_t = transfer.T
    fine_coeffs, coarse_coeffs, packets = upward(
        charges, basis_t, transfer_t, send_fine[0], send_coarse[0], fine_each, coarse_each
    )
    incoming = []
    for slot, offset in enumerate(offset_list()):
        incoming.append(from_behind(packets[slot], axis, offset))

    low, high = halo_pieces(charges, axis, HALO)
    near_field = gather_dot(
        near_source,
        near_blocks,
        [(low, 0, HALO, 0), (charges, HALO, leaves, 0), (high, HALO + leaves, HALO, 0)],
        near_source.shape[0] // leaves,
    )

    coarse_segments = [(coarse_coeffs, 0, parents, 0)]
    for slot in range(2 * REACH):
        coarse_segments.append((incoming[slot], parents + slot * coarse_each, coarse_each, fine_each))
    coarse_round = gather_dot(
        source_coarse, couple_coarse, coarse_segments, source_coarse.shape[0] // parents,
        out_dtype=jnp.bfloat16,
    )

    fine_segments = [(fine_coeffs, 0, leaves, 0)]
    for slot in range(2 * REACH):
        fine_segments.append((incoming[slot], leaves + slot * fine_each, fine_each, 0))

    tb = min(BLOCK_TARGETS, leaves)

    def finish(tt, acc, refs):
        cr_ref, e_ref, v_ref, near_ref = refs
        e = e_ref[tt * RANK:(tt + 1) * RANK, :]
        down = jnp.dot(e, cr_ref[tt // 2], preferred_element_type=jnp.float32)
        fine_round = (acc + down).astype(jnp.bfloat16)
        v = v_ref[tt * LEAF:(tt + 1) * LEAF, :]
        far = jnp.dot(v, fine_round, preferred_element_type=jnp.float32)
        return (far + near_ref[tt]).astype(jnp.bfloat16)

    epilogue = (
        [coarse_round, transfer, leaf_basis, near_field],
        [
            pl.BlockSpec((tb // 2, RANK, RHS), lambda i, ix: (i, 0, 0)),
            pl.BlockSpec((tb * RANK, RANK), lambda i, ix: (i, 0)),
            pl.BlockSpec((tb * LEAF, RANK), lambda i, ix: (i, 0)),
            pl.BlockSpec((tb, LEAF, RHS), lambda i, ix: (i, 0, 0)),
        ],
        finish,
        jnp.bfloat16,
    )
    return gather_dot(
        source_fine, couple_fine, fine_segments, source_fine.shape[0] // leaves, epilogue
    )


def solution(mesh):
    return jax.shard_map(
        on_device,
        mesh=mesh,
        in_specs=(
            P(("leaf", "couple"), None, None),
            P(("leaf", "couple"), None),
            P(("leaf", "couple"), None),
            P(("leaf", "couple"), None),
            P(("leaf", "couple")),
            P(("leaf", "couple"), None),
            P(("leaf", "couple")),
            P(("leaf", "couple"), None),
            P(("leaf", "couple")),
            P(("leaf", "couple"), None),
            P(("leaf", "couple"), None),
        ),
        out_specs=P(("leaf", "couple"), None, None),
        check_vma=False,
    )
```

```python
import functools

import jax
import jax.numpy as jnp
from jax import lax
from jax.experimental import pallas as pl
from jax.experimental.pallas import tpu as pltpu
from jax.sharding import PartitionSpec as P

LEAF = 64
RANK = 64
RHS = 128
HALO = 4
REACH = 3
BLOCK_TARGETS = 8


def from_behind(value, axis, steps):
    count = lax.axis_size(axis)
    first, last = (max(0, -steps), min(count, count - steps))
    return lax.ppermute(value, axis, [(source, source + steps) for source in range(first, last)])


def halo_pieces(block, axis, width):
    count = lax.axis_size(axis)
    forward = [(i, i + 1) for i in range(count - 1)]
    backward = [(target, source) for source, target in forward]
    low = lax.ppermute(lax.slice_in_dim(block, block.shape[0] - width, None, axis=0), axis, forward)
    high = lax.ppermute(lax.slice_in_dim(block, 0, width, axis=0), axis, backward)
    return low, high


def offset_list():
    values = []
    for step in range(REACH):
        values.append(step + 1)
        values.append(-(step + 1))
    return values


def gather_dot(idx, mats, segments, pairs, epilogue=None, out_dtype=jnp.float32):
    rows = mats.shape[0]
    width = mats.shape[1] // pairs
    targets = rows // LEAF
    tb = min(BLOCK_TARGETS, targets)
    steps = targets // tb
    n_seg = len(segments)
    seg_arrays = [s[0] for s in segments]
    seg_meta = [(s[1], s[2], s[3]) for s in segments]
    total = sum(s[2] for s in segments)

    in_specs = [pl.BlockSpec((tb * LEAF, pairs * width), lambda i, ix: (i, 0))]
    for arr in seg_arrays:
        in_specs.append(pl.BlockSpec(memory_space=pl.ANY))
    extra = []
    if epilogue is not None:
        extra, extra_specs, _, out_dtype = epilogue
        in_specs.extend(extra_specs)

    def kernel(idx_ref, mats_ref, *refs):
        seg_refs = refs[:n_seg]
        extra_refs = refs[n_seg:len(refs) - 3]
        out_ref, pool_ref, sem = refs[len(refs) - 3:]
        blk = pl.program_id(0)

        @pl.when(blk == 0)
        def _():
            copies = []
            for j, (ref, (lo, cnt, row)) in enumerate(zip(seg_refs, seg_meta)):
                cp = pltpu.make_async_copy(ref.at[pl.ds(row, cnt)], pool_ref.at[pl.ds(lo, cnt)], sem.at[j])
                cp.start()
                copies.append(cp)
            for cp in copies:
                cp.wait()

        for tt in range(tb):
            base = (blk * tb + tt) * pairs
            blocks = [pool_ref[jnp.clip(idx_ref[base + k], 0, total - 1)] for k in range(pairs)]
            rhs = jnp.concatenate(blocks, axis=0)
            acc = jnp.dot(mats_ref[tt * LEAF:(tt + 1) * LEAF, :], rhs, preferred_element_type=jnp.float32)
            if epilogue is None:
                out_ref[tt] = acc.astype(out_dtype)
            else:
                out_ref[tt] = epilogue[2](tt, acc, extra_refs)

    grid_spec = pltpu.PrefetchScalarGridSpec(
        num_scalar_prefetch=1,
        grid=(steps,),
        in_specs=in_specs,
        out_specs=pl.BlockSpec((tb, LEAF, RHS), lambda i, ix: (i, 0, 0)),
        scratch_shapes=[
            pltpu.VMEM((total, width, RHS), jnp.bfloat16),
            pltpu.SemaphoreType.DMA((n_seg,)),
        ],
    )
    flops = 2 * rows * pairs * width * RHS
    bytes_accessed = mats.size * 2 + total * width * RHS * 2 + targets * LEAF * RHS * 4
    return pl.pallas_call(
        kernel,
        grid_spec=grid_spec,
        out_shape=jax.ShapeDtypeStruct((targets, LEAF, RHS), out_dtype),
        compiler_params=pltpu.CompilerParams(dimension_semantics=("arbitrary",)),
        cost_estimate=pl.CostEstimate(flops=flops, transcendentals=0, bytes_accessed=bytes_accessed),
    )(idx, mats, *seg_arrays, *extra)


def upward(charges, basis_t, transfer_t, send_fine, send_coarse, fine_each, coarse_each):
    leaves = charges.shape[0]
    parents = leaves // 2
    slots = 2 * REACH
    each = fine_each + coarse_each

    def kernel(sf_ref, sc_ref, x_ref, v_ref, e_ref, fine_out, coarse_out, *rest):
        fine_refs = rest[:slots]
        coarse_refs = rest[slots:2 * slots]
        fine_v, coarse_v, sem = rest[2 * slots:]
        for j in range(parents):
            col = j * 2 * RANK
            f0 = jnp.dot(v_ref[:, col:col + RANK], x_ref[2 * j], preferred_element_type=jnp.float32)
            f1 = jnp.dot(v_ref[:, col + RANK:col + 2 * RANK], x_ref[2 * j + 1], preferred_element_type=jnp.float32)
            pair = jnp.concatenate([f0.astype(jnp.bfloat16), f1.astype(jnp.bfloat16)], axis=0)
            fine_v[2 * j] = pair[:RANK]
            fine_v[2 * j + 1] = pair[RANK:]
            e = e_ref[:, col:col + 2 * RANK]
            coarse_v[j] = jnp.dot(e, pair, preferred_element_type=jnp.float32).astype(jnp.bfloat16)

        whole = [
            pltpu.make_async_copy(fine_v, fine_out, sem.at[0]),
            pltpu.make_async_copy(coarse_v, coarse_out, sem.at[1]),
        ]
        for cp in whole:
            cp.start()

        def picks(q, m, start):
            base = 2 + q * each + m
            if m < fine_each:
                dst = fine_refs[q].at[m]
                s = jnp.clip(sf_ref[q * fine_each + m], 0, leaves - 1) if start else 0
                src = fine_v.at[s]
            else:
                dst = coarse_refs[q].at[m - fine_each]
                s = jnp.clip(sc_ref[q * coarse_each + m - fine_each], 0, parents - 1) if start else 0
                src = coarse_v.at[s]
            return pltpu.make_async_copy(src, dst, sem.at[base])

        for q in range(slots):
            for m in range(fine_each, each):
                picks(q, m, True).start()
        for q in range(slots):
            for m in range(fine_each):
                picks(q, m, True).start()
        for cp in whole:
            cp.wait()
        for q in range(slots):
            for m in range(each):
                picks(q, m, False).wait()

    smem = pl.BlockSpec(memory_space=pltpu.SMEM)
    vmem = pl.BlockSpec(memory_space=pltpu.VMEM)
    hbm = pl.BlockSpec(memory_space=pl.ANY)
    block = jax.ShapeDtypeStruct
    outs = pl.pallas_call(
        kernel,
        in_specs=[smem, smem, vmem, vmem, vmem],
        out_specs=[hbm] * (2 + 2 * slots),
        out_shape=[block((leaves, RANK, RHS), jnp.bfloat16), block((parents, RANK, RHS), jnp.bfloat16)]
        + [block((fine_each, RANK, RHS), jnp.bfloat16)] * slots
        + [block((coarse_each, RANK, RHS), jnp.bfloat16)] * slots,
        scratch_shapes=[
            pltpu.VMEM((leaves, RANK, RHS), jnp.bfloat16),
            pltpu.VMEM((parents, RANK, RHS), jnp.bfloat16),
            pltpu.SemaphoreType.DMA((2 + slots * each,)),
        ],
        cost_estimate=pl.CostEstimate(
            flops=2 * leaves * LEAF * RANK * RHS * 2, transcendentals=0, bytes_accessed=16 * 2 ** 20
        ),
    )(send_fine, send_coarse, charges, basis_t, transfer_t)
    return outs[0], outs[1], outs[2:2 + slots], outs[2 + slots:]


def on_device(
    charges,
    leaf_basis,
    transfer,
    near_blocks,
    near_source,
    couple_fine,
    source_fine,
    couple_coarse,
    source_coarse,
    send_fine,
    send_coarse,
):
    leaves = charges.shape[0]
    parents = leaves // 2
    fine_each = send_fine.shape[1] // (2 * REACH)
    coarse_each = send_coarse.shape[1] // (2 * REACH)
    axis = ("leaf", "couple")
    basis_t = leaf_basis.T
    transfer_t = transfer.T
    fine_coeffs, coarse_coeffs, fine_packets, coarse_packets = upward(
        charges, basis_t, transfer_t, send_fine[0], send_coarse[0], fine_each, coarse_each
    )
    coarse_in = []
    for slot, offset in enumerate(offset_list()):
        coarse_in.append(from_behind(coarse_packets[slot], axis, offset))
    fine_in = []
    for slot, offset in enumerate(offset_list()):
        fine_in.append(from_behind(fine_packets[slot], axis, offset))

    low, high = halo_pieces(charges, axis, HALO)
    near_field = gather_dot(
        near_source,
        near_blocks,
        [(low, 0, HALO, 0), (charges, HALO, leaves, 0), (high, HALO + leaves, HALO, 0)],
        near_source.shape[0] // leaves,
    )

    coarse_segments = [(coarse_coeffs, 0, parents, 0)]
    for slot in range(2 * REACH):
        coarse_segments.append((coarse_in[slot], parents + slot * coarse_each, coarse_each, 0))
    coarse_round = gather_dot(
        source_coarse, couple_coarse, coarse_segments, source_coarse.shape[0] // parents,
        out_dtype=jnp.bfloat16,
    )

    fine_segments = [(fine_coeffs, 0, leaves, 0)]
    for slot in range(2 * REACH):
        fine_segments.append((fine_in[slot], leaves + slot * fine_each, fine_each, 0))

    tb = min(BLOCK_TARGETS, leaves)

    def finish(tt, acc, refs):
        cr_ref, e_ref, v_ref, near_ref = refs
        e = e_ref[tt * RANK:(tt + 1) * RANK, :]
        down = jnp.dot(e, cr_ref[tt // 2], preferred_element_type=jnp.float32)
        fine_round = (acc + down).astype(jnp.bfloat16)
        v = v_ref[tt * LEAF:(tt + 1) * LEAF, :]
        far = jnp.dot(v, fine_round, preferred_element_type=jnp.float32)
        return (far + near_ref[tt]).astype(jnp.bfloat16)

    epilogue = (
        [coarse_round, transfer, leaf_basis, near_field],
        [
            pl.BlockSpec((tb // 2, RANK, RHS), lambda i, ix: (i, 0, 0)),
            pl.BlockSpec((tb * RANK, RANK), lambda i, ix: (i, 0)),
            pl.BlockSpec((tb * LEAF, RANK), lambda i, ix: (i, 0)),
            pl.BlockSpec((tb, LEAF, RHS), lambda i, ix: (i, 0, 0)),
        ],
        finish,
        jnp.bfloat16,
    )
    return gather_dot(
        source_fine, couple_fine, fine_segments, source_fine.shape[0] // leaves, epilogue
    )


def solution(mesh):
    return jax.shard_map(
        on_device,
        mesh=mesh,
        in_specs=(
            P(("leaf", "couple"), None, None),
            P(("leaf", "couple"), None),
            P(("leaf", "couple"), None),
            P(("leaf", "couple"), None),
            P(("leaf", "couple")),
            P(("leaf", "couple"), None),
            P(("leaf", "couple")),
            P(("leaf", "couple"), None),
            P(("leaf", "couple")),
            P(("leaf", "couple"), None),
            P(("leaf", "couple"), None),
        ),
        out_specs=P(("leaf", "couple"), None, None),
        check_vma=False,
    )
```

```python
import functools

import jax
import jax.numpy as jnp
from jax import lax
from jax.experimental import pallas as pl
from jax.experimental.pallas import tpu as pltpu
from jax.sharding import PartitionSpec as P

LEAF = 64
RANK = 64
RHS = 128
HALO = 4
REACH = 3
BLOCK_TARGETS = 8


def from_behind(value, axis, steps):
    count = lax.axis_size(axis)
    first, last = (max(0, -steps), min(count, count - steps))
    return lax.ppermute(value, axis, [(source, source + steps) for source in range(first, last)])


def halo_pieces(block, axis, width):
    count = lax.axis_size(axis)
    forward = [(i, i + 1) for i in range(count - 1)]
    backward = [(target, source) for source, target in forward]
    low = lax.ppermute(lax.slice_in_dim(block, block.shape[0] - width, None, axis=0), axis, forward)
    high = lax.ppermute(lax.slice_in_dim(block, 0, width, axis=0), axis, backward)
    return low, high


def offset_list():
    values = []
    for step in range(REACH):
        values.append(step + 1)
        values.append(-(step + 1))
    return values


def gather_dot(idx, mats, segments, pairs, epilogue=None, out_dtype=jnp.float32):
    rows = mats.shape[0]
    width = mats.shape[1] // pairs
    targets = rows // LEAF
    tb = min(BLOCK_TARGETS, targets)
    steps = targets // tb
    n_seg = len(segments)
    seg_arrays = [s[0] for s in segments]
    seg_meta = [(s[1], s[2], s[3]) for s in segments]
    total = sum(s[2] for s in segments)

    in_specs = [pl.BlockSpec((tb * LEAF, pairs * width), lambda i, ix: (i, 0))]
    for arr in seg_arrays:
        in_specs.append(pl.BlockSpec(memory_space=pl.ANY))
    extra = []
    if epilogue is not None:
        extra, extra_specs, _, out_dtype = epilogue
        in_specs.extend(extra_specs)

    def kernel(idx_ref, mats_ref, *refs):
        seg_refs = refs[:n_seg]
        extra_refs = refs[n_seg:len(refs) - 3]
        out_ref, pool_ref, sem = refs[len(refs) - 3:]
        blk = pl.program_id(0)

        @pl.when(blk == 0)
        def _():
            copies = []
            for j, (ref, (lo, cnt, row)) in enumerate(zip(seg_refs, seg_meta)):
                cp = pltpu.make_async_copy(ref.at[pl.ds(row, cnt)], pool_ref.at[pl.ds(lo, cnt)], sem.at[j])
                cp.start()
                copies.append(cp)
            for cp in copies:
                cp.wait()

        for tt in range(tb):
            base = (blk * tb + tt) * pairs
            blocks = [pool_ref[jnp.clip(idx_ref[base + k], 0, total - 1)] for k in range(pairs)]
            rhs = jnp.concatenate(blocks, axis=0)
            acc = jnp.dot(mats_ref[tt * LEAF:(tt + 1) * LEAF, :], rhs, preferred_element_type=jnp.float32)
            if epilogue is None:
                out_ref[tt] = acc.astype(out_dtype)
            else:
                out_ref[tt] = epilogue[2](tt, acc, extra_refs)

    grid_spec = pltpu.PrefetchScalarGridSpec(
        num_scalar_prefetch=1,
        grid=(steps,),
        in_specs=in_specs,
        out_specs=pl.BlockSpec((tb, LEAF, RHS), lambda i, ix: (i, 0, 0)),
        scratch_shapes=[
            pltpu.VMEM((total, width, RHS), jnp.bfloat16),
            pltpu.SemaphoreType.DMA((n_seg,)),
        ],
    )
    flops = 2 * rows * pairs * width * RHS
    bytes_accessed = mats.size * 2 + total * width * RHS * 2 + targets * LEAF * RHS * 4
    return pl.pallas_call(
        kernel,
        grid_spec=grid_spec,
        out_shape=jax.ShapeDtypeStruct((targets, LEAF, RHS), out_dtype),
        compiler_params=pltpu.CompilerParams(dimension_semantics=("arbitrary",)),
        cost_estimate=pl.CostEstimate(flops=flops, transcendentals=0, bytes_accessed=bytes_accessed),
    )(idx, mats, *seg_arrays, *extra)


def upward(charges, basis_t, transfer_t, send_fine, send_coarse, fine_each, coarse_each):
    leaves = charges.shape[0]
    parents = leaves // 2
    slots = 2 * REACH
    each = fine_each + coarse_each
    sizes = [each + (HALO if q < 2 else 0) for q in range(slots)]

    def kernel(sf_ref, sc_ref, x_ref, v_ref, e_ref, fine_out, coarse_out, *rest):
        packet_refs = rest[:slots]
        fine_v, coarse_v = rest[slots:slots + 2]
        bufs = rest[slots + 2:2 * slots + 2]
        sem = rest[2 * slots + 2]
        for j in range(parents):
            col = j * 2 * RANK
            f0 = jnp.dot(v_ref[:, col:col + RANK], x_ref[2 * j], preferred_element_type=jnp.float32)
            f1 = jnp.dot(v_ref[:, col + RANK:col + 2 * RANK], x_ref[2 * j + 1], preferred_element_type=jnp.float32)
            pair = jnp.concatenate([f0.astype(jnp.bfloat16), f1.astype(jnp.bfloat16)], axis=0)
            fine_v[2 * j] = pair[:RANK]
            fine_v[2 * j + 1] = pair[RANK:]
            e = e_ref[:, col:col + 2 * RANK]
            coarse_v[j] = jnp.dot(e, pair, preferred_element_type=jnp.float32).astype(jnp.bfloat16)

        copies = [
            pltpu.make_async_copy(fine_v, fine_out, sem.at[0]),
            pltpu.make_async_copy(coarse_v, coarse_out, sem.at[1]),
        ]
        for cp in copies:
            cp.start()
        for q in range(slots):
            buf = bufs[q]
            for m in range(fine_each):
                buf[m] = fine_v[jnp.clip(sf_ref[q * fine_each + m], 0, leaves - 1)]
            for m in range(coarse_each):
                buf[fine_each + m] = coarse_v[jnp.clip(sc_ref[q * coarse_each + m], 0, parents - 1)]
            if q == 0:
                buf[each:each + HALO] = x_ref[leaves - HALO:leaves]
            elif q == 1:
                buf[each:each + HALO] = x_ref[0:HALO]
            cp = pltpu.make_async_copy(buf, packet_refs[q], sem.at[2 + q])
            cp.start()
            copies.append(cp)
        for cp in copies:
            cp.wait()

    smem = pl.BlockSpec(memory_space=pltpu.SMEM)
    vmem = pl.BlockSpec(memory_space=pltpu.VMEM)
    hbm = pl.BlockSpec(memory_space=pl.ANY)
    block = jax.ShapeDtypeStruct
    outs = pl.pallas_call(
        kernel,
        in_specs=[smem, smem, vmem, vmem, vmem],
        out_specs=[hbm] * (2 + slots),
        out_shape=[block((leaves, RANK, RHS), jnp.bfloat16), block((parents, RANK, RHS), jnp.bfloat16)]
        + [block((n, RANK, RHS), jnp.bfloat16) for n in sizes],
        scratch_shapes=[
            pltpu.VMEM((leaves, RANK, RHS), jnp.bfloat16),
            pltpu.VMEM((parents, RANK, RHS), jnp.bfloat16),
        ]
        + [pltpu.VMEM((n, RANK, RHS), jnp.bfloat16) for n in sizes]
        + [pltpu.SemaphoreType.DMA((2 + slots,))],
        cost_estimate=pl.CostEstimate(
            flops=2 * leaves * LEAF * RANK * RHS * 2, transcendentals=0, bytes_accessed=16 * 2 ** 20
        ),
    )(send_fine, send_coarse, charges, basis_t, transfer_t)
    return outs[0], outs[1], outs[2:]


def on_device(
    charges,
    leaf_basis,
    transfer,
    near_blocks,
    near_source,
    couple_fine,
    source_fine,
    couple_coarse,
    source_coarse,
    send_fine,
    send_coarse,
):
    leaves = charges.shape[0]
    parents = leaves // 2
    fine_each = send_fine.shape[1] // (2 * REACH)
    coarse_each = send_coarse.shape[1] // (2 * REACH)
    axis = ("leaf", "couple")
    basis_t = leaf_basis.T
    transfer_t = transfer.T
    fine_coeffs, coarse_coeffs, packets = upward(
        charges, basis_t, transfer_t, send_fine[0], send_coarse[0], fine_each, coarse_each
    )
    incoming = []
    for slot, offset in enumerate(offset_list()):
        incoming.append(from_behind(packets[slot], axis, offset))

    each = fine_each + coarse_each
    near_field = gather_dot(
        near_source,
        near_blocks,
        [(incoming[0], 0, HALO, each), (charges, HALO, leaves, 0), (incoming[1], HALO + leaves, HALO, each)],
        near_source.shape[0] // leaves,
    )

    coarse_segments = [(coarse_coeffs, 0, parents, 0)]
    for slot in range(2 * REACH):
        coarse_segments.append((incoming[slot], parents + slot * coarse_each, coarse_each, fine_each))
    coarse_round = gather_dot(
        source_coarse, couple_coarse, coarse_segments, source_coarse.shape[0] // parents,
        out_dtype=jnp.bfloat16,
    )

    fine_segments = [(fine_coeffs, 0, leaves, 0)]
    for slot in range(2 * REACH):
        fine_segments.append((incoming[slot], leaves + slot * fine_each, fine_each, 0))

    tb = min(BLOCK_TARGETS, leaves)

    def finish(tt, acc, refs):
        cr_ref, e_ref, v_ref, near_ref = refs
        e = e_ref[tt * RANK:(tt + 1) * RANK, :]
        down = jnp.dot(e, cr_ref[tt // 2], preferred_element_type=jnp.float32)
        fine_round = (acc + down).astype(jnp.bfloat16)
        v = v_ref[tt * LEAF:(tt + 1) * LEAF, :]
        far = jnp.dot(v, fine_round, preferred_element_type=jnp.float32)
        return (far + near_ref[tt]).astype(jnp.bfloat16)

    epilogue = (
        [coarse_round, transfer, leaf_basis, near_field],
        [
            pl.BlockSpec((tb // 2, RANK, RHS), lambda i, ix: (i, 0, 0)),
            pl.BlockSpec((tb * RANK, RANK), lambda i, ix: (i, 0)),
            pl.BlockSpec((tb * LEAF, RANK), lambda i, ix: (i, 0)),
            pl.BlockSpec((tb, LEAF, RHS), lambda i, ix: (i, 0, 0)),
        ],
        finish,
        jnp.bfloat16,
    )
    return gather_dot(
        source_fine, couple_fine, fine_segments, source_fine.shape[0] // leaves, epilogue
    )


def solution(mesh):
    return jax.shard_map(
        on_device,
        mesh=mesh,
        in_specs=(
            P(("leaf", "couple"), None, None),
            P(("leaf", "couple"), None),
            P(("leaf", "couple"), None),
            P(("leaf", "couple"), None),
            P(("leaf", "couple")),
            P(("leaf", "couple"), None),
            P(("leaf", "couple")),
            P(("leaf", "couple"), None),
            P(("leaf", "couple")),
            P(("leaf", "couple"), None),
            P(("leaf", "couple"), None),
        ),
        out_specs=P(("leaf", "couple"), None, None),
        check_vma=False,
    )
```

```python
import functools

import jax
import jax.numpy as jnp
from jax import lax
from jax.experimental import pallas as pl
from jax.experimental.pallas import tpu as pltpu
from jax.sharding import PartitionSpec as P

LEAF = 64
RANK = 64
RHS = 128
HALO = 4
REACH = 3
BLOCK_TARGETS = 16


def from_behind(value, axis, steps):
    count = lax.axis_size(axis)
    first, last = (max(0, -steps), min(count, count - steps))
    return lax.ppermute(value, axis, [(source, source + steps) for source in range(first, last)])


def halo_pieces(block, axis, width):
    count = lax.axis_size(axis)
    forward = [(i, i + 1) for i in range(count - 1)]
    backward = [(target, source) for source, target in forward]
    low = lax.ppermute(lax.slice_in_dim(block, block.shape[0] - width, None, axis=0), axis, forward)
    high = lax.ppermute(lax.slice_in_dim(block, 0, width, axis=0), axis, backward)
    return low, high


def offset_list():
    values = []
    for step in range(REACH):
        values.append(step + 1)
        values.append(-(step + 1))
    return values


def gather_dot(idx, mats, segments, pairs, epilogue=None, out_dtype=jnp.float32):
    rows = mats.shape[0]
    width = mats.shape[1] // pairs
    targets = rows // LEAF
    tb = min(BLOCK_TARGETS, targets)
    steps = targets // tb
    n_seg = len(segments)
    seg_arrays = [s[0] for s in segments]
    seg_meta = [(s[1], s[2], s[3]) for s in segments]
    total = sum(s[2] for s in segments)

    in_specs = [pl.BlockSpec((tb * LEAF, pairs * width), lambda i, ix: (i, 0))]
    for arr in seg_arrays:
        in_specs.append(pl.BlockSpec(memory_space=pl.ANY))
    extra = []
    if epilogue is not None:
        extra, extra_specs, _, out_dtype = epilogue
        in_specs.extend(extra_specs)

    def kernel(idx_ref, mats_ref, *refs):
        seg_refs = refs[:n_seg]
        extra_refs = refs[n_seg:len(refs) - 3]
        out_ref, pool_ref, sem = refs[len(refs) - 3:]
        blk = pl.program_id(0)

        @pl.when(blk == 0)
        def _():
            copies = []
            for j, (ref, (lo, cnt, row)) in enumerate(zip(seg_refs, seg_meta)):
                cp = pltpu.make_async_copy(ref.at[pl.ds(row, cnt)], pool_ref.at[pl.ds(lo, cnt)], sem.at[j])
                cp.start()
                copies.append(cp)
            for cp in copies:
                cp.wait()

        for tt in range(tb):
            base = (blk * tb + tt) * pairs
            blocks = [pool_ref[jnp.clip(idx_ref[base + k], 0, total - 1)] for k in range(pairs)]
            rhs = jnp.concatenate(blocks, axis=0)
            acc = jnp.dot(mats_ref[tt * LEAF:(tt + 1) * LEAF, :], rhs, preferred_element_type=jnp.float32)
            if epilogue is None:
                out_ref[tt] = acc.astype(out_dtype)
            else:
                out_ref[tt] = epilogue[2](tt, acc, extra_refs)

    grid_spec = pltpu.PrefetchScalarGridSpec(
        num_scalar_prefetch=1,
        grid=(steps,),
        in_specs=in_specs,
        out_specs=pl.BlockSpec((tb, LEAF, RHS), lambda i, ix: (i, 0, 0)),
        scratch_shapes=[
            pltpu.VMEM((total, width, RHS), jnp.bfloat16),
            pltpu.SemaphoreType.DMA((n_seg,)),
        ],
    )
    flops = 2 * rows * pairs * width * RHS
    bytes_accessed = mats.size * 2 + total * width * RHS * 2 + targets * LEAF * RHS * 4
    return pl.pallas_call(
        kernel,
        grid_spec=grid_spec,
        out_shape=jax.ShapeDtypeStruct((targets, LEAF, RHS), out_dtype),
        compiler_params=pltpu.CompilerParams(dimension_semantics=("arbitrary",)),
        cost_estimate=pl.CostEstimate(flops=flops, transcendentals=0, bytes_accessed=bytes_accessed),
    )(idx, mats, *seg_arrays, *extra)


def upward(charges, basis_t, transfer_t, send_fine, send_coarse, fine_each, coarse_each):
    leaves = charges.shape[0]
    parents = leaves // 2
    slots = 2 * REACH
    each = fine_each + coarse_each
    sizes = [each + (HALO if q < 2 else 0) for q in range(slots)]

    def kernel(sf_ref, sc_ref, x_ref, v_ref, e_ref, fine_out, coarse_out, *rest):
        packet_refs = rest[:slots]
        fine_v, coarse_v = rest[slots:slots + 2]
        bufs = rest[slots + 2:2 * slots + 2]
        sem = rest[2 * slots + 2]
        for j in range(parents):
            col = j * 2 * RANK
            f0 = jnp.dot(v_ref[:, col:col + RANK], x_ref[2 * j], preferred_element_type=jnp.float32)
            f1 = jnp.dot(v_ref[:, col + RANK:col + 2 * RANK], x_ref[2 * j + 1], preferred_element_type=jnp.float32)
            pair = jnp.concatenate([f0.astype(jnp.bfloat16), f1.astype(jnp.bfloat16)], axis=0)
            fine_v[2 * j] = pair[:RANK]
            fine_v[2 * j + 1] = pair[RANK:]
            e = e_ref[:, col:col + 2 * RANK]
            coarse_v[j] = jnp.dot(e, pair, preferred_element_type=jnp.float32).astype(jnp.bfloat16)

        copies = [
            pltpu.make_async_copy(fine_v, fine_out, sem.at[0]),
            pltpu.make_async_copy(coarse_v, coarse_out, sem.at[1]),
        ]
        for cp in copies:
            cp.start()
        for q in range(slots):
            buf = bufs[q]
            for m in range(fine_each):
                buf[m] = fine_v[jnp.clip(sf_ref[q * fine_each + m], 0, leaves - 1)]
            for m in range(coarse_each):
                buf[fine_each + m] = coarse_v[jnp.clip(sc_ref[q * coarse_each + m], 0, parents - 1)]
            if q == 0:
                buf[each:each + HALO] = x_ref[leaves - HALO:leaves]
            elif q == 1:
                buf[each:each + HALO] = x_ref[0:HALO]
            cp = pltpu.make_async_copy(buf, packet_refs[q], sem.at[2 + q])
            cp.start()
            copies.append(cp)
        for cp in copies:
            cp.wait()

    smem = pl.BlockSpec(memory_space=pltpu.SMEM)
    vmem = pl.BlockSpec(memory_space=pltpu.VMEM)
    hbm = pl.BlockSpec(memory_space=pl.ANY)
    block = jax.ShapeDtypeStruct
    outs = pl.pallas_call(
        kernel,
        in_specs=[smem, smem, vmem, vmem, vmem],
        out_specs=[hbm] * (2 + slots),
        out_shape=[block((leaves, RANK, RHS), jnp.bfloat16), block((parents, RANK, RHS), jnp.bfloat16)]
        + [block((n, RANK, RHS), jnp.bfloat16) for n in sizes],
        scratch_shapes=[
            pltpu.VMEM((leaves, RANK, RHS), jnp.bfloat16),
            pltpu.VMEM((parents, RANK, RHS), jnp.bfloat16),
        ]
        + [pltpu.VMEM((n, RANK, RHS), jnp.bfloat16) for n in sizes]
        + [pltpu.SemaphoreType.DMA((2 + slots,))],
        cost_estimate=pl.CostEstimate(
            flops=2 * leaves * LEAF * RANK * RHS * 2, transcendentals=0, bytes_accessed=16 * 2 ** 20
        ),
    )(send_fine, send_coarse, charges, basis_t, transfer_t)
    return outs[0], outs[1], outs[2:]


def on_device(
    charges,
    leaf_basis,
    transfer,
    near_blocks,
    near_source,
    couple_fine,
    source_fine,
    couple_coarse,
    source_coarse,
    send_fine,
    send_coarse,
):
    leaves = charges.shape[0]
    parents = leaves // 2
    fine_each = send_fine.shape[1] // (2 * REACH)
    coarse_each = send_coarse.shape[1] // (2 * REACH)
    axis = ("leaf", "couple")
    basis_t = leaf_basis.T
    transfer_t = transfer.T
    fine_coeffs, coarse_coeffs, packets = upward(
        charges, basis_t, transfer_t, send_fine[0], send_coarse[0], fine_each, coarse_each
    )
    incoming = []
    for slot, offset in enumerate(offset_list()):
        incoming.append(from_behind(packets[slot], axis, offset))

    each = fine_each + coarse_each
    near_field = gather_dot(
        near_source,
        near_blocks,
        [(incoming[0], 0, HALO, each), (charges, HALO, leaves, 0), (incoming[1], HALO + leaves, HALO, each)],
        near_source.shape[0] // leaves,
    )

    coarse_segments = [(coarse_coeffs, 0, parents, 0)]
    for slot in range(2 * REACH):
        coarse_segments.append((incoming[slot], parents + slot * coarse_each, coarse_each, fine_each))
    coarse_round = gather_dot(
        source_coarse, couple_coarse, coarse_segments, source_coarse.shape[0] // parents,
        out_dtype=jnp.bfloat16,
    )

    fine_segments = [(fine_coeffs, 0, leaves, 0)]
    for slot in range(2 * REACH):
        fine_segments.append((incoming[slot], leaves + slot * fine_each, fine_each, 0))

    tb = min(BLOCK_TARGETS, leaves)

    def finish(tt, acc, refs):
        cr_ref, e_ref, v_ref, near_ref = refs
        e = e_ref[tt * RANK:(tt + 1) * RANK, :]
        down = jnp.dot(e, cr_ref[tt // 2], preferred_element_type=jnp.float32)
        fine_round = (acc + down).astype(jnp.bfloat16)
        v = v_ref[tt * LEAF:(tt + 1) * LEAF, :]
        far = jnp.dot(v, fine_round, preferred_element_type=jnp.float32)
        return (far + near_ref[tt]).astype(jnp.bfloat16)

    epilogue = (
        [coarse_round, transfer, leaf_basis, near_field],
        [
            pl.BlockSpec((tb // 2, RANK, RHS), lambda i, ix: (i, 0, 0)),
            pl.BlockSpec((tb * RANK, RANK), lambda i, ix: (i, 0)),
            pl.BlockSpec((tb * LEAF, RANK), lambda i, ix: (i, 0)),
            pl.BlockSpec((tb, LEAF, RHS), lambda i, ix: (i, 0, 0)),
        ],
        finish,
        jnp.bfloat16,
    )
    return gather_dot(
        source_fine, couple_fine, fine_segments, source_fine.shape[0] // leaves, epilogue
    )


def solution(mesh):
    return jax.shard_map(
        on_device,
        mesh=mesh,
        in_specs=(
            P(("leaf", "couple"), None, None),
            P(("leaf", "couple"), None),
            P(("leaf", "couple"), None),
            P(("leaf", "couple"), None),
            P(("leaf", "couple")),
            P(("leaf", "couple"), None),
            P(("leaf", "couple")),
            P(("leaf", "couple"), None),
            P(("leaf", "couple")),
            P(("leaf", "couple"), None),
            P(("leaf", "couple"), None),
        ),
        out_specs=P(("leaf", "couple"), None, None),
        check_vma=False,
    )
```

```python
import functools

import jax
import jax.numpy as jnp
from jax import lax
from jax.experimental import pallas as pl
from jax.experimental.pallas import tpu as pltpu
from jax.sharding import PartitionSpec as P

LEAF = 64
RANK = 64
RHS = 128
HALO = 4
REACH = 3
BLOCK_TARGETS = 16


def from_behind(value, axis, steps):
    count = lax.axis_size(axis)
    first, last = (max(0, -steps), min(count, count - steps))
    return lax.ppermute(value, axis, [(source, source + steps) for source in range(first, last)])


def halo_pieces(block, axis, width):
    count = lax.axis_size(axis)
    forward = [(i, i + 1) for i in range(count - 1)]
    backward = [(target, source) for source, target in forward]
    low = lax.ppermute(lax.slice_in_dim(block, block.shape[0] - width, None, axis=0), axis, forward)
    high = lax.ppermute(lax.slice_in_dim(block, 0, width, axis=0), axis, backward)
    return low, high


def offset_list():
    values = []
    for step in range(REACH):
        values.append(step + 1)
        values.append(-(step + 1))
    return values


def gather_dot(idx, mats, segments, pairs, epilogue=None, out_dtype=jnp.float32):
    rows = mats.shape[0]
    width = mats.shape[1] // pairs
    targets = rows // LEAF
    tb = min(BLOCK_TARGETS, targets)
    steps = targets // tb
    n_seg = len(segments)
    seg_arrays = [s[0] for s in segments]
    seg_meta = [(s[1], s[2], s[3]) for s in segments]
    total = sum(s[2] for s in segments)

    in_specs = [pl.BlockSpec((tb * LEAF, pairs * width), lambda i, ix: (i, 0))]
    for arr in seg_arrays:
        in_specs.append(pl.BlockSpec(memory_space=pl.ANY))
    extra = []
    if epilogue is not None:
        extra, extra_specs, _, out_dtype = epilogue
        in_specs.extend(extra_specs)

    def kernel(idx_ref, mats_ref, *refs):
        seg_refs = refs[:n_seg]
        extra_refs = refs[n_seg:len(refs) - 4]
        out_ref, pool_ref, sem, acc_ref = refs[len(refs) - 4:]
        blk = pl.program_id(0)

        @pl.when(blk == 0)
        def _():
            copies = []
            for j, (ref, (lo, cnt, row)) in enumerate(zip(seg_refs, seg_meta)):
                cp = pltpu.make_async_copy(ref.at[pl.ds(row, cnt)], pool_ref.at[pl.ds(lo, cnt)], sem.at[j])
                cp.start()
                copies.append(cp)
            for cp in copies:
                cp.wait()

        for tt in range(tb):
            base = (blk * tb + tt) * pairs
            blocks = [pool_ref[jnp.clip(idx_ref[base + k], 0, total - 1)] for k in range(pairs)]
            rhs = jnp.concatenate(blocks, axis=0)
            acc = jnp.dot(mats_ref[tt * LEAF:(tt + 1) * LEAF, :], rhs, preferred_element_type=jnp.float32)
            if epilogue is None:
                out_ref[tt] = acc.astype(out_dtype)
            else:
                acc_ref[tt] = acc
        if epilogue is not None:
            epilogue[2](tb, acc_ref, extra_refs, out_ref)

    grid_spec = pltpu.PrefetchScalarGridSpec(
        num_scalar_prefetch=1,
        grid=(steps,),
        in_specs=in_specs,
        out_specs=pl.BlockSpec((tb, LEAF, RHS), lambda i, ix: (i, 0, 0)),
        scratch_shapes=[
            pltpu.VMEM((total, width, RHS), jnp.bfloat16),
            pltpu.SemaphoreType.DMA((n_seg,)),
            pltpu.VMEM((tb if epilogue is not None else 1, LEAF, RHS), jnp.float32),
        ],
    )
    flops = 2 * rows * pairs * width * RHS
    bytes_accessed = mats.size * 2 + total * width * RHS * 2 + targets * LEAF * RHS * 4
    return pl.pallas_call(
        kernel,
        grid_spec=grid_spec,
        out_shape=jax.ShapeDtypeStruct((targets, LEAF, RHS), out_dtype),
        compiler_params=pltpu.CompilerParams(dimension_semantics=("arbitrary",)),
        cost_estimate=pl.CostEstimate(flops=flops, transcendentals=0, bytes_accessed=bytes_accessed),
    )(idx, mats, *seg_arrays, *extra)


def upward(charges, basis_t, transfer_t, send_fine, send_coarse, fine_each, coarse_each):
    leaves = charges.shape[0]
    parents = leaves // 2
    slots = 2 * REACH
    each = fine_each + coarse_each
    sizes = [each + (HALO if q < 2 else 0) for q in range(slots)]

    def kernel(sf_ref, sc_ref, x_ref, v_ref, e_ref, fine_out, coarse_out, *rest):
        packet_refs = rest[:slots]
        fine_v, coarse_v = rest[slots:slots + 2]
        bufs = rest[slots + 2:2 * slots + 2]
        sem = rest[2 * slots + 2]
        for j in range(parents):
            col = j * 2 * RANK
            f0 = jnp.dot(v_ref[:, col:col + RANK], x_ref[2 * j], preferred_element_type=jnp.float32)
            f1 = jnp.dot(v_ref[:, col + RANK:col + 2 * RANK], x_ref[2 * j + 1], preferred_element_type=jnp.float32)
            pair = jnp.concatenate([f0.astype(jnp.bfloat16), f1.astype(jnp.bfloat16)], axis=0)
            fine_v[2 * j] = pair[:RANK]
            fine_v[2 * j + 1] = pair[RANK:]
            e = e_ref[:, col:col + 2 * RANK]
            coarse_v[j] = jnp.dot(e, pair, preferred_element_type=jnp.float32).astype(jnp.bfloat16)

        copies = [
            pltpu.make_async_copy(fine_v, fine_out, sem.at[0]),
            pltpu.make_async_copy(coarse_v, coarse_out, sem.at[1]),
        ]
        for cp in copies:
            cp.start()
        for q in range(slots):
            buf = bufs[q]
            for m in range(fine_each):
                buf[m] = fine_v[jnp.clip(sf_ref[q * fine_each + m], 0, leaves - 1)]
            for m in range(coarse_each):
                buf[fine_each + m] = coarse_v[jnp.clip(sc_ref[q * coarse_each + m], 0, parents - 1)]
            if q == 0:
                buf[each:each + HALO] = x_ref[leaves - HALO:leaves]
            elif q == 1:
                buf[each:each + HALO] = x_ref[0:HALO]
            cp = pltpu.make_async_copy(buf, packet_refs[q], sem.at[2 + q])
            cp.start()
            copies.append(cp)
        for cp in copies:
            cp.wait()

    smem = pl.BlockSpec(memory_space=pltpu.SMEM)
    vmem = pl.BlockSpec(memory_space=pltpu.VMEM)
    hbm = pl.BlockSpec(memory_space=pl.ANY)
    block = jax.ShapeDtypeStruct
    outs = pl.pallas_call(
        kernel,
        in_specs=[smem, smem, vmem, vmem, vmem],
        out_specs=[hbm] * (2 + slots),
        out_shape=[block((leaves, RANK, RHS), jnp.bfloat16), block((parents, RANK, RHS), jnp.bfloat16)]
        + [block((n, RANK, RHS), jnp.bfloat16) for n in sizes],
        scratch_shapes=[
            pltpu.VMEM((leaves, RANK, RHS), jnp.bfloat16),
            pltpu.VMEM((parents, RANK, RHS), jnp.bfloat16),
        ]
        + [pltpu.VMEM((n, RANK, RHS), jnp.bfloat16) for n in sizes]
        + [pltpu.SemaphoreType.DMA((2 + slots,))],
        cost_estimate=pl.CostEstimate(
            flops=2 * leaves * LEAF * RANK * RHS * 2, transcendentals=0, bytes_accessed=16 * 2 ** 20
        ),
    )(send_fine, send_coarse, charges, basis_t, transfer_t)
    return outs[0], outs[1], outs[2:]


def on_device(
    charges,
    leaf_basis,
    transfer,
    near_blocks,
    near_source,
    couple_fine,
    source_fine,
    couple_coarse,
    source_coarse,
    send_fine,
    send_coarse,
):
    leaves = charges.shape[0]
    parents = leaves // 2
    fine_each = send_fine.shape[1] // (2 * REACH)
    coarse_each = send_coarse.shape[1] // (2 * REACH)
    axis = ("leaf", "couple")
    basis_t = leaf_basis.T
    transfer_t = transfer.T
    fine_coeffs, coarse_coeffs, packets = upward(
        charges, basis_t, transfer_t, send_fine[0], send_coarse[0], fine_each, coarse_each
    )
    incoming = []
    for slot, offset in enumerate(offset_list()):
        incoming.append(from_behind(packets[slot], axis, offset))

    each = fine_each + coarse_each
    near_field = gather_dot(
        near_source,
        near_blocks,
        [(incoming[0], 0, HALO, each), (charges, HALO, leaves, 0), (incoming[1], HALO + leaves, HALO, each)],
        near_source.shape[0] // leaves,
    )

    coarse_segments = [(coarse_coeffs, 0, parents, 0)]
    for slot in range(2 * REACH):
        coarse_segments.append((incoming[slot], parents + slot * coarse_each, coarse_each, fine_each))
    coarse_round = gather_dot(
        source_coarse, couple_coarse, coarse_segments, source_coarse.shape[0] // parents,
        out_dtype=jnp.bfloat16,
    )

    fine_segments = [(fine_coeffs, 0, leaves, 0)]
    for slot in range(2 * REACH):
        fine_segments.append((incoming[slot], leaves + slot * fine_each, fine_each, 0))

    tb = min(BLOCK_TARGETS, leaves)

    def finish(count, acc_ref, refs, out_ref):
        cr_ref, e_ref, v_ref, near_ref = refs
        rounded = []
        for tt in range(count):
            e = e_ref[tt * RANK:(tt + 1) * RANK, :]
            down = jnp.dot(e, cr_ref[tt // 2], preferred_element_type=jnp.float32)
            rounded.append((acc_ref[tt] + down).astype(jnp.bfloat16))
        for tt in range(count):
            v = v_ref[tt * LEAF:(tt + 1) * LEAF, :]
            far = jnp.dot(v, rounded[tt], preferred_element_type=jnp.float32)
            out_ref[tt] = (far + near_ref[tt]).astype(jnp.bfloat16)

    epilogue = (
        [coarse_round, transfer, leaf_basis, near_field],
        [
            pl.BlockSpec((tb // 2, RANK, RHS), lambda i, ix: (i, 0, 0)),
            pl.BlockSpec((tb * RANK, RANK), lambda i, ix: (i, 0)),
            pl.BlockSpec((tb * LEAF, RANK), lambda i, ix: (i, 0)),
            pl.BlockSpec((tb, LEAF, RHS), lambda i, ix: (i, 0, 0)),
        ],
        finish,
        jnp.bfloat16,
    )
    return gather_dot(
        source_fine, couple_fine, fine_segments, source_fine.shape[0] // leaves, epilogue
    )


def solution(mesh):
    return jax.shard_map(
        on_device,
        mesh=mesh,
        in_specs=(
            P(("leaf", "couple"), None, None),
            P(("leaf", "couple"), None),
            P(("leaf", "couple"), None),
            P(("leaf", "couple"), None),
            P(("leaf", "couple")),
            P(("leaf", "couple"), None),
            P(("leaf", "couple")),
            P(("leaf", "couple"), None),
            P(("leaf", "couple")),
            P(("leaf", "couple"), None),
            P(("leaf", "couple"), None),
        ),
        out_specs=P(("leaf", "couple"), None, None),
        check_vma=False,
    )
```

```python
import functools

import jax
import jax.numpy as jnp
from jax import lax
from jax.experimental import pallas as pl
from jax.experimental.pallas import tpu as pltpu
from jax.sharding import PartitionSpec as P

LEAF = 64
RANK = 64
RHS = 128
HALO = 4
REACH = 3
BLOCK_TARGETS = 16


def from_behind(value, axis, steps):
    count = lax.axis_size(axis)
    first, last = (max(0, -steps), min(count, count - steps))
    return lax.ppermute(value, axis, [(source, source + steps) for source in range(first, last)])


def halo_pieces(block, axis, width):
    count = lax.axis_size(axis)
    forward = [(i, i + 1) for i in range(count - 1)]
    backward = [(target, source) for source, target in forward]
    low = lax.ppermute(lax.slice_in_dim(block, block.shape[0] - width, None, axis=0), axis, forward)
    high = lax.ppermute(lax.slice_in_dim(block, 0, width, axis=0), axis, backward)
    return low, high


def offset_list():
    values = []
    for step in range(REACH):
        values.append(step + 1)
        values.append(-(step + 1))
    return values


def gather_dot(idx, mats, segments, pairs, epilogue=None, out_dtype=jnp.float32):
    rows = mats.shape[0]
    width = mats.shape[1] // pairs
    targets = rows // LEAF
    tb = min(BLOCK_TARGETS, targets)
    steps = targets // tb
    n_seg = len(segments)
    seg_arrays = [s[0] for s in segments]
    seg_meta = [(s[1], s[2], s[3]) for s in segments]
    total = sum(s[2] for s in segments)

    in_specs = [pl.BlockSpec((tb * LEAF, pairs * width), lambda i, ix: (i, 0))]
    for arr in seg_arrays:
        in_specs.append(pl.BlockSpec(memory_space=pl.ANY))
    extra = []
    if epilogue is not None:
        extra, extra_specs, _, out_dtype = epilogue
        in_specs.extend(extra_specs)

    def kernel(idx_ref, mats_ref, *refs):
        seg_refs = refs[:n_seg]
        extra_refs = refs[n_seg:len(refs) - 4]
        out_ref, pool_ref, sem, acc_ref = refs[len(refs) - 4:]
        blk = pl.program_id(0)

        @pl.when(blk == 0)
        def _():
            copies = []
            for j, (ref, (lo, cnt, row)) in enumerate(zip(seg_refs, seg_meta)):
                cp = pltpu.make_async_copy(ref.at[pl.ds(row, cnt)], pool_ref.at[pl.ds(lo, cnt)], sem.at[j])
                cp.start()
                copies.append(cp)
            for cp in copies:
                cp.wait()

        for tt in range(tb):
            base = (blk * tb + tt) * pairs
            blocks = [pool_ref[idx_ref[base + k]] for k in range(pairs)]
            rhs = jnp.concatenate(blocks, axis=0)
            acc = jnp.dot(mats_ref[tt * LEAF:(tt + 1) * LEAF, :], rhs, preferred_element_type=jnp.float32)
            if epilogue is None:
                out_ref[tt] = acc.astype(out_dtype)
            else:
                acc_ref[tt] = acc
        if epilogue is not None:
            epilogue[2](tb, acc_ref, extra_refs, out_ref)

    grid_spec = pltpu.PrefetchScalarGridSpec(
        num_scalar_prefetch=1,
        grid=(steps,),
        in_specs=in_specs,
        out_specs=pl.BlockSpec((tb, LEAF, RHS), lambda i, ix: (i, 0, 0)),
        scratch_shapes=[
            pltpu.VMEM((total, width, RHS), jnp.bfloat16),
            pltpu.SemaphoreType.DMA((n_seg,)),
            pltpu.VMEM((tb if epilogue is not None else 1, LEAF, RHS), jnp.float32),
        ],
    )
    flops = 2 * rows * pairs * width * RHS
    bytes_accessed = mats.size * 2 + total * width * RHS * 2 + targets * LEAF * RHS * 4
    return pl.pallas_call(
        kernel,
        grid_spec=grid_spec,
        out_shape=jax.ShapeDtypeStruct((targets, LEAF, RHS), out_dtype),
        compiler_params=pltpu.CompilerParams(dimension_semantics=("arbitrary",)),
        cost_estimate=pl.CostEstimate(flops=flops, transcendentals=0, bytes_accessed=bytes_accessed),
    )(idx, mats, *seg_arrays, *extra)


def upward(charges, basis_t, transfer_t, send_fine, send_coarse, fine_each, coarse_each):
    leaves = charges.shape[0]
    parents = leaves // 2
    slots = 2 * REACH
    each = fine_each + coarse_each
    sizes = [each + (HALO if q < 2 else 0) for q in range(slots)]

    def kernel(sf_ref, sc_ref, x_ref, v_ref, e_ref, fine_out, coarse_out, *rest):
        packet_refs = rest[:slots]
        fine_v, coarse_v = rest[slots:slots + 2]
        bufs = rest[slots + 2:2 * slots + 2]
        sem = rest[2 * slots + 2]
        for j in range(parents):
            col = j * 2 * RANK
            f0 = jnp.dot(v_ref[:, col:col + RANK], x_ref[2 * j], preferred_element_type=jnp.float32)
            f1 = jnp.dot(v_ref[:, col + RANK:col + 2 * RANK], x_ref[2 * j + 1], preferred_element_type=jnp.float32)
            pair = jnp.concatenate([f0.astype(jnp.bfloat16), f1.astype(jnp.bfloat16)], axis=0)
            fine_v[2 * j] = pair[:RANK]
            fine_v[2 * j + 1] = pair[RANK:]
            e = e_ref[:, col:col + 2 * RANK]
            coarse_v[j] = jnp.dot(e, pair, preferred_element_type=jnp.float32).astype(jnp.bfloat16)

        copies = [
            pltpu.make_async_copy(fine_v, fine_out, sem.at[0]),
            pltpu.make_async_copy(coarse_v, coarse_out, sem.at[1]),
        ]
        for cp in copies:
            cp.start()
        for q in range(slots):
            buf = bufs[q]
            for m in range(fine_each):
                buf[m] = fine_v[jnp.clip(sf_ref[q * fine_each + m], 0, leaves - 1)]
            for m in range(coarse_each):
                buf[fine_each + m] = coarse_v[jnp.clip(sc_ref[q * coarse_each + m], 0, parents - 1)]
            if q == 0:
                buf[each:each + HALO] = x_ref[leaves - HALO:leaves]
            elif q == 1:
                buf[each:each + HALO] = x_ref[0:HALO]
            cp = pltpu.make_async_copy(buf, packet_refs[q], sem.at[2 + q])
            cp.start()
            copies.append(cp)
        for cp in copies:
            cp.wait()

    smem = pl.BlockSpec(memory_space=pltpu.SMEM)
    vmem = pl.BlockSpec(memory_space=pltpu.VMEM)
    hbm = pl.BlockSpec(memory_space=pl.ANY)
    block = jax.ShapeDtypeStruct
    outs = pl.pallas_call(
        kernel,
        in_specs=[smem, smem, vmem, vmem, vmem],
        out_specs=[hbm] * (2 + slots),
        out_shape=[block((leaves, RANK, RHS), jnp.bfloat16), block((parents, RANK, RHS), jnp.bfloat16)]
        + [block((n, RANK, RHS), jnp.bfloat16) for n in sizes],
        scratch_shapes=[
            pltpu.VMEM((leaves, RANK, RHS), jnp.bfloat16),
            pltpu.VMEM((parents, RANK, RHS), jnp.bfloat16),
        ]
        + [pltpu.VMEM((n, RANK, RHS), jnp.bfloat16) for n in sizes]
        + [pltpu.SemaphoreType.DMA((2 + slots,))],
        cost_estimate=pl.CostEstimate(
            flops=2 * leaves * LEAF * RANK * RHS * 2, transcendentals=0, bytes_accessed=16 * 2 ** 20
        ),
    )(send_fine, send_coarse, charges, basis_t, transfer_t)
    return outs[0], outs[1], outs[2:]


def on_device(
    charges,
    leaf_basis,
    transfer,
    near_blocks,
    near_source,
    couple_fine,
    source_fine,
    couple_coarse,
    source_coarse,
    send_fine,
    send_coarse,
):
    leaves = charges.shape[0]
    parents = leaves // 2
    fine_each = send_fine.shape[1] // (2 * REACH)
    coarse_each = send_coarse.shape[1] // (2 * REACH)
    axis = ("leaf", "couple")
    basis_t = leaf_basis.T
    transfer_t = transfer.T
    fine_coeffs, coarse_coeffs, packets = upward(
        charges, basis_t, transfer_t, send_fine[0], send_coarse[0], fine_each, coarse_each
    )
    incoming = []
    for slot, offset in enumerate(offset_list()):
        incoming.append(from_behind(packets[slot], axis, offset))

    each = fine_each + coarse_each
    near_field = gather_dot(
        near_source,
        near_blocks,
        [(incoming[0], 0, HALO, each), (charges, HALO, leaves, 0), (incoming[1], HALO + leaves, HALO, each)],
        near_source.shape[0] // leaves,
    )

    coarse_segments = [(coarse_coeffs, 0, parents, 0)]
    for slot in range(2 * REACH):
        coarse_segments.append((incoming[slot], parents + slot * coarse_each, coarse_each, fine_each))
    coarse_round = gather_dot(
        source_coarse, couple_coarse, coarse_segments, source_coarse.shape[0] // parents,
        out_dtype=jnp.bfloat16,
    )

    fine_segments = [(fine_coeffs, 0, leaves, 0)]
    for slot in range(2 * REACH):
        fine_segments.append((incoming[slot], leaves + slot * fine_each, fine_each, 0))

    tb = min(BLOCK_TARGETS, leaves)

    def finish(count, acc_ref, refs, out_ref):
        cr_ref, e_ref, v_ref, near_ref = refs
        rounded = []
        for tt in range(count):
            e = e_ref[tt * RANK:(tt + 1) * RANK, :]
            down = jnp.dot(e, cr_ref[tt // 2], preferred_element_type=jnp.float32)
            rounded.append((acc_ref[tt] + down).astype(jnp.bfloat16))
        for tt in range(count):
            v = v_ref[tt * LEAF:(tt + 1) * LEAF, :]
            far = jnp.dot(v, rounded[tt], preferred_element_type=jnp.float32)
            out_ref[tt] = (far + near_ref[tt]).astype(jnp.bfloat16)

    epilogue = (
        [coarse_round, transfer, leaf_basis, near_field],
        [
            pl.BlockSpec((tb // 2, RANK, RHS), lambda i, ix: (i, 0, 0)),
            pl.BlockSpec((tb * RANK, RANK), lambda i, ix: (i, 0)),
            pl.BlockSpec((tb * LEAF, RANK), lambda i, ix: (i, 0)),
            pl.BlockSpec((tb, LEAF, RHS), lambda i, ix: (i, 0, 0)),
        ],
        finish,
        jnp.bfloat16,
    )
    return gather_dot(
        source_fine, couple_fine, fine_segments, source_fine.shape[0] // leaves, epilogue
    )


def solution(mesh):
    return jax.shard_map(
        on_device,
        mesh=mesh,
        in_specs=(
            P(("leaf", "couple"), None, None),
            P(("leaf", "couple"), None),
            P(("leaf", "couple"), None),
            P(("leaf", "couple"), None),
            P(("leaf", "couple")),
            P(("leaf", "couple"), None),
            P(("leaf", "couple")),
            P(("leaf", "couple"), None),
            P(("leaf", "couple")),
            P(("leaf", "couple"), None),
            P(("leaf", "couple"), None),
        ),
        out_specs=P(("leaf", "couple"), None, None),
        check_vma=False,
    )
```

```python
import functools

import jax
import jax.numpy as jnp
from jax import lax
from jax.experimental import pallas as pl
from jax.experimental.pallas import tpu as pltpu
from jax.sharding import PartitionSpec as P

LEAF = 64
RANK = 64
RHS = 128
HALO = 4
REACH = 3
BLOCK_TARGETS = 16


def from_behind(value, axis, steps):
    count = lax.axis_size(axis)
    first, last = (max(0, -steps), min(count, count - steps))
    return lax.ppermute(value, axis, [(source, source + steps) for source in range(first, last)])


def halo_pieces(block, axis, width):
    count = lax.axis_size(axis)
    forward = [(i, i + 1) for i in range(count - 1)]
    backward = [(target, source) for source, target in forward]
    low = lax.ppermute(lax.slice_in_dim(block, block.shape[0] - width, None, axis=0), axis, forward)
    high = lax.ppermute(lax.slice_in_dim(block, 0, width, axis=0), axis, backward)
    return low, high


def offset_list():
    values = []
    for step in range(REACH):
        values.append(step + 1)
        values.append(-(step + 1))
    return values


def gather_dot(idx, mats, segments, pairs, epilogue=None, out_dtype=jnp.float32):
    rows = mats.shape[0]
    width = mats.shape[1] // pairs
    targets = rows // LEAF
    tb = min(BLOCK_TARGETS, targets)
    steps = targets // tb
    n_seg = len(segments)
    seg_arrays = [s[0] for s in segments]
    seg_meta = [(s[1], s[2], s[3]) for s in segments]
    total = sum(s[2] for s in segments)

    in_specs = [pl.BlockSpec((tb * LEAF, pairs * width), lambda i, ix: (i, 0))]
    for arr in seg_arrays:
        in_specs.append(pl.BlockSpec(memory_space=pl.ANY))
    extra = []
    if epilogue is not None:
        extra, extra_specs, _, out_dtype = epilogue
        in_specs.extend(extra_specs)

    def kernel(idx_ref, mats_ref, *refs):
        seg_refs = refs[:n_seg]
        extra_refs = refs[n_seg:len(refs) - 4]
        out_ref, pool_ref, sem, acc_ref = refs[len(refs) - 4:]
        blk = pl.program_id(0)

        @pl.when(blk == 0)
        def _():
            copies = []
            for j, (ref, (lo, cnt, row)) in enumerate(zip(seg_refs, seg_meta)):
                cp = pltpu.make_async_copy(ref.at[pl.ds(row, cnt)], pool_ref.at[pl.ds(lo, cnt)], sem.at[j])
                cp.start()
                copies.append(cp)
            for cp in copies:
                cp.wait()

        for tt in range(tb):
            base = (blk * tb + tt) * pairs
            blocks = [pool_ref[idx_ref[base + k]] for k in range(pairs)]
            rhs = jnp.concatenate(blocks, axis=0)
            acc = jnp.dot(mats_ref[tt * LEAF:(tt + 1) * LEAF, :], rhs, preferred_element_type=jnp.float32)
            if epilogue is None:
                out_ref[tt] = acc.astype(out_dtype)
            else:
                acc_ref[tt] = acc
        if epilogue is not None:
            epilogue[2](tb, acc_ref, extra_refs, out_ref)

    grid_spec = pltpu.PrefetchScalarGridSpec(
        num_scalar_prefetch=1,
        grid=(steps,),
        in_specs=in_specs,
        out_specs=pl.BlockSpec((tb, LEAF, RHS), lambda i, ix: (i, 0, 0)),
        scratch_shapes=[
            pltpu.VMEM((total, width, RHS), jnp.bfloat16),
            pltpu.SemaphoreType.DMA((n_seg,)),
            pltpu.VMEM((tb if epilogue is not None else 1, LEAF, RHS), jnp.float32),
        ],
    )
    flops = 2 * rows * pairs * width * RHS
    bytes_accessed = mats.size * 2 + total * width * RHS * 2 + targets * LEAF * RHS * 4
    return pl.pallas_call(
        kernel,
        grid_spec=grid_spec,
        out_shape=jax.ShapeDtypeStruct((targets, LEAF, RHS), out_dtype),
        compiler_params=pltpu.CompilerParams(dimension_semantics=("arbitrary",)),
        cost_estimate=pl.CostEstimate(flops=flops, transcendentals=0, bytes_accessed=bytes_accessed),
    )(idx, mats, *seg_arrays, *extra)


def upward(charges, basis_t, transfer_t, send_fine, send_coarse, fine_each, coarse_each):
    leaves = charges.shape[0]
    parents = leaves // 2
    slots = 2 * REACH
    each = fine_each + coarse_each
    sizes = [each + (HALO if q < 2 else 0) for q in range(slots)]

    def kernel(sf_ref, sc_ref, x_ref, v_ref, e_ref, fine_out, coarse_out, *rest):
        packet_refs = rest[:slots]
        fine_v, coarse_v = rest[slots:slots + 2]
        bufs = rest[slots + 2:2 * slots + 2]
        sem = rest[2 * slots + 2]
        for j in range(parents):
            col = j * 2 * RANK
            f0 = jnp.dot(v_ref[:, col:col + RANK], x_ref[2 * j], preferred_element_type=jnp.float32)
            f1 = jnp.dot(v_ref[:, col + RANK:col + 2 * RANK], x_ref[2 * j + 1], preferred_element_type=jnp.float32)
            pair = jnp.concatenate([f0.astype(jnp.bfloat16), f1.astype(jnp.bfloat16)], axis=0)
            fine_v[2 * j] = pair[:RANK]
            fine_v[2 * j + 1] = pair[RANK:]
            e = e_ref[:, col:col + 2 * RANK]
            coarse_v[j] = jnp.dot(e, pair, preferred_element_type=jnp.float32).astype(jnp.bfloat16)

        copies = [
            pltpu.make_async_copy(fine_v, fine_out, sem.at[0]),
            pltpu.make_async_copy(coarse_v, coarse_out, sem.at[1]),
        ]
        for cp in copies:
            cp.start()
        for q in range(slots):
            buf = bufs[q]
            for m in range(fine_each):
                buf[m] = fine_v[jnp.clip(sf_ref[q * fine_each + m], 0, leaves - 1)]
            for m in range(coarse_each):
                buf[fine_each + m] = coarse_v[jnp.clip(sc_ref[q * coarse_each + m], 0, parents - 1)]
            if q == 0:
                buf[each:each + HALO] = x_ref[leaves - HALO:leaves]
            elif q == 1:
                buf[each:each + HALO] = x_ref[0:HALO]
            cp = pltpu.make_async_copy(buf, packet_refs[q], sem.at[2 + q])
            cp.start()
            copies.append(cp)
        for cp in copies:
            cp.wait()

    smem = pl.BlockSpec(memory_space=pltpu.SMEM)
    vmem = pl.BlockSpec(memory_space=pltpu.VMEM)
    hbm = pl.BlockSpec(memory_space=pl.ANY)
    block = jax.ShapeDtypeStruct
    outs = pl.pallas_call(
        kernel,
        in_specs=[smem, smem, vmem, vmem, vmem],
        out_specs=[hbm] * (2 + slots),
        out_shape=[block((leaves, RANK, RHS), jnp.bfloat16), block((parents, RANK, RHS), jnp.bfloat16)]
        + [block((n, RANK, RHS), jnp.bfloat16) for n in sizes],
        scratch_shapes=[
            pltpu.VMEM((leaves, RANK, RHS), jnp.bfloat16),
            pltpu.VMEM((parents, RANK, RHS), jnp.bfloat16),
        ]
        + [pltpu.VMEM((n, RANK, RHS), jnp.bfloat16) for n in sizes]
        + [pltpu.SemaphoreType.DMA((2 + slots,))],
        cost_estimate=pl.CostEstimate(
            flops=2 * leaves * LEAF * RANK * RHS * 2, transcendentals=0, bytes_accessed=16 * 2 ** 20
        ),
    )(send_fine, send_coarse, charges, basis_t, transfer_t)
    return outs[0], outs[1], outs[2:]


def coupled_product(coarse_part, fine_part, transfer, leaf_basis, near_field):
    c_idx, c_mats, c_segs, c_pairs = coarse_part
    f_idx, f_mats, f_segs, f_pairs = fine_part
    width = RANK
    parents = c_mats.shape[0] // RANK
    leaves = f_mats.shape[0] // LEAF
    tb = min(BLOCK_TARGETS, leaves)
    steps = leaves // tb
    halves = 2 if parents % 2 == 0 else 1
    c_rows = parents * RANK // halves
    c_total = sum(s[2] for s in c_segs)
    f_total = sum(s[2] for s in f_segs)
    segs = c_segs + f_segs
    n_c = len(c_segs)
    n_seg = len(segs)

    hbm = pl.BlockSpec(memory_space=pl.ANY)
    in_specs = [hbm] + [pl.BlockSpec((tb * LEAF, f_pairs * width), lambda i, a, b: (i, 0))]
    in_specs += [hbm] * n_seg
    in_specs += [
        pl.BlockSpec((tb * RANK, RANK), lambda i, a, b: (i, 0)),
        pl.BlockSpec((tb * LEAF, RANK), lambda i, a, b: (i, 0)),
        pl.BlockSpec((tb, LEAF, RHS), lambda i, a, b: (i, 0, 0)),
    ]

    def gather_sum(idx_ref, pool_ref, mats, base, pairs):
        blocks = [pool_ref[idx_ref[base + k]] for k in range(pairs)]
        return jnp.dot(mats, jnp.concatenate(blocks, axis=0), preferred_element_type=jnp.float32)

    def kernel(ci_ref, fi_ref, cm_hbm, fm_ref, *refs):
        seg_refs = refs[:n_seg]
        e_ref, v_ref, near_ref, out_ref = refs[n_seg:n_seg + 4]
        c_pool, f_pool, c_mats_v, cr_ref, acc_ref, sem = refs[n_seg + 4:]
        blk = pl.program_id(0)

        @pl.when(blk == 0)
        def _():
            seg_copies = []
            for j, (ref, (_, lo, cnt, row)) in enumerate(zip(seg_refs, segs)):
                pool = c_pool if j < n_c else f_pool
                cp = pltpu.make_async_copy(ref.at[pl.ds(row, cnt)], pool.at[pl.ds(lo, cnt)], sem.at[j])
                cp.start()
                seg_copies.append(cp)
            mat_copies = []
            for h in range(halves):
                cp = pltpu.make_async_copy(
                    cm_hbm.at[pl.ds(h * c_rows, c_rows)], c_mats_v.at[pl.ds(h * c_rows, c_rows)], sem.at[n_seg + h]
                )
                cp.start()
                mat_copies.append(cp)
            for cp in seg_copies[:n_c]:
                cp.wait()
            per_half = parents // halves
            for h in range(halves):
                mat_copies[h].wait()
                for p in range(h * per_half, (h + 1) * per_half):
                    acc = gather_sum(ci_ref, c_pool, c_mats_v[p * RANK:(p + 1) * RANK, :], p * c_pairs, c_pairs)
                    cr_ref[p] = acc.astype(jnp.bfloat16)
            for cp in seg_copies[n_c:]:
                cp.wait()

        for tt in range(tb):
            base = (blk * tb + tt) * f_pairs
            acc_ref[tt] = gather_sum(fi_ref, f_pool, fm_ref[tt * LEAF:(tt + 1) * LEAF, :], base, f_pairs)
        rounded = []
        for tt in range(tb):
            e = e_ref[tt * RANK:(tt + 1) * RANK, :]
            down = jnp.dot(e, cr_ref[(blk * tb + tt) // 2], preferred_element_type=jnp.float32)
            rounded.append((acc_ref[tt] + down).astype(jnp.bfloat16))
        for tt in range(tb):
            v = v_ref[tt * LEAF:(tt + 1) * LEAF, :]
            far = jnp.dot(v, rounded[tt], preferred_element_type=jnp.float32)
            out_ref[tt] = (far + near_ref[tt]).astype(jnp.bfloat16)

    grid_spec = pltpu.PrefetchScalarGridSpec(
        num_scalar_prefetch=2,
        grid=(steps,),
        in_specs=in_specs,
        out_specs=pl.BlockSpec((tb, LEAF, RHS), lambda i, a, b: (i, 0, 0)),
        scratch_shapes=[
            pltpu.VMEM((c_total, width, RHS), jnp.bfloat16),
            pltpu.VMEM((f_total, width, RHS), jnp.bfloat16),
            pltpu.VMEM(c_mats.shape, jnp.bfloat16),
            pltpu.VMEM((parents, RANK, RHS), jnp.bfloat16),
            pltpu.VMEM((tb, LEAF, RHS), jnp.float32),
            pltpu.SemaphoreType.DMA((n_seg + halves,)),
        ],
    )
    flops = 2 * (c_mats.size + f_mats.size) * RHS
    bytes_accessed = (c_mats.size + f_mats.size) * 2 + (c_total + f_total) * width * RHS * 2
    return pl.pallas_call(
        kernel,
        grid_spec=grid_spec,
        out_shape=jax.ShapeDtypeStruct((leaves, LEAF, RHS), jnp.bfloat16),
        compiler_params=pltpu.CompilerParams(dimension_semantics=("arbitrary",)),
        cost_estimate=pl.CostEstimate(flops=flops, transcendentals=0, bytes_accessed=bytes_accessed),
    )(c_idx, f_idx, c_mats, f_mats, *[s[0] for s in segs], transfer, leaf_basis, near_field)


def on_device(
    charges,
    leaf_basis,
    transfer,
    near_blocks,
    near_source,
    couple_fine,
    source_fine,
    couple_coarse,
    source_coarse,
    send_fine,
    send_coarse,
):
    leaves = charges.shape[0]
    parents = leaves // 2
    fine_each = send_fine.shape[1] // (2 * REACH)
    coarse_each = send_coarse.shape[1] // (2 * REACH)
    axis = ("leaf", "couple")
    basis_t = leaf_basis.T
    transfer_t = transfer.T
    fine_coeffs, coarse_coeffs, packets = upward(
        charges, basis_t, transfer_t, send_fine[0], send_coarse[0], fine_each, coarse_each
    )
    incoming = []
    for slot, offset in enumerate(offset_list()):
        incoming.append(from_behind(packets[slot], axis, offset))

    each = fine_each + coarse_each
    near_field = gather_dot(
        near_source,
        near_blocks,
        [(incoming[0], 0, HALO, each), (charges, HALO, leaves, 0), (incoming[1], HALO + leaves, HALO, each)],
        near_source.shape[0] // leaves,
    )

    coarse_segments = [(coarse_coeffs, 0, parents, 0)]
    for slot in range(2 * REACH):
        coarse_segments.append((incoming[slot], parents + slot * coarse_each, coarse_each, fine_each))
    fine_segments = [(fine_coeffs, 0, leaves, 0)]
    for slot in range(2 * REACH):
        fine_segments.append((incoming[slot], leaves + slot * fine_each, fine_each, 0))
    return coupled_product(
        (source_coarse, couple_coarse, coarse_segments, source_coarse.shape[0] // parents),
        (source_fine, couple_fine, fine_segments, source_fine.shape[0] // leaves),
        transfer,
        leaf_basis,
        near_field,
    )


def solution(mesh):
    return jax.shard_map(
        on_device,
        mesh=mesh,
        in_specs=(
            P(("leaf", "couple"), None, None),
            P(("leaf", "couple"), None),
            P(("leaf", "couple"), None),
            P(("leaf", "couple"), None),
            P(("leaf", "couple")),
            P(("leaf", "couple"), None),
            P(("leaf", "couple")),
            P(("leaf", "couple"), None),
            P(("leaf", "couple")),
            P(("leaf", "couple"), None),
            P(("leaf", "couple"), None),
        ),
        out_specs=P(("leaf", "couple"), None, None),
        check_vma=False,
    )
```

```python
import functools

import jax
import jax.numpy as jnp
from jax import lax
from jax.experimental import pallas as pl
from jax.experimental.pallas import tpu as pltpu
from jax.sharding import PartitionSpec as P

LEAF = 64
RANK = 64
RHS = 128
HALO = 4
REACH = 3
BLOCK_TARGETS = 16


def from_behind(value, axis, steps):
    count = lax.axis_size(axis)
    first, last = (max(0, -steps), min(count, count - steps))
    return lax.ppermute(value, axis, [(source, source + steps) for source in range(first, last)])


def halo_pieces(block, axis, width):
    count = lax.axis_size(axis)
    forward = [(i, i + 1) for i in range(count - 1)]
    backward = [(target, source) for source, target in forward]
    low = lax.ppermute(lax.slice_in_dim(block, block.shape[0] - width, None, axis=0), axis, forward)
    high = lax.ppermute(lax.slice_in_dim(block, 0, width, axis=0), axis, backward)
    return low, high


def offset_list():
    values = []
    for step in range(REACH):
        values.append(step + 1)
        values.append(-(step + 1))
    return values


def gather_dot(idx, mats, segments, pairs, epilogue=None, out_dtype=jnp.float32):
    rows = mats.shape[0]
    width = mats.shape[1] // pairs
    targets = rows // LEAF
    tb = min(BLOCK_TARGETS, targets)
    steps = targets // tb
    n_seg = len(segments)
    seg_arrays = [s[0] for s in segments]
    seg_meta = [(s[1], s[2], s[3]) for s in segments]
    total = sum(s[2] for s in segments)

    in_specs = [pl.BlockSpec((tb * LEAF, pairs * width), lambda i, ix: (i, 0))]
    for arr in seg_arrays:
        in_specs.append(pl.BlockSpec(memory_space=pl.ANY))
    extra = []
    if epilogue is not None:
        extra, extra_specs, _, out_dtype = epilogue
        in_specs.extend(extra_specs)

    def kernel(idx_ref, mats_ref, *refs):
        seg_refs = refs[:n_seg]
        extra_refs = refs[n_seg:len(refs) - 4]
        out_ref, pool_ref, sem, acc_ref = refs[len(refs) - 4:]
        blk = pl.program_id(0)

        @pl.when(blk == 0)
        def _():
            copies = []
            for j, (ref, (lo, cnt, row)) in enumerate(zip(seg_refs, seg_meta)):
                cp = pltpu.make_async_copy(ref.at[pl.ds(row, cnt)], pool_ref.at[pl.ds(lo, cnt)], sem.at[j])
                cp.start()
                copies.append(cp)
            for cp in copies:
                cp.wait()

        for tt in range(tb):
            base = (blk * tb + tt) * pairs
            blocks = [pool_ref[idx_ref[base + k]] for k in range(pairs)]
            rhs = jnp.concatenate(blocks, axis=0)
            acc = jnp.dot(mats_ref[tt * LEAF:(tt + 1) * LEAF, :], rhs, preferred_element_type=jnp.float32)
            if epilogue is None:
                out_ref[tt] = acc.astype(out_dtype)
            else:
                acc_ref[tt] = acc
        if epilogue is not None:
            epilogue[2](tb, acc_ref, extra_refs, out_ref)

    grid_spec = pltpu.PrefetchScalarGridSpec(
        num_scalar_prefetch=1,
        grid=(steps,),
        in_specs=in_specs,
        out_specs=pl.BlockSpec((tb, LEAF, RHS), lambda i, ix: (i, 0, 0)),
        scratch_shapes=[
            pltpu.VMEM((total, width, RHS), jnp.bfloat16),
            pltpu.SemaphoreType.DMA((n_seg,)),
            pltpu.VMEM((tb if epilogue is not None else 1, LEAF, RHS), jnp.float32),
        ],
    )
    flops = 2 * rows * pairs * width * RHS
    bytes_accessed = mats.size * 2 + total * width * RHS * 2 + targets * LEAF * RHS * 4
    return pl.pallas_call(
        kernel,
        grid_spec=grid_spec,
        out_shape=jax.ShapeDtypeStruct((targets, LEAF, RHS), out_dtype),
        compiler_params=pltpu.CompilerParams(dimension_semantics=("arbitrary",)),
        cost_estimate=pl.CostEstimate(flops=flops, transcendentals=0, bytes_accessed=bytes_accessed),
    )(idx, mats, *seg_arrays, *extra)


def upward(charges, basis_t, transfer_t, send_fine, send_coarse, fine_each, coarse_each):
    leaves = charges.shape[0]
    parents = leaves // 2
    slots = 2 * REACH
    each = fine_each + coarse_each
    sizes = [each + (HALO if q < 2 else 0) for q in range(slots)]

    def kernel(sf_ref, sc_ref, x_ref, v_ref, e_ref, fine_out, coarse_out, *rest):
        packet_refs = rest[:slots]
        fine_v, coarse_v = rest[slots:slots + 2]
        bufs = rest[slots + 2:2 * slots + 2]
        sem = rest[2 * slots + 2]
        for j in range(parents):
            col = j * 2 * RANK
            f0 = jnp.dot(v_ref[:, col:col + RANK], x_ref[2 * j], preferred_element_type=jnp.float32)
            f1 = jnp.dot(v_ref[:, col + RANK:col + 2 * RANK], x_ref[2 * j + 1], preferred_element_type=jnp.float32)
            pair = jnp.concatenate([f0.astype(jnp.bfloat16), f1.astype(jnp.bfloat16)], axis=0)
            fine_v[2 * j] = pair[:RANK]
            fine_v[2 * j + 1] = pair[RANK:]
            e = e_ref[:, col:col + 2 * RANK]
            coarse_v[j] = jnp.dot(e, pair, preferred_element_type=jnp.float32).astype(jnp.bfloat16)

        copies = [
            pltpu.make_async_copy(fine_v, fine_out, sem.at[0]),
            pltpu.make_async_copy(coarse_v, coarse_out, sem.at[1]),
        ]
        for cp in copies:
            cp.start()
        for q in range(slots):
            buf = bufs[q]
            for m in range(fine_each):
                buf[m] = fine_v[jnp.clip(sf_ref[q * fine_each + m], 0, leaves - 1)]
            for m in range(coarse_each):
                buf[fine_each + m] = coarse_v[jnp.clip(sc_ref[q * coarse_each + m], 0, parents - 1)]
            if q == 0:
                buf[each:each + HALO] = x_ref[leaves - HALO:leaves]
            elif q == 1:
                buf[each:each + HALO] = x_ref[0:HALO]
            cp = pltpu.make_async_copy(buf, packet_refs[q], sem.at[2 + q])
            cp.start()
            copies.append(cp)
        for cp in copies:
            cp.wait()

    smem = pl.BlockSpec(memory_space=pltpu.SMEM)
    vmem = pl.BlockSpec(memory_space=pltpu.VMEM)
    hbm = pl.BlockSpec(memory_space=pl.ANY)
    block = jax.ShapeDtypeStruct
    outs = pl.pallas_call(
        kernel,
        in_specs=[smem, smem, vmem, vmem, vmem],
        out_specs=[hbm] * (2 + slots),
        out_shape=[block((leaves, RANK, RHS), jnp.bfloat16), block((parents, RANK, RHS), jnp.bfloat16)]
        + [block((n, RANK, RHS), jnp.bfloat16) for n in sizes],
        scratch_shapes=[
            pltpu.VMEM((leaves, RANK, RHS), jnp.bfloat16),
            pltpu.VMEM((parents, RANK, RHS), jnp.bfloat16),
        ]
        + [pltpu.VMEM((n, RANK, RHS), jnp.bfloat16) for n in sizes]
        + [pltpu.SemaphoreType.DMA((2 + slots,))],
        cost_estimate=pl.CostEstimate(
            flops=2 * leaves * LEAF * RANK * RHS * 2, transcendentals=0, bytes_accessed=16 * 2 ** 20
        ),
    )(send_fine, send_coarse, charges, basis_t, transfer_t)
    return outs[0], outs[1], outs[2:]


def coupled_product(coarse_part, fine_part, transfer, leaf_basis, near_field):
    c_idx, c_mats, c_segs, c_pairs = coarse_part
    f_idx, f_mats, f_segs, f_pairs = fine_part
    width = RANK
    parents = c_mats.shape[0] // RANK
    leaves = f_mats.shape[0] // LEAF
    tb = min(BLOCK_TARGETS, leaves)
    steps = leaves // tb
    halves = 4 if parents % 4 == 0 else 1
    c_rows = parents * RANK // halves
    c_total = sum(s[2] for s in c_segs)
    f_total = sum(s[2] for s in f_segs)
    segs = c_segs + f_segs
    n_c = len(c_segs)
    n_seg = len(segs)

    hbm = pl.BlockSpec(memory_space=pl.ANY)
    in_specs = [hbm] + [pl.BlockSpec((tb * LEAF, f_pairs * width), lambda i, a, b: (i, 0))]
    in_specs += [hbm] * n_seg
    in_specs += [
        pl.BlockSpec((tb * RANK, RANK), lambda i, a, b: (i, 0)),
        pl.BlockSpec((tb * LEAF, RANK), lambda i, a, b: (i, 0)),
        pl.BlockSpec((tb, LEAF, RHS), lambda i, a, b: (i, 0, 0)),
    ]

    def gather_sum(idx_ref, pool_ref, mats, base, pairs):
        blocks = [pool_ref[idx_ref[base + k]] for k in range(pairs)]
        return jnp.dot(mats, jnp.concatenate(blocks, axis=0), preferred_element_type=jnp.float32)

    def kernel(ci_ref, fi_ref, cm_hbm, fm_ref, *refs):
        seg_refs = refs[:n_seg]
        e_ref, v_ref, near_ref, out_ref = refs[n_seg:n_seg + 4]
        c_pool, f_pool, c_mats_v, cr_ref, acc_ref, sem = refs[n_seg + 4:]
        blk = pl.program_id(0)

        @pl.when(blk == 0)
        def _():
            seg_copies = []
            for j, (ref, (_, lo, cnt, row)) in enumerate(zip(seg_refs, segs)):
                pool = c_pool if j < n_c else f_pool
                seg_copies.append(
                    pltpu.make_async_copy(ref.at[pl.ds(row, cnt)], pool.at[pl.ds(lo, cnt)], sem.at[j])
                )
            for cp in seg_copies[:n_c]:
                cp.start()
            mat_copies = []
            for h in range(halves):
                cp = pltpu.make_async_copy(
                    cm_hbm.at[pl.ds(h * c_rows, c_rows)], c_mats_v.at[pl.ds(h * c_rows, c_rows)], sem.at[n_seg + h]
                )
                cp.start()
                mat_copies.append(cp)
            for cp in seg_copies[:n_c]:
                cp.wait()
            per_half = parents // halves
            for h in range(halves):
                mat_copies[h].wait()
                if h == 0:
                    for cp in seg_copies[n_c:]:
                        cp.start()
                for p in range(h * per_half, (h + 1) * per_half):
                    acc = gather_sum(ci_ref, c_pool, c_mats_v[p * RANK:(p + 1) * RANK, :], p * c_pairs, c_pairs)
                    cr_ref[p] = acc.astype(jnp.bfloat16)
            for cp in seg_copies[n_c:]:
                cp.wait()

        for tt in range(tb):
            base = (blk * tb + tt) * f_pairs
            acc_ref[tt] = gather_sum(fi_ref, f_pool, fm_ref[tt * LEAF:(tt + 1) * LEAF, :], base, f_pairs)
        rounded = []
        for tt in range(tb):
            e = e_ref[tt * RANK:(tt + 1) * RANK, :]
            down = jnp.dot(e, cr_ref[(blk * tb + tt) // 2], preferred_element_type=jnp.float32)
            rounded.append((acc_ref[tt] + down).astype(jnp.bfloat16))
        for tt in range(tb):
            v = v_ref[tt * LEAF:(tt + 1) * LEAF, :]
            far = jnp.dot(v, rounded[tt], preferred_element_type=jnp.float32)
            out_ref[tt] = (far + near_ref[tt]).astype(jnp.bfloat16)

    grid_spec = pltpu.PrefetchScalarGridSpec(
        num_scalar_prefetch=2,
        grid=(steps,),
        in_specs=in_specs,
        out_specs=pl.BlockSpec((tb, LEAF, RHS), lambda i, a, b: (i, 0, 0)),
        scratch_shapes=[
            pltpu.VMEM((c_total, width, RHS), jnp.bfloat16),
            pltpu.VMEM((f_total, width, RHS), jnp.bfloat16),
            pltpu.VMEM(c_mats.shape, jnp.bfloat16),
            pltpu.VMEM((parents, RANK, RHS), jnp.bfloat16),
            pltpu.VMEM((tb, LEAF, RHS), jnp.float32),
            pltpu.SemaphoreType.DMA((n_seg + halves,)),
        ],
    )
    flops = 2 * (c_mats.size + f_mats.size) * RHS
    bytes_accessed = (c_mats.size + f_mats.size) * 2 + (c_total + f_total) * width * RHS * 2
    return pl.pallas_call(
        kernel,
        grid_spec=grid_spec,
        out_shape=jax.ShapeDtypeStruct((leaves, LEAF, RHS), jnp.bfloat16),
        compiler_params=pltpu.CompilerParams(dimension_semantics=("arbitrary",)),
        cost_estimate=pl.CostEstimate(flops=flops, transcendentals=0, bytes_accessed=bytes_accessed),
    )(c_idx, f_idx, c_mats, f_mats, *[s[0] for s in segs], transfer, leaf_basis, near_field)


def on_device(
    charges,
    leaf_basis,
    transfer,
    near_blocks,
    near_source,
    couple_fine,
    source_fine,
    couple_coarse,
    source_coarse,
    send_fine,
    send_coarse,
):
    leaves = charges.shape[0]
    parents = leaves // 2
    fine_each = send_fine.shape[1] // (2 * REACH)
    coarse_each = send_coarse.shape[1] // (2 * REACH)
    axis = ("leaf", "couple")
    basis_t = leaf_basis.T
    transfer_t = transfer.T
    fine_coeffs, coarse_coeffs, packets = upward(
        charges, basis_t, transfer_t, send_fine[0], send_coarse[0], fine_each, coarse_each
    )
    incoming = []
    for slot, offset in enumerate(offset_list()):
        incoming.append(from_behind(packets[slot], axis, offset))

    each = fine_each + coarse_each
    near_field = gather_dot(
        near_source,
        near_blocks,
        [(incoming[0], 0, HALO, each), (charges, HALO, leaves, 0), (incoming[1], HALO + leaves, HALO, each)],
        near_source.shape[0] // leaves,
    )

    coarse_segments = [(coarse_coeffs, 0, parents, 0)]
    for slot in range(2 * REACH):
        coarse_segments.append((incoming[slot], parents + slot * coarse_each, coarse_each, fine_each))
    fine_segments = [(fine_coeffs, 0, leaves, 0)]
    for slot in range(2 * REACH):
        fine_segments.append((incoming[slot], leaves + slot * fine_each, fine_each, 0))
    return coupled_product(
        (source_coarse, couple_coarse, coarse_segments, source_coarse.shape[0] // parents),
        (source_fine, couple_fine, fine_segments, source_fine.shape[0] // leaves),
        transfer,
        leaf_basis,
        near_field,
    )


def solution(mesh):
    return jax.shard_map(
        on_device,
        mesh=mesh,
        in_specs=(
            P(("leaf", "couple"), None, None),
            P(("leaf", "couple"), None),
            P(("leaf", "couple"), None),
            P(("leaf", "couple"), None),
            P(("leaf", "couple")),
            P(("leaf", "couple"), None),
            P(("leaf", "couple")),
            P(("leaf", "couple"), None),
            P(("leaf", "couple")),
            P(("leaf", "couple"), None),
            P(("leaf", "couple"), None),
        ),
        out_specs=P(("leaf", "couple"), None, None),
        check_vma=False,
    )
```

```python
import functools

import jax
import jax.numpy as jnp
from jax import lax
from jax.experimental import pallas as pl
from jax.experimental.pallas import tpu as pltpu
from jax.sharding import PartitionSpec as P

LEAF = 64
RANK = 64
RHS = 128
HALO = 4
REACH = 3
BLOCK_TARGETS = 16


def from_behind(value, axis, steps):
    count = lax.axis_size(axis)
    first, last = (max(0, -steps), min(count, count - steps))
    return lax.ppermute(value, axis, [(source, source + steps) for source in range(first, last)])


def halo_pieces(block, axis, width):
    count = lax.axis_size(axis)
    forward = [(i, i + 1) for i in range(count - 1)]
    backward = [(target, source) for source, target in forward]
    low = lax.ppermute(lax.slice_in_dim(block, block.shape[0] - width, None, axis=0), axis, forward)
    high = lax.ppermute(lax.slice_in_dim(block, 0, width, axis=0), axis, backward)
    return low, high


def offset_list():
    values = []
    for step in range(REACH):
        values.append(step + 1)
        values.append(-(step + 1))
    return values


def gather_dot(idx, mats, segments, pairs, epilogue=None, out_dtype=jnp.float32):
    rows = mats.shape[0]
    width = mats.shape[1] // pairs
    targets = rows // LEAF
    tb = min(BLOCK_TARGETS, targets)
    steps = targets // tb
    n_seg = len(segments)
    seg_arrays = [s[0] for s in segments]
    seg_meta = [(s[1], s[2], s[3]) for s in segments]
    total = sum(s[2] for s in segments)

    in_specs = [pl.BlockSpec((tb * LEAF, pairs * width), lambda i, ix: (i, 0))]
    for arr in seg_arrays:
        in_specs.append(pl.BlockSpec(memory_space=pl.ANY))
    extra = []
    if epilogue is not None:
        extra, extra_specs, _, out_dtype = epilogue
        in_specs.extend(extra_specs)

    def kernel(idx_ref, mats_ref, *refs):
        seg_refs = refs[:n_seg]
        extra_refs = refs[n_seg:len(refs) - 4]
        out_ref, pool_ref, sem, acc_ref = refs[len(refs) - 4:]
        blk = pl.program_id(0)

        @pl.when(blk == 0)
        def _():
            copies = []
            for j, (ref, (lo, cnt, row)) in enumerate(zip(seg_refs, seg_meta)):
                cp = pltpu.make_async_copy(ref.at[pl.ds(row, cnt)], pool_ref.at[pl.ds(lo, cnt)], sem.at[j])
                cp.start()
                copies.append(cp)
            for cp in copies:
                cp.wait()

        for tt in range(tb):
            base = (blk * tb + tt) * pairs
            blocks = [pool_ref[idx_ref[base + k]] for k in range(pairs)]
            rhs = jnp.concatenate(blocks, axis=0)
            acc = jnp.dot(mats_ref[tt * LEAF:(tt + 1) * LEAF, :], rhs, preferred_element_type=jnp.float32)
            if epilogue is None:
                out_ref[tt] = acc.astype(out_dtype)
            else:
                acc_ref[tt] = acc
        if epilogue is not None:
            epilogue[2](tb, acc_ref, extra_refs, out_ref)

    grid_spec = pltpu.PrefetchScalarGridSpec(
        num_scalar_prefetch=1,
        grid=(steps,),
        in_specs=in_specs,
        out_specs=pl.BlockSpec((tb, LEAF, RHS), lambda i, ix: (i, 0, 0)),
        scratch_shapes=[
            pltpu.VMEM((total, width, RHS), jnp.bfloat16),
            pltpu.SemaphoreType.DMA((n_seg,)),
            pltpu.VMEM((tb if epilogue is not None else 1, LEAF, RHS), jnp.float32),
        ],
    )
    flops = 2 * rows * pairs * width * RHS
    bytes_accessed = mats.size * 2 + total * width * RHS * 2 + targets * LEAF * RHS * 4
    return pl.pallas_call(
        kernel,
        grid_spec=grid_spec,
        out_shape=jax.ShapeDtypeStruct((targets, LEAF, RHS), out_dtype),
        compiler_params=pltpu.CompilerParams(dimension_semantics=("arbitrary",)),
        cost_estimate=pl.CostEstimate(flops=flops, transcendentals=0, bytes_accessed=bytes_accessed),
    )(idx, mats, *seg_arrays, *extra)


def upward(charges, basis_t, transfer_t, send_fine, send_coarse, fine_each, coarse_each, packets):
    leaves = charges.shape[0]
    parents = leaves // 2
    slots = 2 * REACH
    each = fine_each + coarse_each
    sizes = [each + (HALO if q < 2 else 0) for q in range(slots)]
    chunks = 4 if parents % 4 == 0 else 1
    per = parents // chunks

    def kernel(sf_ref, sc_ref, x_hbm, v_hbm, e_hbm, *rest):
        n_out = slots if packets else 2
        outs = rest[:n_out]
        x_ref, v_ref, e_ref, fine_v, coarse_v = rest[n_out:n_out + 5]
        bufs = rest[n_out + 5:len(rest) - 2]
        in_sem, sem = rest[len(rest) - 2:]
        loads = []
        for c in range(chunks):
            lo, cols = 2 * c * per, 2 * c * per * RANK
            span = pl.ds(cols, 2 * per * RANK)
            trio = [
                pltpu.make_async_copy(x_hbm.at[pl.ds(lo, 2 * per)], x_ref.at[pl.ds(lo, 2 * per)], in_sem.at[3 * c]),
                pltpu.make_async_copy(v_hbm.at[:, span], v_ref.at[:, span], in_sem.at[3 * c + 1]),
                pltpu.make_async_copy(e_hbm.at[:, span], e_ref.at[:, span], in_sem.at[3 * c + 2]),
            ]
            for cp in trio:
                cp.start()
            loads.append(trio)
        for c in range(chunks):
            for cp in loads[c]:
                cp.wait()
            for j in range(c * per, (c + 1) * per):
                col = j * 2 * RANK
                f0 = jnp.dot(v_ref[:, col:col + RANK], x_ref[2 * j], preferred_element_type=jnp.float32)
                f1 = jnp.dot(v_ref[:, col + RANK:col + 2 * RANK], x_ref[2 * j + 1], preferred_element_type=jnp.float32)
                pair = jnp.concatenate([f0.astype(jnp.bfloat16), f1.astype(jnp.bfloat16)], axis=0)
                fine_v[2 * j] = pair[:RANK]
                fine_v[2 * j + 1] = pair[RANK:]
                e = e_ref[:, col:col + 2 * RANK]
                coarse_v[j] = jnp.dot(e, pair, preferred_element_type=jnp.float32).astype(jnp.bfloat16)

        copies = []
        if not packets:
            copies = [
                pltpu.make_async_copy(fine_v, outs[0], sem.at[0]),
                pltpu.make_async_copy(coarse_v, outs[1], sem.at[1]),
            ]
            for cp in copies:
                cp.start()
        else:
            for q in range(slots):
                buf = bufs[q]
                for m in range(fine_each):
                    buf[m] = fine_v[sf_ref[q * fine_each + m]]
                for m in range(coarse_each):
                    buf[fine_each + m] = coarse_v[sc_ref[q * coarse_each + m]]
                if q == 0:
                    buf[each:each + HALO] = x_ref[leaves - HALO:leaves]
                elif q == 1:
                    buf[each:each + HALO] = x_ref[0:HALO]
                cp = pltpu.make_async_copy(buf, outs[q], sem.at[q])
                cp.start()
                copies.append(cp)
        for cp in copies:
            cp.wait()

    smem = pl.BlockSpec(memory_space=pltpu.SMEM)
    hbm = pl.BlockSpec(memory_space=pl.ANY)
    block = jax.ShapeDtypeStruct
    if packets:
        out_shape = [block((n, RANK, RHS), jnp.bfloat16) for n in sizes]
        bufs = [pltpu.VMEM((n, RANK, RHS), jnp.bfloat16) for n in sizes]
    else:
        out_shape = [block((leaves, RANK, RHS), jnp.bfloat16), block((parents, RANK, RHS), jnp.bfloat16)]
        bufs = []
    return pl.pallas_call(
        kernel,
        in_specs=[smem, smem, hbm, hbm, hbm],
        out_specs=[hbm] * len(out_shape),
        out_shape=out_shape,
        scratch_shapes=[
            pltpu.VMEM(charges.shape, jnp.bfloat16),
            pltpu.VMEM(basis_t.shape, jnp.bfloat16),
            pltpu.VMEM(transfer_t.shape, jnp.bfloat16),
            pltpu.VMEM((leaves, RANK, RHS), jnp.bfloat16),
            pltpu.VMEM((parents, RANK, RHS), jnp.bfloat16),
        ]
        + bufs
        + [pltpu.SemaphoreType.DMA((3 * chunks,)), pltpu.SemaphoreType.DMA((len(out_shape),))],
        cost_estimate=pl.CostEstimate(
            flops=2 * leaves * LEAF * RANK * RHS * 2, transcendentals=0, bytes_accessed=8 * 2 ** 20
        ),
    )(send_fine, send_coarse, charges, basis_t, transfer_t)


def coupled_product(coarse_part, fine_part, transfer, leaf_basis, near_field):
    c_idx, c_mats, c_segs, c_pairs = coarse_part
    f_idx, f_mats, f_segs, f_pairs = fine_part
    width = RANK
    parents = c_mats.shape[0] // RANK
    leaves = f_mats.shape[0] // LEAF
    tb = min(BLOCK_TARGETS, leaves)
    steps = leaves // tb
    halves = 4 if parents % 4 == 0 else 1
    c_rows = parents * RANK // halves
    c_total = sum(s[2] for s in c_segs)
    f_total = sum(s[2] for s in f_segs)
    segs = c_segs + f_segs
    n_c = len(c_segs)
    n_seg = len(segs)

    hbm = pl.BlockSpec(memory_space=pl.ANY)
    in_specs = [hbm] + [pl.BlockSpec((tb * LEAF, f_pairs * width), lambda i, a, b: (i, 0))]
    in_specs += [hbm] * n_seg
    in_specs += [
        pl.BlockSpec((tb * RANK, RANK), lambda i, a, b: (i, 0)),
        pl.BlockSpec((tb * LEAF, RANK), lambda i, a, b: (i, 0)),
        pl.BlockSpec((tb, LEAF, RHS), lambda i, a, b: (i, 0, 0)),
    ]

    def gather_sum(idx_ref, pool_ref, mats, base, pairs):
        blocks = [pool_ref[idx_ref[base + k]] for k in range(pairs)]
        return jnp.dot(mats, jnp.concatenate(blocks, axis=0), preferred_element_type=jnp.float32)

    def kernel(ci_ref, fi_ref, cm_hbm, fm_ref, *refs):
        seg_refs = refs[:n_seg]
        e_ref, v_ref, near_ref, out_ref = refs[n_seg:n_seg + 4]
        c_pool, f_pool, c_mats_v, cr_ref, acc_ref, sem = refs[n_seg + 4:]
        blk = pl.program_id(0)

        @pl.when(blk == 0)
        def _():
            seg_copies = []
            for j, (ref, (_, lo, cnt, row)) in enumerate(zip(seg_refs, segs)):
                pool = c_pool if j < n_c else f_pool
                seg_copies.append(
                    pltpu.make_async_copy(ref.at[pl.ds(row, cnt)], pool.at[pl.ds(lo, cnt)], sem.at[j])
                )
            for cp in seg_copies[:n_c]:
                cp.start()
            mat_copies = []
            for h in range(halves):
                cp = pltpu.make_async_copy(
                    cm_hbm.at[pl.ds(h * c_rows, c_rows)], c_mats_v.at[pl.ds(h * c_rows, c_rows)], sem.at[n_seg + h]
                )
                cp.start()
                mat_copies.append(cp)
            for cp in seg_copies[:n_c]:
                cp.wait()
            per_half = parents // halves
            for h in range(halves):
                mat_copies[h].wait()
                if h == 0:
                    for cp in seg_copies[n_c:]:
                        cp.start()
                for p in range(h * per_half, (h + 1) * per_half):
                    acc = gather_sum(ci_ref, c_pool, c_mats_v[p * RANK:(p + 1) * RANK, :], p * c_pairs, c_pairs)
                    cr_ref[p] = acc.astype(jnp.bfloat16)
            for cp in seg_copies[n_c:]:
                cp.wait()

        for tt in range(tb):
            base = (blk * tb + tt) * f_pairs
            acc_ref[tt] = gather_sum(fi_ref, f_pool, fm_ref[tt * LEAF:(tt + 1) * LEAF, :], base, f_pairs)
        rounded = []
        for tt in range(tb):
            e = e_ref[tt * RANK:(tt + 1) * RANK, :]
            down = jnp.dot(e, cr_ref[(blk * tb + tt) // 2], preferred_element_type=jnp.float32)
            rounded.append((acc_ref[tt] + down).astype(jnp.bfloat16))
        for tt in range(tb):
            v = v_ref[tt * LEAF:(tt + 1) * LEAF, :]
            far = jnp.dot(v, rounded[tt], preferred_element_type=jnp.float32)
            out_ref[tt] = (far + near_ref[tt]).astype(jnp.bfloat16)

    grid_spec = pltpu.PrefetchScalarGridSpec(
        num_scalar_prefetch=2,
        grid=(steps,),
        in_specs=in_specs,
        out_specs=pl.BlockSpec((tb, LEAF, RHS), lambda i, a, b: (i, 0, 0)),
        scratch_shapes=[
            pltpu.VMEM((c_total, width, RHS), jnp.bfloat16),
            pltpu.VMEM((f_total, width, RHS), jnp.bfloat16),
            pltpu.VMEM(c_mats.shape, jnp.bfloat16),
            pltpu.VMEM((parents, RANK, RHS), jnp.bfloat16),
            pltpu.VMEM((tb, LEAF, RHS), jnp.float32),
            pltpu.SemaphoreType.DMA((n_seg + halves,)),
        ],
    )
    flops = 2 * (c_mats.size + f_mats.size) * RHS
    bytes_accessed = (c_mats.size + f_mats.size) * 2 + (c_total + f_total) * width * RHS * 2
    return pl.pallas_call(
        kernel,
        grid_spec=grid_spec,
        out_shape=jax.ShapeDtypeStruct((leaves, LEAF, RHS), jnp.bfloat16),
        compiler_params=pltpu.CompilerParams(dimension_semantics=("arbitrary",)),
        cost_estimate=pl.CostEstimate(flops=flops, transcendentals=0, bytes_accessed=bytes_accessed),
    )(c_idx, f_idx, c_mats, f_mats, *[s[0] for s in segs], transfer, leaf_basis, near_field)


def on_device(
    charges,
    leaf_basis,
    transfer,
    near_blocks,
    near_source,
    couple_fine,
    source_fine,
    couple_coarse,
    source_coarse,
    send_fine,
    send_coarse,
):
    leaves = charges.shape[0]
    parents = leaves // 2
    fine_each = send_fine.shape[1] // (2 * REACH)
    coarse_each = send_coarse.shape[1] // (2 * REACH)
    axis = ("leaf", "couple")
    basis_t = leaf_basis.T
    transfer_t = transfer.T
    packets = upward(
        charges, basis_t, transfer_t, send_fine[0], send_coarse[0], fine_each, coarse_each, True
    )
    fine_coeffs, coarse_coeffs = upward(
        charges, basis_t, transfer_t, send_fine[0], send_coarse[0], fine_each, coarse_each, False
    )
    incoming = []
    for slot, offset in enumerate(offset_list()):
        incoming.append(from_behind(packets[slot], axis, offset))

    each = fine_each + coarse_each
    near_field = gather_dot(
        near_source,
        near_blocks,
        [(incoming[0], 0, HALO, each), (charges, HALO, leaves, 0), (incoming[1], HALO + leaves, HALO, each)],
        near_source.shape[0] // leaves,
    )

    coarse_segments = [(coarse_coeffs, 0, parents, 0)]
    for slot in range(2 * REACH):
        coarse_segments.append((incoming[slot], parents + slot * coarse_each, coarse_each, fine_each))
    fine_segments = [(fine_coeffs, 0, leaves, 0)]
    for slot in range(2 * REACH):
        fine_segments.append((incoming[slot], leaves + slot * fine_each, fine_each, 0))
    return coupled_product(
        (source_coarse, couple_coarse, coarse_segments, source_coarse.shape[0] // parents),
        (source_fine, couple_fine, fine_segments, source_fine.shape[0] // leaves),
        transfer,
        leaf_basis,
        near_field,
    )


def solution(mesh):
    return jax.shard_map(
        on_device,
        mesh=mesh,
        in_specs=(
            P(("leaf", "couple"), None, None),
            P(("leaf", "couple"), None),
            P(("leaf", "couple"), None),
            P(("leaf", "couple"), None),
            P(("leaf", "couple")),
            P(("leaf", "couple"), None),
            P(("leaf", "couple")),
            P(("leaf", "couple"), None),
            P(("leaf", "couple")),
            P(("leaf", "couple"), None),
            P(("leaf", "couple"), None),
        ),
        out_specs=P(("leaf", "couple"), None, None),
        check_vma=False,
    )
```

```python
import functools

import jax
import jax.numpy as jnp
from jax import lax
from jax.experimental import pallas as pl
from jax.experimental.pallas import tpu as pltpu
from jax.sharding import PartitionSpec as P

LEAF = 64
RANK = 64
RHS = 128
HALO = 4
REACH = 3
BLOCK_TARGETS = 16


def from_behind(value, axis, steps):
    count = lax.axis_size(axis)
    first, last = (max(0, -steps), min(count, count - steps))
    return lax.ppermute(value, axis, [(source, source + steps) for source in range(first, last)])


def halo_pieces(block, axis, width):
    count = lax.axis_size(axis)
    forward = [(i, i + 1) for i in range(count - 1)]
    backward = [(target, source) for source, target in forward]
    low = lax.ppermute(lax.slice_in_dim(block, block.shape[0] - width, None, axis=0), axis, forward)
    high = lax.ppermute(lax.slice_in_dim(block, 0, width, axis=0), axis, backward)
    return low, high


def offset_list():
    values = []
    for step in range(REACH):
        values.append(step + 1)
        values.append(-(step + 1))
    return values


def gather_dot(idx, mats, segments, pairs, epilogue=None, out_dtype=jnp.float32):
    rows = mats.shape[0]
    width = mats.shape[1] // pairs
    targets = rows // LEAF
    tb = min(BLOCK_TARGETS, targets)
    steps = targets // tb
    n_seg = len(segments)
    seg_arrays = [s[0] for s in segments]
    seg_meta = [(s[1], s[2], s[3]) for s in segments]
    total = sum(s[2] for s in segments)

    in_specs = [pl.BlockSpec((tb * LEAF, pairs * width), lambda i, ix: (i, 0))]
    for arr in seg_arrays:
        in_specs.append(pl.BlockSpec(memory_space=pl.ANY))
    extra = []
    if epilogue is not None:
        extra, extra_specs, _, out_dtype = epilogue
        in_specs.extend(extra_specs)

    def kernel(idx_ref, mats_ref, *refs):
        seg_refs = refs[:n_seg]
        extra_refs = refs[n_seg:len(refs) - 4]
        out_ref, pool_ref, sem, acc_ref = refs[len(refs) - 4:]
        blk = pl.program_id(0)

        @pl.when(blk == 0)
        def _():
            copies = []
            for j, (ref, (lo, cnt, row)) in enumerate(zip(seg_refs, seg_meta)):
                cp = pltpu.make_async_copy(ref.at[pl.ds(row, cnt)], pool_ref.at[pl.ds(lo, cnt)], sem.at[j])
                cp.start()
                copies.append(cp)
            for cp in copies:
                cp.wait()

        for tt in range(tb):
            base = (blk * tb + tt) * pairs
            blocks = [pool_ref[idx_ref[base + k]] for k in range(pairs)]
            rhs = jnp.concatenate(blocks, axis=0)
            acc = jnp.dot(mats_ref[tt * LEAF:(tt + 1) * LEAF, :], rhs, preferred_element_type=jnp.float32)
            if epilogue is None:
                out_ref[tt] = acc.astype(out_dtype)
            else:
                acc_ref[tt] = acc
        if epilogue is not None:
            epilogue[2](tb, acc_ref, extra_refs, out_ref)

    grid_spec = pltpu.PrefetchScalarGridSpec(
        num_scalar_prefetch=1,
        grid=(steps,),
        in_specs=in_specs,
        out_specs=pl.BlockSpec((tb, LEAF, RHS), lambda i, ix: (i, 0, 0)),
        scratch_shapes=[
            pltpu.VMEM((total, width, RHS), jnp.bfloat16),
            pltpu.SemaphoreType.DMA((n_seg,)),
            pltpu.VMEM((tb if epilogue is not None else 1, LEAF, RHS), jnp.float32),
        ],
    )
    flops = 2 * rows * pairs * width * RHS
    bytes_accessed = mats.size * 2 + total * width * RHS * 2 + targets * LEAF * RHS * 4
    return pl.pallas_call(
        kernel,
        grid_spec=grid_spec,
        out_shape=jax.ShapeDtypeStruct((targets, LEAF, RHS), out_dtype),
        compiler_params=pltpu.CompilerParams(dimension_semantics=("arbitrary",)),
        cost_estimate=pl.CostEstimate(flops=flops, transcendentals=0, bytes_accessed=bytes_accessed),
    )(idx, mats, *seg_arrays, *extra)


def upward(charges, basis_t, transfer_t, send_fine, send_coarse, fine_each, coarse_each, packets):
    leaves = charges.shape[0]
    parents = leaves // 2
    slots = 2 * REACH
    each = fine_each + coarse_each
    sizes = [each + (HALO if q < 2 else 0) for q in range(slots)]
    chunks = 4 if parents % 4 == 0 else 1
    per = parents // chunks

    def kernel(sf_ref, sc_ref, x_ref, v_ref, e_ref, *rest):
        n_out = slots if packets else 2
        outs = rest[:n_out]
        fine_v, coarse_v = rest[n_out:n_out + 2]
        bufs = rest[n_out + 2:len(rest) - 1]
        sem = rest[len(rest) - 1]
        for c in range(chunks):
            for j in range(c * per, (c + 1) * per):
                col = j * 2 * RANK
                f0 = jnp.dot(v_ref[:, col:col + RANK], x_ref[2 * j], preferred_element_type=jnp.float32)
                f1 = jnp.dot(v_ref[:, col + RANK:col + 2 * RANK], x_ref[2 * j + 1], preferred_element_type=jnp.float32)
                pair = jnp.concatenate([f0.astype(jnp.bfloat16), f1.astype(jnp.bfloat16)], axis=0)
                fine_v[2 * j] = pair[:RANK]
                fine_v[2 * j + 1] = pair[RANK:]
                e = e_ref[:, col:col + 2 * RANK]
                coarse_v[j] = jnp.dot(e, pair, preferred_element_type=jnp.float32).astype(jnp.bfloat16)

        copies = []
        if not packets:
            copies = [
                pltpu.make_async_copy(fine_v, outs[0], sem.at[0]),
                pltpu.make_async_copy(coarse_v, outs[1], sem.at[1]),
            ]
            for cp in copies:
                cp.start()
        else:
            for q in range(slots):
                buf = bufs[q]
                for m in range(fine_each):
                    buf[m] = fine_v[sf_ref[q * fine_each + m]]
                for m in range(coarse_each):
                    buf[fine_each + m] = coarse_v[sc_ref[q * coarse_each + m]]
                if q == 0:
                    buf[each:each + HALO] = x_ref[leaves - HALO:leaves]
                elif q == 1:
                    buf[each:each + HALO] = x_ref[0:HALO]
                cp = pltpu.make_async_copy(buf, outs[q], sem.at[q])
                cp.start()
                copies.append(cp)
        for cp in copies:
            cp.wait()

    smem = pl.BlockSpec(memory_space=pltpu.SMEM)
    vmem = pl.BlockSpec(memory_space=pltpu.VMEM)
    hbm = pl.BlockSpec(memory_space=pl.ANY)
    block = jax.ShapeDtypeStruct
    if packets:
        out_shape = [block((n, RANK, RHS), jnp.bfloat16) for n in sizes]
        bufs = [pltpu.VMEM((n, RANK, RHS), jnp.bfloat16) for n in sizes]
    else:
        out_shape = [block((leaves, RANK, RHS), jnp.bfloat16), block((parents, RANK, RHS), jnp.bfloat16)]
        bufs = []
    return pl.pallas_call(
        kernel,
        in_specs=[smem, smem, vmem, vmem, vmem],
        out_specs=[hbm] * len(out_shape),
        out_shape=out_shape,
        scratch_shapes=[
            pltpu.VMEM((leaves, RANK, RHS), jnp.bfloat16),
            pltpu.VMEM((parents, RANK, RHS), jnp.bfloat16),
        ]
        + bufs
        + [pltpu.SemaphoreType.DMA((len(out_shape),))],
        cost_estimate=pl.CostEstimate(
            flops=2 * leaves * LEAF * RANK * RHS * 2, transcendentals=0, bytes_accessed=8 * 2 ** 20
        ),
    )(send_fine, send_coarse, charges, basis_t, transfer_t)


def coupled_product(coarse_part, fine_part, transfer, leaf_basis, near_field):
    c_idx, c_mats, c_segs, c_pairs = coarse_part
    f_idx, f_mats, f_segs, f_pairs = fine_part
    width = RANK
    parents = c_mats.shape[0] // RANK
    leaves = f_mats.shape[0] // LEAF
    tb = min(BLOCK_TARGETS, leaves)
    steps = leaves // tb
    halves = 4 if parents % 4 == 0 else 1
    c_rows = parents * RANK // halves
    c_total = sum(s[2] for s in c_segs)
    f_total = sum(s[2] for s in f_segs)
    segs = c_segs + f_segs
    n_c = len(c_segs)
    n_seg = len(segs)

    hbm = pl.BlockSpec(memory_space=pl.ANY)
    in_specs = [hbm] + [pl.BlockSpec((tb * LEAF, f_pairs * width), lambda i, a, b: (i, 0))]
    in_specs += [hbm] * n_seg
    in_specs += [
        pl.BlockSpec((tb * RANK, RANK), lambda i, a, b: (i, 0)),
        pl.BlockSpec((tb * LEAF, RANK), lambda i, a, b: (i, 0)),
        pl.BlockSpec((tb, LEAF, RHS), lambda i, a, b: (i, 0, 0)),
    ]

    def gather_sum(idx_ref, pool_ref, mats, base, pairs):
        blocks = [pool_ref[idx_ref[base + k]] for k in range(pairs)]
        return jnp.dot(mats, jnp.concatenate(blocks, axis=0), preferred_element_type=jnp.float32)

    def kernel(ci_ref, fi_ref, cm_hbm, fm_ref, *refs):
        seg_refs = refs[:n_seg]
        e_ref, v_ref, near_ref, out_ref = refs[n_seg:n_seg + 4]
        c_pool, f_pool, c_mats_v, cr_ref, acc_ref, sem = refs[n_seg + 4:]
        blk = pl.program_id(0)

        @pl.when(blk == 0)
        def _():
            seg_copies = []
            for j, (ref, (_, lo, cnt, row)) in enumerate(zip(seg_refs, segs)):
                pool = c_pool if j < n_c else f_pool
                seg_copies.append(
                    pltpu.make_async_copy(ref.at[pl.ds(row, cnt)], pool.at[pl.ds(lo, cnt)], sem.at[j])
                )
            for cp in seg_copies[:n_c]:
                cp.start()
            mat_copies = []
            for h in range(halves):
                cp = pltpu.make_async_copy(
                    cm_hbm.at[pl.ds(h * c_rows, c_rows)], c_mats_v.at[pl.ds(h * c_rows, c_rows)], sem.at[n_seg + h]
                )
                cp.start()
                mat_copies.append(cp)
            for cp in seg_copies[:n_c]:
                cp.wait()
            per_half = parents // halves
            for h in range(halves):
                mat_copies[h].wait()
                if h == 0:
                    for cp in seg_copies[n_c:]:
                        cp.start()
                for p in range(h * per_half, (h + 1) * per_half):
                    acc = gather_sum(ci_ref, c_pool, c_mats_v[p * RANK:(p + 1) * RANK, :], p * c_pairs, c_pairs)
                    cr_ref[p] = acc.astype(jnp.bfloat16)
            for cp in seg_copies[n_c:]:
                cp.wait()

        for tt in range(tb):
            base = (blk * tb + tt) * f_pairs
            acc_ref[tt] = gather_sum(fi_ref, f_pool, fm_ref[tt * LEAF:(tt + 1) * LEAF, :], base, f_pairs)
        rounded = []
        for tt in range(tb):
            e = e_ref[tt * RANK:(tt + 1) * RANK, :]
            down = jnp.dot(e, cr_ref[(blk * tb + tt) // 2], preferred_element_type=jnp.float32)
            rounded.append((acc_ref[tt] + down).astype(jnp.bfloat16))
        for tt in range(tb):
            v = v_ref[tt * LEAF:(tt + 1) * LEAF, :]
            far = jnp.dot(v, rounded[tt], preferred_element_type=jnp.float32)
            out_ref[tt] = (far + near_ref[tt]).astype(jnp.bfloat16)

    grid_spec = pltpu.PrefetchScalarGridSpec(
        num_scalar_prefetch=2,
        grid=(steps,),
        in_specs=in_specs,
        out_specs=pl.BlockSpec((tb, LEAF, RHS), lambda i, a, b: (i, 0, 0)),
        scratch_shapes=[
            pltpu.VMEM((c_total, width, RHS), jnp.bfloat16),
            pltpu.VMEM((f_total, width, RHS), jnp.bfloat16),
            pltpu.VMEM(c_mats.shape, jnp.bfloat16),
            pltpu.VMEM((parents, RANK, RHS), jnp.bfloat16),
            pltpu.VMEM((tb, LEAF, RHS), jnp.float32),
            pltpu.SemaphoreType.DMA((n_seg + halves,)),
        ],
    )
    flops = 2 * (c_mats.size + f_mats.size) * RHS
    bytes_accessed = (c_mats.size + f_mats.size) * 2 + (c_total + f_total) * width * RHS * 2
    return pl.pallas_call(
        kernel,
        grid_spec=grid_spec,
        out_shape=jax.ShapeDtypeStruct((leaves, LEAF, RHS), jnp.bfloat16),
        compiler_params=pltpu.CompilerParams(dimension_semantics=("arbitrary",)),
        cost_estimate=pl.CostEstimate(flops=flops, transcendentals=0, bytes_accessed=bytes_accessed),
    )(c_idx, f_idx, c_mats, f_mats, *[s[0] for s in segs], transfer, leaf_basis, near_field)


def on_device(
    charges,
    leaf_basis,
    transfer,
    near_blocks,
    near_source,
    couple_fine,
    source_fine,
    couple_coarse,
    source_coarse,
    send_fine,
    send_coarse,
):
    leaves = charges.shape[0]
    parents = leaves // 2
    fine_each = send_fine.shape[1] // (2 * REACH)
    coarse_each = send_coarse.shape[1] // (2 * REACH)
    axis = ("leaf", "couple")
    basis_t = leaf_basis.T
    transfer_t = transfer.T
    packets = upward(
        charges, basis_t, transfer_t, send_fine[0], send_coarse[0], fine_each, coarse_each, True
    )
    fine_coeffs, coarse_coeffs = upward(
        charges, basis_t, transfer_t, send_fine[0], send_coarse[0], fine_each, coarse_each, False
    )
    incoming = []
    for slot, offset in enumerate(offset_list()):
        incoming.append(from_behind(packets[slot], axis, offset))

    each = fine_each + coarse_each
    near_field = gather_dot(
        near_source,
        near_blocks,
        [(incoming[0], 0, HALO, each), (charges, HALO, leaves, 0), (incoming[1], HALO + leaves, HALO, each)],
        near_source.shape[0] // leaves,
    )

    coarse_segments = [(coarse_coeffs, 0, parents, 0)]
    for slot in range(2 * REACH):
        coarse_segments.append((incoming[slot], parents + slot * coarse_each, coarse_each, fine_each))
    fine_segments = [(fine_coeffs, 0, leaves, 0)]
    for slot in range(2 * REACH):
        fine_segments.append((incoming[slot], leaves + slot * fine_each, fine_each, 0))
    return coupled_product(
        (source_coarse, couple_coarse, coarse_segments, source_coarse.shape[0] // parents),
        (source_fine, couple_fine, fine_segments, source_fine.shape[0] // leaves),
        transfer,
        leaf_basis,
        near_field,
    )


def solution(mesh):
    return jax.shard_map(
        on_device,
        mesh=mesh,
        in_specs=(
            P(("leaf", "couple"), None, None),
            P(("leaf", "couple"), None),
            P(("leaf", "couple"), None),
            P(("leaf", "couple"), None),
            P(("leaf", "couple")),
            P(("leaf", "couple"), None),
            P(("leaf", "couple")),
            P(("leaf", "couple"), None),
            P(("leaf", "couple")),
            P(("leaf", "couple"), None),
            P(("leaf", "couple"), None),
        ),
        out_specs=P(("leaf", "couple"), None, None),
        check_vma=False,
    )
```

```python
import functools

import jax
import jax.numpy as jnp
from jax import lax
from jax.experimental import pallas as pl
from jax.experimental.pallas import tpu as pltpu
from jax.sharding import PartitionSpec as P

LEAF = 64
RANK = 64
RHS = 128
HALO = 4
REACH = 3
BLOCK_TARGETS = 32


def from_behind(value, axis, steps):
    count = lax.axis_size(axis)
    first, last = (max(0, -steps), min(count, count - steps))
    return lax.ppermute(value, axis, [(source, source + steps) for source in range(first, last)])


def halo_pieces(block, axis, width):
    count = lax.axis_size(axis)
    forward = [(i, i + 1) for i in range(count - 1)]
    backward = [(target, source) for source, target in forward]
    low = lax.ppermute(lax.slice_in_dim(block, block.shape[0] - width, None, axis=0), axis, forward)
    high = lax.ppermute(lax.slice_in_dim(block, 0, width, axis=0), axis, backward)
    return low, high


def offset_list():
    values = []
    for step in range(REACH):
        values.append(step + 1)
        values.append(-(step + 1))
    return values


def gather_dot(idx, mats, segments, pairs, epilogue=None, out_dtype=jnp.float32):
    rows = mats.shape[0]
    width = mats.shape[1] // pairs
    targets = rows // LEAF
    tb = min(BLOCK_TARGETS, targets)
    steps = targets // tb
    n_seg = len(segments)
    seg_arrays = [s[0] for s in segments]
    seg_meta = [(s[1], s[2], s[3]) for s in segments]
    total = sum(s[2] for s in segments)

    in_specs = [pl.BlockSpec((tb * LEAF, pairs * width), lambda i, ix: (i, 0))]
    for arr in seg_arrays:
        in_specs.append(pl.BlockSpec(memory_space=pl.ANY))
    extra = []
    if epilogue is not None:
        extra, extra_specs, _, out_dtype = epilogue
        in_specs.extend(extra_specs)

    def kernel(idx_ref, mats_ref, *refs):
        seg_refs = refs[:n_seg]
        extra_refs = refs[n_seg:len(refs) - 4]
        out_ref, pool_ref, sem, acc_ref = refs[len(refs) - 4:]
        blk = pl.program_id(0)

        @pl.when(blk == 0)
        def _():
            copies = []
            for j, (ref, (lo, cnt, row)) in enumerate(zip(seg_refs, seg_meta)):
                cp = pltpu.make_async_copy(ref.at[pl.ds(row, cnt)], pool_ref.at[pl.ds(lo, cnt)], sem.at[j])
                cp.start()
                copies.append(cp)
            for cp in copies:
                cp.wait()

        for tt in range(tb):
            base = (blk * tb + tt) * pairs
            blocks = [pool_ref[idx_ref[base + k]] for k in range(pairs)]
            rhs = jnp.concatenate(blocks, axis=0)
            acc = jnp.dot(mats_ref[tt * LEAF:(tt + 1) * LEAF, :], rhs, preferred_element_type=jnp.float32)
            if epilogue is None:
                out_ref[tt] = acc.astype(out_dtype)
            else:
                acc_ref[tt] = acc
        if epilogue is not None:
            epilogue[2](tb, acc_ref, extra_refs, out_ref)

    grid_spec = pltpu.PrefetchScalarGridSpec(
        num_scalar_prefetch=1,
        grid=(steps,),
        in_specs=in_specs,
        out_specs=pl.BlockSpec((tb, LEAF, RHS), lambda i, ix: (i, 0, 0)),
        scratch_shapes=[
            pltpu.VMEM((total, width, RHS), jnp.bfloat16),
            pltpu.SemaphoreType.DMA((n_seg,)),
            pltpu.VMEM((tb if epilogue is not None else 1, LEAF, RHS), jnp.float32),
        ],
    )
    flops = 2 * rows * pairs * width * RHS
    bytes_accessed = mats.size * 2 + total * width * RHS * 2 + targets * LEAF * RHS * 4
    return pl.pallas_call(
        kernel,
        grid_spec=grid_spec,
        out_shape=jax.ShapeDtypeStruct((targets, LEAF, RHS), out_dtype),
        compiler_params=pltpu.CompilerParams(dimension_semantics=("arbitrary",)),
        cost_estimate=pl.CostEstimate(flops=flops, transcendentals=0, bytes_accessed=bytes_accessed),
    )(idx, mats, *seg_arrays, *extra)


def upward(charges, basis_t, transfer_t, send_fine, send_coarse, fine_each, coarse_each, packets):
    leaves = charges.shape[0]
    parents = leaves // 2
    slots = 2 * REACH
    each = fine_each + coarse_each
    sizes = [each + (HALO if q < 2 else 0) for q in range(slots)]
    chunks = 4 if parents % 4 == 0 else 1
    per = parents // chunks

    def kernel(sf_ref, sc_ref, x_ref, v_ref, e_ref, *rest):
        n_out = slots if packets else 2
        outs = rest[:n_out]
        fine_v, coarse_v = rest[n_out:n_out + 2]
        bufs = rest[n_out + 2:len(rest) - 1]
        sem = rest[len(rest) - 1]
        for c in range(chunks):
            for j in range(c * per, (c + 1) * per):
                col = j * 2 * RANK
                f0 = jnp.dot(v_ref[:, col:col + RANK], x_ref[2 * j], preferred_element_type=jnp.float32)
                f1 = jnp.dot(v_ref[:, col + RANK:col + 2 * RANK], x_ref[2 * j + 1], preferred_element_type=jnp.float32)
                pair = jnp.concatenate([f0.astype(jnp.bfloat16), f1.astype(jnp.bfloat16)], axis=0)
                fine_v[2 * j] = pair[:RANK]
                fine_v[2 * j + 1] = pair[RANK:]
                e = e_ref[:, col:col + 2 * RANK]
                coarse_v[j] = jnp.dot(e, pair, preferred_element_type=jnp.float32).astype(jnp.bfloat16)

        copies = []
        if not packets:
            copies = [
                pltpu.make_async_copy(fine_v, outs[0], sem.at[0]),
                pltpu.make_async_copy(coarse_v, outs[1], sem.at[1]),
            ]
            for cp in copies:
                cp.start()
        else:
            for q in range(slots):
                buf = bufs[q]
                for m in range(fine_each):
                    buf[m] = fine_v[sf_ref[q * fine_each + m]]
                for m in range(coarse_each):
                    buf[fine_each + m] = coarse_v[sc_ref[q * coarse_each + m]]
                if q == 0:
                    buf[each:each + HALO] = x_ref[leaves - HALO:leaves]
                elif q == 1:
                    buf[each:each + HALO] = x_ref[0:HALO]
                cp = pltpu.make_async_copy(buf, outs[q], sem.at[q])
                cp.start()
                copies.append(cp)
        for cp in copies:
            cp.wait()

    smem = pl.BlockSpec(memory_space=pltpu.SMEM)
    vmem = pl.BlockSpec(memory_space=pltpu.VMEM)
    hbm = pl.BlockSpec(memory_space=pl.ANY)
    block = jax.ShapeDtypeStruct
    if packets:
        out_shape = [block((n, RANK, RHS), jnp.bfloat16) for n in sizes]
        bufs = [pltpu.VMEM((n, RANK, RHS), jnp.bfloat16) for n in sizes]
    else:
        out_shape = [block((leaves, RANK, RHS), jnp.bfloat16), block((parents, RANK, RHS), jnp.bfloat16)]
        bufs = []
    return pl.pallas_call(
        kernel,
        in_specs=[smem, smem, vmem, vmem, vmem],
        out_specs=[hbm] * len(out_shape),
        out_shape=out_shape,
        scratch_shapes=[
            pltpu.VMEM((leaves, RANK, RHS), jnp.bfloat16),
            pltpu.VMEM((parents, RANK, RHS), jnp.bfloat16),
        ]
        + bufs
        + [pltpu.SemaphoreType.DMA((len(out_shape),))],
        cost_estimate=pl.CostEstimate(
            flops=2 * leaves * LEAF * RANK * RHS * 2, transcendentals=0, bytes_accessed=8 * 2 ** 20
        ),
    )(send_fine, send_coarse, charges, basis_t, transfer_t)


def coupled_product(coarse_part, fine_part, transfer, leaf_basis, near_field):
    c_idx, c_mats, c_segs, c_pairs = coarse_part
    f_idx, f_mats, f_segs, f_pairs = fine_part
    width = RANK
    parents = c_mats.shape[0] // RANK
    leaves = f_mats.shape[0] // LEAF
    tb = min(BLOCK_TARGETS, leaves)
    steps = leaves // tb
    halves = 4 if parents % 4 == 0 else 1
    c_rows = parents * RANK // halves
    c_total = sum(s[2] for s in c_segs)
    f_total = sum(s[2] for s in f_segs)
    segs = c_segs + f_segs
    n_c = len(c_segs)
    n_seg = len(segs)

    hbm = pl.BlockSpec(memory_space=pl.ANY)
    in_specs = [hbm] + [pl.BlockSpec((tb * LEAF, f_pairs * width), lambda i, a, b: (i, 0))]
    in_specs += [hbm] * n_seg
    in_specs += [
        pl.BlockSpec((tb * RANK, RANK), lambda i, a, b: (i, 0)),
        pl.BlockSpec((tb * LEAF, RANK), lambda i, a, b: (i, 0)),
        pl.BlockSpec((tb, LEAF, RHS), lambda i, a, b: (i, 0, 0)),
    ]

    def gather_sum(idx_ref, pool_ref, mats, base, pairs):
        blocks = [pool_ref[idx_ref[base + k]] for k in range(pairs)]
        return jnp.dot(mats, jnp.concatenate(blocks, axis=0), preferred_element_type=jnp.float32)

    def kernel(ci_ref, fi_ref, cm_hbm, fm_ref, *refs):
        seg_refs = refs[:n_seg]
        e_ref, v_ref, near_ref, out_ref = refs[n_seg:n_seg + 4]
        c_pool, f_pool, c_mats_v, cr_ref, acc_ref, sem = refs[n_seg + 4:]
        blk = pl.program_id(0)

        @pl.when(blk == 0)
        def _():
            seg_copies = []
            for j, (ref, (_, lo, cnt, row)) in enumerate(zip(seg_refs, segs)):
                pool = c_pool if j < n_c else f_pool
                seg_copies.append(
                    pltpu.make_async_copy(ref.at[pl.ds(row, cnt)], pool.at[pl.ds(lo, cnt)], sem.at[j])
                )
            for cp in seg_copies[:n_c]:
                cp.start()
            mat_copies = []
            for h in range(halves):
                cp = pltpu.make_async_copy(
                    cm_hbm.at[pl.ds(h * c_rows, c_rows)], c_mats_v.at[pl.ds(h * c_rows, c_rows)], sem.at[n_seg + h]
                )
                cp.start()
                mat_copies.append(cp)
            for cp in seg_copies[:n_c]:
                cp.wait()
            per_half = parents // halves
            for h in range(halves):
                mat_copies[h].wait()
                if h == 0:
                    for cp in seg_copies[n_c:]:
                        cp.start()
                for p in range(h * per_half, (h + 1) * per_half):
                    acc = gather_sum(ci_ref, c_pool, c_mats_v[p * RANK:(p + 1) * RANK, :], p * c_pairs, c_pairs)
                    cr_ref[p] = acc.astype(jnp.bfloat16)
            for cp in seg_copies[n_c:]:
                cp.wait()

        for tt in range(tb):
            base = (blk * tb + tt) * f_pairs
            acc_ref[tt] = gather_sum(fi_ref, f_pool, fm_ref[tt * LEAF:(tt + 1) * LEAF, :], base, f_pairs)
        rounded = []
        for tt in range(tb):
            e = e_ref[tt * RANK:(tt + 1) * RANK, :]
            down = jnp.dot(e, cr_ref[(blk * tb + tt) // 2], preferred_element_type=jnp.float32)
            rounded.append((acc_ref[tt] + down).astype(jnp.bfloat16))
        for tt in range(tb):
            v = v_ref[tt * LEAF:(tt + 1) * LEAF, :]
            far = jnp.dot(v, rounded[tt], preferred_element_type=jnp.float32)
            out_ref[tt] = (far + near_ref[tt]).astype(jnp.bfloat16)

    grid_spec = pltpu.PrefetchScalarGridSpec(
        num_scalar_prefetch=2,
        grid=(steps,),
        in_specs=in_specs,
        out_specs=pl.BlockSpec((tb, LEAF, RHS), lambda i, a, b: (i, 0, 0)),
        scratch_shapes=[
            pltpu.VMEM((c_total, width, RHS), jnp.bfloat16),
            pltpu.VMEM((f_total, width, RHS), jnp.bfloat16),
            pltpu.VMEM(c_mats.shape, jnp.bfloat16),
            pltpu.VMEM((parents, RANK, RHS), jnp.bfloat16),
            pltpu.VMEM((tb, LEAF, RHS), jnp.float32),
            pltpu.SemaphoreType.DMA((n_seg + halves,)),
        ],
    )
    flops = 2 * (c_mats.size + f_mats.size) * RHS
    bytes_accessed = (c_mats.size + f_mats.size) * 2 + (c_total + f_total) * width * RHS * 2
    return pl.pallas_call(
        kernel,
        grid_spec=grid_spec,
        out_shape=jax.ShapeDtypeStruct((leaves, LEAF, RHS), jnp.bfloat16),
        compiler_params=pltpu.CompilerParams(dimension_semantics=("arbitrary",)),
        cost_estimate=pl.CostEstimate(flops=flops, transcendentals=0, bytes_accessed=bytes_accessed),
    )(c_idx, f_idx, c_mats, f_mats, *[s[0] for s in segs], transfer, leaf_basis, near_field)


def on_device(
    charges,
    leaf_basis,
    transfer,
    near_blocks,
    near_source,
    couple_fine,
    source_fine,
    couple_coarse,
    source_coarse,
    send_fine,
    send_coarse,
):
    leaves = charges.shape[0]
    parents = leaves // 2
    fine_each = send_fine.shape[1] // (2 * REACH)
    coarse_each = send_coarse.shape[1] // (2 * REACH)
    axis = ("leaf", "couple")
    basis_t = leaf_basis.T
    transfer_t = transfer.T
    packets = upward(
        charges, basis_t, transfer_t, send_fine[0], send_coarse[0], fine_each, coarse_each, True
    )
    fine_coeffs, coarse_coeffs = upward(
        charges, basis_t, transfer_t, send_fine[0], send_coarse[0], fine_each, coarse_each, False
    )
    incoming = []
    for slot, offset in enumerate(offset_list()):
        incoming.append(from_behind(packets[slot], axis, offset))

    each = fine_each + coarse_each
    near_field = gather_dot(
        near_source,
        near_blocks,
        [(incoming[0], 0, HALO, each), (charges, HALO, leaves, 0), (incoming[1], HALO + leaves, HALO, each)],
        near_source.shape[0] // leaves,
    )

    coarse_segments = [(coarse_coeffs, 0, parents, 0)]
    for slot in range(2 * REACH):
        coarse_segments.append((incoming[slot], parents + slot * coarse_each, coarse_each, fine_each))
    fine_segments = [(fine_coeffs, 0, leaves, 0)]
    for slot in range(2 * REACH):
        fine_segments.append((incoming[slot], leaves + slot * fine_each, fine_each, 0))
    return coupled_product(
        (source_coarse, couple_coarse, coarse_segments, source_coarse.shape[0] // parents),
        (source_fine, couple_fine, fine_segments, source_fine.shape[0] // leaves),
        transfer,
        leaf_basis,
        near_field,
    )


def solution(mesh):
    return jax.shard_map(
        on_device,
        mesh=mesh,
        in_specs=(
            P(("leaf", "couple"), None, None),
            P(("leaf", "couple"), None),
            P(("leaf", "couple"), None),
            P(("leaf", "couple"), None),
            P(("leaf", "couple")),
            P(("leaf", "couple"), None),
            P(("leaf", "couple")),
            P(("leaf", "couple"), None),
            P(("leaf", "couple")),
            P(("leaf", "couple"), None),
            P(("leaf", "couple"), None),
        ),
        out_specs=P(("leaf", "couple"), None, None),
        check_vma=False,
    )
```

```python
import functools

import jax
import jax.numpy as jnp
from jax import lax
from jax.experimental import pallas as pl
from jax.experimental.pallas import tpu as pltpu
from jax.sharding import PartitionSpec as P

LEAF = 64
RANK = 64
RHS = 128
HALO = 4
REACH = 3
BLOCK_TARGETS = 16


def from_behind(value, axis, steps):
    count = lax.axis_size(axis)
    first, last = (max(0, -steps), min(count, count - steps))
    return lax.ppermute(value, axis, [(source, source + steps) for source in range(first, last)])


def halo_pieces(block, axis, width):
    count = lax.axis_size(axis)
    forward = [(i, i + 1) for i in range(count - 1)]
    backward = [(target, source) for source, target in forward]
    low = lax.ppermute(lax.slice_in_dim(block, block.shape[0] - width, None, axis=0), axis, forward)
    high = lax.ppermute(lax.slice_in_dim(block, 0, width, axis=0), axis, backward)
    return low, high


def offset_list():
    values = []
    for step in range(REACH):
        values.append(step + 1)
        values.append(-(step + 1))
    return values


def gather_dot(idx, mats, segments, pairs, epilogue=None, out_dtype=jnp.float32):
    rows = mats.shape[0]
    width = mats.shape[1] // pairs
    targets = rows // LEAF
    tb = min(BLOCK_TARGETS, targets)
    steps = targets // tb
    n_seg = len(segments)
    seg_arrays = [s[0] for s in segments]
    seg_meta = [(s[1], s[2], s[3]) for s in segments]
    total = sum(s[2] for s in segments)

    in_specs = [pl.BlockSpec((tb * LEAF, pairs * width), lambda i, ix: (i, 0))]
    for arr in seg_arrays:
        in_specs.append(pl.BlockSpec(memory_space=pl.ANY))
    extra = []
    if epilogue is not None:
        extra, extra_specs, _, out_dtype = epilogue
        in_specs.extend(extra_specs)

    def kernel(idx_ref, mats_ref, *refs):
        seg_refs = refs[:n_seg]
        extra_refs = refs[n_seg:len(refs) - 4]
        out_ref, pool_ref, sem, acc_ref = refs[len(refs) - 4:]
        blk = pl.program_id(0)

        @pl.when(blk == 0)
        def _():
            copies = []
            for j, (ref, (lo, cnt, row)) in enumerate(zip(seg_refs, seg_meta)):
                cp = pltpu.make_async_copy(ref.at[pl.ds(row, cnt)], pool_ref.at[pl.ds(lo, cnt)], sem.at[j])
                cp.start()
                copies.append(cp)
            for cp in copies:
                cp.wait()

        for tt in range(tb):
            base = (blk * tb + tt) * pairs
            blocks = [pool_ref[idx_ref[base + k]] for k in range(pairs)]
            rhs = jnp.concatenate(blocks, axis=0)
            acc = jnp.dot(mats_ref[tt * LEAF:(tt + 1) * LEAF, :], rhs, preferred_element_type=jnp.float32)
            if epilogue is None:
                out_ref[tt] = acc.astype(out_dtype)
            else:
                acc_ref[tt] = acc
        if epilogue is not None:
            epilogue[2](tb, acc_ref, extra_refs, out_ref)

    grid_spec = pltpu.PrefetchScalarGridSpec(
        num_scalar_prefetch=1,
        grid=(steps,),
        in_specs=in_specs,
        out_specs=pl.BlockSpec((tb, LEAF, RHS), lambda i, ix: (i, 0, 0)),
        scratch_shapes=[
            pltpu.VMEM((total, width, RHS), jnp.bfloat16),
            pltpu.SemaphoreType.DMA((n_seg,)),
            pltpu.VMEM((tb if epilogue is not None else 1, LEAF, RHS), jnp.float32),
        ],
    )
    flops = 2 * rows * pairs * width * RHS
    bytes_accessed = mats.size * 2 + total * width * RHS * 2 + targets * LEAF * RHS * 4
    return pl.pallas_call(
        kernel,
        grid_spec=grid_spec,
        out_shape=jax.ShapeDtypeStruct((targets, LEAF, RHS), out_dtype),
        compiler_params=pltpu.CompilerParams(dimension_semantics=("arbitrary",)),
        cost_estimate=pl.CostEstimate(flops=flops, transcendentals=0, bytes_accessed=bytes_accessed),
    )(idx, mats, *seg_arrays, *extra)


def upward(charges, basis_t, transfer_t, send_fine, send_coarse, fine_each, coarse_each, packets):
    leaves = charges.shape[0]
    parents = leaves // 2
    slots = 2 * REACH
    each = fine_each + coarse_each
    sizes = [each + (HALO if q < 2 else 0) for q in range(slots)]
    chunks = 4 if parents % 4 == 0 else 1
    per = parents // chunks

    def kernel(sf_ref, sc_ref, x_ref, v_ref, e_ref, *rest):
        n_out = slots if packets else 2
        outs = rest[:n_out]
        fine_v, coarse_v = rest[n_out:n_out + 2]
        bufs = rest[n_out + 2:len(rest) - 1]
        sem = rest[len(rest) - 1]
        for c in range(chunks):
            for j in range(c * per, (c + 1) * per):
                col = j * 2 * RANK
                f0 = jnp.dot(v_ref[:, col:col + RANK], x_ref[2 * j], preferred_element_type=jnp.float32)
                f1 = jnp.dot(v_ref[:, col + RANK:col + 2 * RANK], x_ref[2 * j + 1], preferred_element_type=jnp.float32)
                pair = jnp.concatenate([f0.astype(jnp.bfloat16), f1.astype(jnp.bfloat16)], axis=0)
                fine_v[2 * j] = pair[:RANK]
                fine_v[2 * j + 1] = pair[RANK:]
                e = e_ref[:, col:col + 2 * RANK]
                coarse_v[j] = jnp.dot(e, pair, preferred_element_type=jnp.float32).astype(jnp.bfloat16)

        copies = []
        if not packets:
            copies = [
                pltpu.make_async_copy(fine_v, outs[0], sem.at[0]),
                pltpu.make_async_copy(coarse_v, outs[1], sem.at[1]),
            ]
            for cp in copies:
                cp.start()
        else:
            for q in range(slots):
                buf = bufs[q]
                for m in range(fine_each):
                    buf[m] = fine_v[sf_ref[q * fine_each + m]]
                for m in range(coarse_each):
                    buf[fine_each + m] = coarse_v[sc_ref[q * coarse_each + m]]
                if q == 0:
                    buf[each:each + HALO] = x_ref[leaves - HALO:leaves]
                elif q == 1:
                    buf[each:each + HALO] = x_ref[0:HALO]
                cp = pltpu.make_async_copy(buf, outs[q], sem.at[q])
                cp.start()
                copies.append(cp)
        for cp in copies:
            cp.wait()

    smem = pl.BlockSpec(memory_space=pltpu.SMEM)
    vmem = pl.BlockSpec(memory_space=pltpu.VMEM)
    hbm = pl.BlockSpec(memory_space=pl.ANY)
    block = jax.ShapeDtypeStruct
    if packets:
        out_shape = [block((n, RANK, RHS), jnp.bfloat16) for n in sizes]
        bufs = [pltpu.VMEM((n, RANK, RHS), jnp.bfloat16) for n in sizes]
    else:
        out_shape = [block((leaves, RANK, RHS), jnp.bfloat16), block((parents, RANK, RHS), jnp.bfloat16)]
        bufs = []
    return pl.pallas_call(
        kernel,
        in_specs=[smem, smem, vmem, vmem, vmem],
        out_specs=[hbm] * len(out_shape),
        out_shape=out_shape,
        scratch_shapes=[
            pltpu.VMEM((leaves, RANK, RHS), jnp.bfloat16),
            pltpu.VMEM((parents, RANK, RHS), jnp.bfloat16),
        ]
        + bufs
        + [pltpu.SemaphoreType.DMA((len(out_shape),))],
        cost_estimate=pl.CostEstimate(
            flops=2 * leaves * LEAF * RANK * RHS * 2, transcendentals=0, bytes_accessed=8 * 2 ** 20
        ),
    )(send_fine, send_coarse, charges, basis_t, transfer_t)


def coupled_product(coarse_part, fine_part, transfer, leaf_basis, near_field):
    c_idx, c_mats, c_segs, c_pairs = coarse_part
    f_idx, f_mats, f_segs, f_pairs = fine_part
    width = RANK
    parents = c_mats.shape[0] // RANK
    leaves = f_mats.shape[0] // LEAF
    tb = min(BLOCK_TARGETS, leaves)
    steps = leaves // tb
    halves = 4 if parents % 4 == 0 else 1
    c_rows = parents * RANK // halves
    c_total = sum(s[2] for s in c_segs)
    f_total = sum(s[2] for s in f_segs)
    segs = c_segs + f_segs
    n_c = len(c_segs)
    n_seg = len(segs)

    hbm = pl.BlockSpec(memory_space=pl.ANY)
    in_specs = [hbm, hbm]
    in_specs += [hbm] * n_seg
    in_specs += [
        pl.BlockSpec((tb * RANK, RANK), lambda i, a, b: (i, 0)),
        pl.BlockSpec((tb * LEAF, RANK), lambda i, a, b: (i, 0)),
        pl.BlockSpec((tb, LEAF, RHS), lambda i, a, b: (i, 0, 0)),
    ]

    def gather_sum(idx_ref, pool_ref, mats, base, pairs):
        blocks = [pool_ref[idx_ref[base + k]] for k in range(pairs)]
        return jnp.dot(mats, jnp.concatenate(blocks, axis=0), preferred_element_type=jnp.float32)

    def kernel(ci_ref, fi_ref, cm_hbm, fm_hbm, *refs):
        seg_refs = refs[:n_seg]
        e_ref, v_ref, near_ref, out_ref = refs[n_seg:n_seg + 4]
        c_pool, f_pool, c_mats_v, cr_ref, acc_ref, sem, fm_v, fm_sem = refs[n_seg + 4:]
        blk = pl.program_id(0)
        rows = tb * LEAF

        def fine_block(step, slot):
            return pltpu.make_async_copy(fm_hbm.at[pl.ds(step * rows, rows)], fm_v.at[slot], fm_sem.at[slot])

        @pl.when(blk == 0)
        def _():
            seg_copies = []
            for j, (ref, (_, lo, cnt, row)) in enumerate(zip(seg_refs, segs)):
                pool = c_pool if j < n_c else f_pool
                seg_copies.append(
                    pltpu.make_async_copy(ref.at[pl.ds(row, cnt)], pool.at[pl.ds(lo, cnt)], sem.at[j])
                )
            for cp in seg_copies[:n_c]:
                cp.start()
            mat_copies = []
            for h in range(halves):
                cp = pltpu.make_async_copy(
                    cm_hbm.at[pl.ds(h * c_rows, c_rows)], c_mats_v.at[pl.ds(h * c_rows, c_rows)], sem.at[n_seg + h]
                )
                cp.start()
                mat_copies.append(cp)
            for cp in seg_copies[:n_c]:
                cp.wait()
            per_half = parents // halves
            for h in range(halves):
                mat_copies[h].wait()
                if h == 0:
                    for cp in seg_copies[n_c:]:
                        cp.start()
                    fine_block(0, 0).start()
                for p in range(h * per_half, (h + 1) * per_half):
                    acc = gather_sum(ci_ref, c_pool, c_mats_v[p * RANK:(p + 1) * RANK, :], p * c_pairs, c_pairs)
                    cr_ref[p] = acc.astype(jnp.bfloat16)
            for cp in seg_copies[n_c:]:
                cp.wait()

        slot = blk % 2
        fine_block(blk, slot).wait()

        @pl.when(blk + 1 < steps)
        def _():
            fine_block(blk + 1, 1 - slot).start()

        fm_ref = fm_v.at[slot]
        for tt in range(tb):
            base = (blk * tb + tt) * f_pairs
            acc_ref[tt] = gather_sum(fi_ref, f_pool, fm_ref[tt * LEAF:(tt + 1) * LEAF, :], base, f_pairs)
        rounded = []
        for tt in range(tb):
            e = e_ref[tt * RANK:(tt + 1) * RANK, :]
            down = jnp.dot(e, cr_ref[(blk * tb + tt) // 2], preferred_element_type=jnp.float32)
            rounded.append((acc_ref[tt] + down).astype(jnp.bfloat16))
        for tt in range(tb):
            v = v_ref[tt * LEAF:(tt + 1) * LEAF, :]
            far = jnp.dot(v, rounded[tt], preferred_element_type=jnp.float32)
            out_ref[tt] = (far + near_ref[tt]).astype(jnp.bfloat16)

    grid_spec = pltpu.PrefetchScalarGridSpec(
        num_scalar_prefetch=2,
        grid=(steps,),
        in_specs=in_specs,
        out_specs=pl.BlockSpec((tb, LEAF, RHS), lambda i, a, b: (i, 0, 0)),
        scratch_shapes=[
            pltpu.VMEM((c_total, width, RHS), jnp.bfloat16),
            pltpu.VMEM((f_total, width, RHS), jnp.bfloat16),
            pltpu.VMEM(c_mats.shape, jnp.bfloat16),
            pltpu.VMEM((parents, RANK, RHS), jnp.bfloat16),
            pltpu.VMEM((tb, LEAF, RHS), jnp.float32),
            pltpu.SemaphoreType.DMA((n_seg + halves,)),
            pltpu.VMEM((2, tb * LEAF, f_pairs * width), jnp.bfloat16),
            pltpu.SemaphoreType.DMA((2,)),
        ],
    )
    flops = 2 * (c_mats.size + f_mats.size) * RHS
    bytes_accessed = (c_mats.size + f_mats.size) * 2 + (c_total + f_total) * width * RHS * 2
    return pl.pallas_call(
        kernel,
        grid_spec=grid_spec,
        out_shape=jax.ShapeDtypeStruct((leaves, LEAF, RHS), jnp.bfloat16),
        compiler_params=pltpu.CompilerParams(dimension_semantics=("arbitrary",)),
        cost_estimate=pl.CostEstimate(flops=flops, transcendentals=0, bytes_accessed=bytes_accessed),
    )(c_idx, f_idx, c_mats, f_mats, *[s[0] for s in segs], transfer, leaf_basis, near_field)


def on_device(
    charges,
    leaf_basis,
    transfer,
    near_blocks,
    near_source,
    couple_fine,
    source_fine,
    couple_coarse,
    source_coarse,
    send_fine,
    send_coarse,
):
    leaves = charges.shape[0]
    parents = leaves // 2
    fine_each = send_fine.shape[1] // (2 * REACH)
    coarse_each = send_coarse.shape[1] // (2 * REACH)
    axis = ("leaf", "couple")
    basis_t = leaf_basis.T
    transfer_t = transfer.T
    packets = upward(
        charges, basis_t, transfer_t, send_fine[0], send_coarse[0], fine_each, coarse_each, True
    )
    fine_coeffs, coarse_coeffs = upward(
        charges, basis_t, transfer_t, send_fine[0], send_coarse[0], fine_each, coarse_each, False
    )
    incoming = []
    for slot, offset in enumerate(offset_list()):
        incoming.append(from_behind(packets[slot], axis, offset))

    each = fine_each + coarse_each
    near_field = gather_dot(
        near_source,
        near_blocks,
        [(incoming[0], 0, HALO, each), (charges, HALO, leaves, 0), (incoming[1], HALO + leaves, HALO, each)],
        near_source.shape[0] // leaves,
    )

    coarse_segments = [(coarse_coeffs, 0, parents, 0)]
    for slot in range(2 * REACH):
        coarse_segments.append((incoming[slot], parents + slot * coarse_each, coarse_each, fine_each))
    fine_segments = [(fine_coeffs, 0, leaves, 0)]
    for slot in range(2 * REACH):
        fine_segments.append((incoming[slot], leaves + slot * fine_each, fine_each, 0))
    return coupled_product(
        (source_coarse, couple_coarse, coarse_segments, source_coarse.shape[0] // parents),
        (source_fine, couple_fine, fine_segments, source_fine.shape[0] // leaves),
        transfer,
        leaf_basis,
        near_field,
    )


def solution(mesh):
    return jax.shard_map(
        on_device,
        mesh=mesh,
        in_specs=(
            P(("leaf", "couple"), None, None),
            P(("leaf", "couple"), None),
            P(("leaf", "couple"), None),
            P(("leaf", "couple"), None),
            P(("leaf", "couple")),
            P(("leaf", "couple"), None),
            P(("leaf", "couple")),
            P(("leaf", "couple"), None),
            P(("leaf", "couple")),
            P(("leaf", "couple"), None),
            P(("leaf", "couple"), None),
        ),
        out_specs=P(("leaf", "couple"), None, None),
        check_vma=False,
    )
```

```python
import functools

import jax
import jax.numpy as jnp
from jax import lax
from jax.experimental import pallas as pl
from jax.experimental.pallas import tpu as pltpu
from jax.sharding import PartitionSpec as P

LEAF = 64
RANK = 64
RHS = 128
HALO = 4
REACH = 3
BLOCK_TARGETS = 16


def from_behind(value, axis, steps):
    count = lax.axis_size(axis)
    first, last = (max(0, -steps), min(count, count - steps))
    return lax.ppermute(value, axis, [(source, source + steps) for source in range(first, last)])


def halo_pieces(block, axis, width):
    count = lax.axis_size(axis)
    forward = [(i, i + 1) for i in range(count - 1)]
    backward = [(target, source) for source, target in forward]
    low = lax.ppermute(lax.slice_in_dim(block, block.shape[0] - width, None, axis=0), axis, forward)
    high = lax.ppermute(lax.slice_in_dim(block, 0, width, axis=0), axis, backward)
    return low, high


def offset_list():
    values = []
    for step in range(REACH):
        values.append(step + 1)
        values.append(-(step + 1))
    return values


def gather_dot(idx, mats, segments, pairs, epilogue=None, out_dtype=jnp.float32):
    rows = mats.shape[0]
    width = mats.shape[1] // pairs
    targets = rows // LEAF
    tb = min(BLOCK_TARGETS, targets)
    steps = targets // tb
    n_seg = len(segments)
    seg_arrays = [s[0] for s in segments]
    seg_meta = [(s[1], s[2], s[3]) for s in segments]
    total = sum(s[2] for s in segments)

    in_specs = [pl.BlockSpec((tb * LEAF, pairs * width), lambda i, ix: (i, 0))]
    for arr in seg_arrays:
        in_specs.append(pl.BlockSpec(memory_space=pl.ANY))
    extra = []
    if epilogue is not None:
        extra, extra_specs, _, out_dtype = epilogue
        in_specs.extend(extra_specs)

    def kernel(idx_ref, mats_ref, *refs):
        seg_refs = refs[:n_seg]
        extra_refs = refs[n_seg:len(refs) - 4]
        out_ref, pool_ref, sem, acc_ref = refs[len(refs) - 4:]
        blk = pl.program_id(0)

        @pl.when(blk == 0)
        def _():
            copies = []
            for j, (ref, (lo, cnt, row)) in enumerate(zip(seg_refs, seg_meta)):
                cp = pltpu.make_async_copy(ref.at[pl.ds(row, cnt)], pool_ref.at[pl.ds(lo, cnt)], sem.at[j])
                cp.start()
                copies.append(cp)
            for cp in copies:
                cp.wait()

        for tt in range(tb):
            base = (blk * tb + tt) * pairs
            blocks = [pool_ref[idx_ref[base + k]] for k in range(pairs)]
            rhs = jnp.concatenate(blocks, axis=0)
            acc = jnp.dot(mats_ref[tt * LEAF:(tt + 1) * LEAF, :], rhs, preferred_element_type=jnp.float32)
            if epilogue is None:
                out_ref[tt] = acc.astype(out_dtype)
            else:
                acc_ref[tt] = acc
        if epilogue is not None:
            epilogue[2](tb, acc_ref, extra_refs, out_ref)

    grid_spec = pltpu.PrefetchScalarGridSpec(
        num_scalar_prefetch=1,
        grid=(steps,),
        in_specs=in_specs,
        out_specs=pl.BlockSpec((tb, LEAF, RHS), lambda i, ix: (i, 0, 0)),
        scratch_shapes=[
            pltpu.VMEM((total, width, RHS), jnp.bfloat16),
            pltpu.SemaphoreType.DMA((n_seg,)),
            pltpu.VMEM((tb if epilogue is not None else 1, LEAF, RHS), jnp.float32),
        ],
    )
    flops = 2 * rows * pairs * width * RHS
    bytes_accessed = mats.size * 2 + total * width * RHS * 2 + targets * LEAF * RHS * 4
    return pl.pallas_call(
        kernel,
        grid_spec=grid_spec,
        out_shape=jax.ShapeDtypeStruct((targets, LEAF, RHS), out_dtype),
        compiler_params=pltpu.CompilerParams(dimension_semantics=("arbitrary",)),
        cost_estimate=pl.CostEstimate(flops=flops, transcendentals=0, bytes_accessed=bytes_accessed),
    )(idx, mats, *seg_arrays, *extra)


def upward(charges, basis_t, transfer_t, send_fine, send_coarse, fine_each, coarse_each, packets):
    leaves = charges.shape[0]
    parents = leaves // 2
    slots = 2 * REACH
    each = fine_each + coarse_each
    sizes = [each + (HALO if q < 2 else 0) for q in range(slots)]
    chunks = 4 if parents % 4 == 0 else 1
    per = parents // chunks

    def kernel(sf_ref, sc_ref, x_ref, v_ref, e_ref, *rest):
        n_out = slots if packets else 2
        outs = rest[:n_out]
        fine_v, coarse_v = rest[n_out:n_out + 2]
        bufs = rest[n_out + 2:len(rest) - 1]
        sem = rest[len(rest) - 1]
        for c in range(chunks):
            for j in range(c * per, (c + 1) * per):
                col = j * 2 * RANK
                f0 = jnp.dot(v_ref[:, col:col + RANK], x_ref[2 * j], preferred_element_type=jnp.float32)
                f1 = jnp.dot(v_ref[:, col + RANK:col + 2 * RANK], x_ref[2 * j + 1], preferred_element_type=jnp.float32)
                pair = jnp.concatenate([f0.astype(jnp.bfloat16), f1.astype(jnp.bfloat16)], axis=0)
                fine_v[2 * j] = pair[:RANK]
                fine_v[2 * j + 1] = pair[RANK:]
                e = e_ref[:, col:col + 2 * RANK]
                coarse_v[j] = jnp.dot(e, pair, preferred_element_type=jnp.float32).astype(jnp.bfloat16)

        copies = []
        if not packets:
            copies = [
                pltpu.make_async_copy(fine_v, outs[0], sem.at[0]),
                pltpu.make_async_copy(coarse_v, outs[1], sem.at[1]),
            ]
            for cp in copies:
                cp.start()
        else:
            for q in range(slots):
                buf = bufs[q]
                for m in range(fine_each):
                    buf[m] = fine_v[sf_ref[q * fine_each + m]]
                for m in range(coarse_each):
                    buf[fine_each + m] = coarse_v[sc_ref[q * coarse_each + m]]
                if q == 0:
                    buf[each:each + HALO] = x_ref[leaves - HALO:leaves]
                elif q == 1:
                    buf[each:each + HALO] = x_ref[0:HALO]
                cp = pltpu.make_async_copy(buf, outs[q], sem.at[q])
                cp.start()
                copies.append(cp)
        for cp in copies:
            cp.wait()

    smem = pl.BlockSpec(memory_space=pltpu.SMEM)
    vmem = pl.BlockSpec(memory_space=pltpu.VMEM)
    hbm = pl.BlockSpec(memory_space=pl.ANY)
    block = jax.ShapeDtypeStruct
    if packets:
        out_shape = [block((n, RANK, RHS), jnp.bfloat16) for n in sizes]
        bufs = [pltpu.VMEM((n, RANK, RHS), jnp.bfloat16) for n in sizes]
    else:
        out_shape = [block((leaves, RANK, RHS), jnp.bfloat16), block((parents, RANK, RHS), jnp.bfloat16)]
        bufs = []
    return pl.pallas_call(
        kernel,
        in_specs=[smem, smem, vmem, vmem, vmem],
        out_specs=[hbm] * len(out_shape),
        out_shape=out_shape,
        scratch_shapes=[
            pltpu.VMEM((leaves, RANK, RHS), jnp.bfloat16),
            pltpu.VMEM((parents, RANK, RHS), jnp.bfloat16),
        ]
        + bufs
        + [pltpu.SemaphoreType.DMA((len(out_shape),))],
        cost_estimate=pl.CostEstimate(
            flops=2 * leaves * LEAF * RANK * RHS * 2, transcendentals=0, bytes_accessed=8 * 2 ** 20
        ),
    )(send_fine, send_coarse, charges, basis_t, transfer_t)


def coupled_product(coarse_part, fine_part, transfer, leaf_basis, near_field):
    c_idx, c_mats, c_segs, c_pairs = coarse_part
    f_idx, f_mats, f_segs, f_pairs = fine_part
    width = RANK
    parents = c_mats.shape[0] // RANK
    leaves = f_mats.shape[0] // LEAF
    tb = min(BLOCK_TARGETS, leaves)
    steps = leaves // tb
    halves = 4 if parents % 4 == 0 else 1
    c_rows = parents * RANK // halves
    c_total = sum(s[2] for s in c_segs)
    f_total = sum(s[2] for s in f_segs)
    segs = c_segs + f_segs
    n_c = len(c_segs)
    n_seg = len(segs)

    hbm = pl.BlockSpec(memory_space=pl.ANY)
    in_specs = [hbm] + [pl.BlockSpec((tb * LEAF, f_pairs * width), lambda i, a, b: (i, 0))]
    in_specs += [hbm] * n_seg
    in_specs += [
        pl.BlockSpec((tb * RANK, RANK), lambda i, a, b: (i, 0)),
        pl.BlockSpec((tb * LEAF, RANK), lambda i, a, b: (i, 0)),
        pl.BlockSpec((tb, LEAF, RHS), lambda i, a, b: (i, 0, 0)),
    ]

    def gather_sum(idx_ref, pool_ref, mats, base, pairs):
        blocks = [pool_ref[idx_ref[base + k]] for k in range(pairs)]
        return jnp.dot(mats, jnp.concatenate(blocks, axis=0), preferred_element_type=jnp.float32)

    def kernel(ci_ref, fi_ref, cm_hbm, fm_ref, *refs):
        seg_refs = refs[:n_seg]
        e_ref, v_ref, near_ref, out_ref = refs[n_seg:n_seg + 4]
        c_pool, f_pool, c_mats_v, cr_ref, acc_ref, sem = refs[n_seg + 4:]
        blk = pl.program_id(0)

        @pl.when(blk == 0)
        def _():
            seg_copies = []
            for j, (ref, (_, lo, cnt, row)) in enumerate(zip(seg_refs, segs)):
                pool = c_pool if j < n_c else f_pool
                seg_copies.append(
                    pltpu.make_async_copy(ref.at[pl.ds(row, cnt)], pool.at[pl.ds(lo, cnt)], sem.at[j])
                )
            for cp in seg_copies[:n_c]:
                cp.start()
            mat_copies = []
            for h in range(halves):
                cp = pltpu.make_async_copy(
                    cm_hbm.at[pl.ds(h * c_rows, c_rows)], c_mats_v.at[pl.ds(h * c_rows, c_rows)], sem.at[n_seg + h]
                )
                cp.start()
                mat_copies.append(cp)
            for cp in seg_copies[:n_c]:
                cp.wait()
            per_half = parents // halves
            for h in range(halves):
                mat_copies[h].wait()
                if h == 0:
                    for cp in seg_copies[n_c:]:
                        cp.start()
                for p in range(h * per_half, (h + 1) * per_half):
                    acc = gather_sum(ci_ref, c_pool, c_mats_v[p * RANK:(p + 1) * RANK, :], p * c_pairs, c_pairs)
                    cr_ref[p] = acc.astype(jnp.bfloat16)
            for cp in seg_copies[n_c:]:
                cp.wait()

        for tt in range(tb):
            base = (blk * tb + tt) * f_pairs
            acc_ref[tt] = gather_sum(fi_ref, f_pool, fm_ref[tt * LEAF:(tt + 1) * LEAF, :], base, f_pairs)
        rounded = []
        for j in range(tb // 2):
            e = e_ref[2 * j * RANK:(2 * j + 2) * RANK, :]
            down = jnp.dot(e, cr_ref[blk * (tb // 2) + j], preferred_element_type=jnp.float32)
            for h in range(2):
                rounded.append((acc_ref[2 * j + h] + down[h * RANK:(h + 1) * RANK]).astype(jnp.bfloat16))
        for tt in range(tb):
            v = v_ref[tt * LEAF:(tt + 1) * LEAF, :]
            far = jnp.dot(v, rounded[tt], preferred_element_type=jnp.float32)
            out_ref[tt] = (far + near_ref[tt]).astype(jnp.bfloat16)

    grid_spec = pltpu.PrefetchScalarGridSpec(
        num_scalar_prefetch=2,
        grid=(steps,),
        in_specs=in_specs,
        out_specs=pl.BlockSpec((tb, LEAF, RHS), lambda i, a, b: (i, 0, 0)),
        scratch_shapes=[
            pltpu.VMEM((c_total, width, RHS), jnp.bfloat16),
            pltpu.VMEM((f_total, width, RHS), jnp.bfloat16),
            pltpu.VMEM(c_mats.shape, jnp.bfloat16),
            pltpu.VMEM((parents, RANK, RHS), jnp.bfloat16),
            pltpu.VMEM((tb, LEAF, RHS), jnp.float32),
            pltpu.SemaphoreType.DMA((n_seg + halves,)),
        ],
    )
    flops = 2 * (c_mats.size + f_mats.size) * RHS
    bytes_accessed = (c_mats.size + f_mats.size) * 2 + (c_total + f_total) * width * RHS * 2
    return pl.pallas_call(
        kernel,
        grid_spec=grid_spec,
        out_shape=jax.ShapeDtypeStruct((leaves, LEAF, RHS), jnp.bfloat16),
        compiler_params=pltpu.CompilerParams(dimension_semantics=("arbitrary",)),
        cost_estimate=pl.CostEstimate(flops=flops, transcendentals=0, bytes_accessed=bytes_accessed),
    )(c_idx, f_idx, c_mats, f_mats, *[s[0] for s in segs], transfer, leaf_basis, near_field)


def on_device(
    charges,
    leaf_basis,
    transfer,
    near_blocks,
    near_source,
    couple_fine,
    source_fine,
    couple_coarse,
    source_coarse,
    send_fine,
    send_coarse,
):
    leaves = charges.shape[0]
    parents = leaves // 2
    fine_each = send_fine.shape[1] // (2 * REACH)
    coarse_each = send_coarse.shape[1] // (2 * REACH)
    axis = ("leaf", "couple")
    basis_t = leaf_basis.T
    transfer_t = transfer.T
    packets = upward(
        charges, basis_t, transfer_t, send_fine[0], send_coarse[0], fine_each, coarse_each, True
    )
    fine_coeffs, coarse_coeffs = upward(
        charges, basis_t, transfer_t, send_fine[0], send_coarse[0], fine_each, coarse_each, False
    )
    incoming = []
    for slot, offset in enumerate(offset_list()):
        incoming.append(from_behind(packets[slot], axis, offset))

    each = fine_each + coarse_each
    near_field = gather_dot(
        near_source,
        near_blocks,
        [(incoming[0], 0, HALO, each), (charges, HALO, leaves, 0), (incoming[1], HALO + leaves, HALO, each)],
        near_source.shape[0] // leaves,
    )

    coarse_segments = [(coarse_coeffs, 0, parents, 0)]
    for slot in range(2 * REACH):
        coarse_segments.append((incoming[slot], parents + slot * coarse_each, coarse_each, fine_each))
    fine_segments = [(fine_coeffs, 0, leaves, 0)]
    for slot in range(2 * REACH):
        fine_segments.append((incoming[slot], leaves + slot * fine_each, fine_each, 0))
    return coupled_product(
        (source_coarse, couple_coarse, coarse_segments, source_coarse.shape[0] // parents),
        (source_fine, couple_fine, fine_segments, source_fine.shape[0] // leaves),
        transfer,
        leaf_basis,
        near_field,
    )


def solution(mesh):
    return jax.shard_map(
        on_device,
        mesh=mesh,
        in_specs=(
            P(("leaf", "couple"), None, None),
            P(("leaf", "couple"), None),
            P(("leaf", "couple"), None),
            P(("leaf", "couple"), None),
            P(("leaf", "couple")),
            P(("leaf", "couple"), None),
            P(("leaf", "couple")),
            P(("leaf", "couple"), None),
            P(("leaf", "couple")),
            P(("leaf", "couple"), None),
            P(("leaf", "couple"), None),
        ),
        out_specs=P(("leaf", "couple"), None, None),
        check_vma=False,
    )
```

```python
import functools

import jax
import jax.numpy as jnp
from jax import lax
from jax.experimental import pallas as pl
from jax.experimental.pallas import tpu as pltpu
from jax.sharding import PartitionSpec as P

LEAF = 64
RANK = 64
RHS = 128
HALO = 4
REACH = 3
BLOCK_TARGETS = 16


def from_behind(value, axis, steps):
    count = lax.axis_size(axis)
    first, last = (max(0, -steps), min(count, count - steps))
    return lax.ppermute(value, axis, [(source, source + steps) for source in range(first, last)])


def halo_pieces(block, axis, width):
    count = lax.axis_size(axis)
    forward = [(i, i + 1) for i in range(count - 1)]
    backward = [(target, source) for source, target in forward]
    low = lax.ppermute(lax.slice_in_dim(block, block.shape[0] - width, None, axis=0), axis, forward)
    high = lax.ppermute(lax.slice_in_dim(block, 0, width, axis=0), axis, backward)
    return low, high


def offset_list():
    values = []
    for step in range(REACH):
        values.append(step + 1)
        values.append(-(step + 1))
    return values


def gather_dot(idx, mats, segments, pairs, epilogue=None, out_dtype=jnp.float32):
    rows = mats.shape[0]
    width = mats.shape[1] // pairs
    targets = rows // LEAF
    tb = min(BLOCK_TARGETS, targets)
    steps = targets // tb
    n_seg = len(segments)
    seg_arrays = [s[0] for s in segments]
    seg_meta = [(s[1], s[2], s[3]) for s in segments]
    total = sum(s[2] for s in segments)

    in_specs = [pl.BlockSpec((tb * LEAF, pairs * width), lambda i, ix: (i, 0))]
    for arr in seg_arrays:
        in_specs.append(pl.BlockSpec(memory_space=pl.ANY))
    extra = []
    if epilogue is not None:
        extra, extra_specs, _, out_dtype = epilogue
        in_specs.extend(extra_specs)

    def kernel(idx_ref, mats_ref, *refs):
        seg_refs = refs[:n_seg]
        extra_refs = refs[n_seg:len(refs) - 4]
        out_ref, pool_ref, sem, acc_ref = refs[len(refs) - 4:]
        blk = pl.program_id(0)

        @pl.when(blk == 0)
        def _():
            copies = []
            for j, (ref, (lo, cnt, row)) in enumerate(zip(seg_refs, seg_meta)):
                cp = pltpu.make_async_copy(ref.at[pl.ds(row, cnt)], pool_ref.at[pl.ds(lo, cnt)], sem.at[j])
                cp.start()
                copies.append(cp)
            for cp in copies:
                cp.wait()

        for tt in range(tb):
            base = (blk * tb + tt) * pairs
            blocks = [pool_ref[idx_ref[base + k]] for k in range(pairs)]
            rhs = jnp.concatenate(blocks, axis=0)
            acc = jnp.dot(mats_ref[tt * LEAF:(tt + 1) * LEAF, :], rhs, preferred_element_type=jnp.float32)
            if epilogue is None:
                out_ref[tt] = acc.astype(out_dtype)
            else:
                acc_ref[tt] = acc
        if epilogue is not None:
            epilogue[2](tb, acc_ref, extra_refs, out_ref)

    grid_spec = pltpu.PrefetchScalarGridSpec(
        num_scalar_prefetch=1,
        grid=(steps,),
        in_specs=in_specs,
        out_specs=pl.BlockSpec((tb, LEAF, RHS), lambda i, ix: (i, 0, 0)),
        scratch_shapes=[
            pltpu.VMEM((total, width, RHS), jnp.bfloat16),
            pltpu.SemaphoreType.DMA((n_seg,)),
            pltpu.VMEM((tb if epilogue is not None else 1, LEAF, RHS), jnp.float32),
        ],
    )
    flops = 2 * rows * pairs * width * RHS
    bytes_accessed = mats.size * 2 + total * width * RHS * 2 + targets * LEAF * RHS * 4
    return pl.pallas_call(
        kernel,
        grid_spec=grid_spec,
        out_shape=jax.ShapeDtypeStruct((targets, LEAF, RHS), out_dtype),
        compiler_params=pltpu.CompilerParams(dimension_semantics=("arbitrary",)),
        cost_estimate=pl.CostEstimate(flops=flops, transcendentals=0, bytes_accessed=bytes_accessed),
    )(idx, mats, *seg_arrays, *extra)


def upward(charges, basis_t, transfer_t, send_fine, send_coarse, fine_each, coarse_each, packets):
    leaves = charges.shape[0]
    parents = leaves // 2
    slots = 2 * REACH
    each = fine_each + coarse_each
    sizes = [each + (HALO if q < 2 else 0) for q in range(slots)]
    chunks = 4 if parents % 4 == 0 else 1
    per = parents // chunks

    def kernel(sf_ref, sc_ref, x_hbm, v_ref, e_hbm, *rest):
        n_out = slots if packets else 2
        outs = rest[:n_out]
        fine_v, coarse_v, x_ref, e_ref = rest[n_out:n_out + 4]
        bufs = rest[n_out + 4:len(rest) - 2]
        sem, in_sem = rest[len(rest) - 2:]
        loads = []
        for c in range(chunks):
            rows = pl.ds(2 * c * per, 2 * per)
            cp = pltpu.make_async_copy(x_hbm.at[rows], x_ref.at[rows], in_sem.at[c])
            cp.start()
            loads.append(cp)
        e_load = pltpu.make_async_copy(e_hbm, e_ref, in_sem.at[chunks])
        e_load.start()
        pairs_v = []
        for c in range(chunks):
            loads[c].wait()
            for j in range(c * per, (c + 1) * per):
                col = j * 2 * RANK
                f0 = jnp.dot(v_ref[:, col:col + RANK], x_ref[2 * j], preferred_element_type=jnp.float32)
                f1 = jnp.dot(v_ref[:, col + RANK:col + 2 * RANK], x_ref[2 * j + 1], preferred_element_type=jnp.float32)
                pair = jnp.concatenate([f0.astype(jnp.bfloat16), f1.astype(jnp.bfloat16)], axis=0)
                fine_v[2 * j] = pair[:RANK]
                fine_v[2 * j + 1] = pair[RANK:]
        e_load.wait()
        for j in range(parents):
            col = j * 2 * RANK
            pair = jnp.concatenate([fine_v[2 * j], fine_v[2 * j + 1]], axis=0)
            e = e_ref[:, col:col + 2 * RANK]
            coarse_v[j] = jnp.dot(e, pair, preferred_element_type=jnp.float32).astype(jnp.bfloat16)

        copies = []
        if not packets:
            copies = [
                pltpu.make_async_copy(fine_v, outs[0], sem.at[0]),
                pltpu.make_async_copy(coarse_v, outs[1], sem.at[1]),
            ]
            for cp in copies:
                cp.start()
        else:
            for q in range(slots):
                buf = bufs[q]
                for m in range(fine_each):
                    buf[m] = fine_v[sf_ref[q * fine_each + m]]
                for m in range(coarse_each):
                    buf[fine_each + m] = coarse_v[sc_ref[q * coarse_each + m]]
                if q == 0:
                    buf[each:each + HALO] = x_ref[leaves - HALO:leaves]
                elif q == 1:
                    buf[each:each + HALO] = x_ref[0:HALO]
                cp = pltpu.make_async_copy(buf, outs[q], sem.at[q])
                cp.start()
                copies.append(cp)
        for cp in copies:
            cp.wait()

    smem = pl.BlockSpec(memory_space=pltpu.SMEM)
    vmem = pl.BlockSpec(memory_space=pltpu.VMEM)
    hbm = pl.BlockSpec(memory_space=pl.ANY)
    block = jax.ShapeDtypeStruct
    if packets:
        out_shape = [block((n, RANK, RHS), jnp.bfloat16) for n in sizes]
        bufs = [pltpu.VMEM((n, RANK, RHS), jnp.bfloat16) for n in sizes]
    else:
        out_shape = [block((leaves, RANK, RHS), jnp.bfloat16), block((parents, RANK, RHS), jnp.bfloat16)]
        bufs = []
    return pl.pallas_call(
        kernel,
        in_specs=[smem, smem, hbm, vmem, hbm],
        out_specs=[hbm] * len(out_shape),
        out_shape=out_shape,
        scratch_shapes=[
            pltpu.VMEM((leaves, RANK, RHS), jnp.bfloat16),
            pltpu.VMEM((parents, RANK, RHS), jnp.bfloat16),
            pltpu.VMEM(charges.shape, jnp.bfloat16),
            pltpu.VMEM(transfer_t.shape, jnp.bfloat16),
        ]
        + bufs
        + [pltpu.SemaphoreType.DMA((len(out_shape),)), pltpu.SemaphoreType.DMA((chunks + 1,))],
        cost_estimate=pl.CostEstimate(
            flops=2 * leaves * LEAF * RANK * RHS * 2, transcendentals=0, bytes_accessed=8 * 2 ** 20
        ),
    )(send_fine, send_coarse, charges, basis_t, transfer_t)


def coupled_product(coarse_part, fine_part, transfer, leaf_basis, near_field):
    c_idx, c_mats, c_segs, c_pairs = coarse_part
    f_idx, f_mats, f_segs, f_pairs = fine_part
    width = RANK
    parents = c_mats.shape[0] // RANK
    leaves = f_mats.shape[0] // LEAF
    tb = min(BLOCK_TARGETS, leaves)
    steps = leaves // tb
    halves = 4 if parents % 4 == 0 else 1
    c_rows = parents * RANK // halves
    c_total = sum(s[2] for s in c_segs)
    f_total = sum(s[2] for s in f_segs)
    segs = c_segs + f_segs
    n_c = len(c_segs)
    n_seg = len(segs)

    hbm = pl.BlockSpec(memory_space=pl.ANY)
    in_specs = [hbm] + [pl.BlockSpec((tb * LEAF, f_pairs * width), lambda i, a, b: (i, 0))]
    in_specs += [hbm] * n_seg
    in_specs += [
        pl.BlockSpec((tb * RANK, RANK), lambda i, a, b: (i, 0)),
        pl.BlockSpec((tb * LEAF, RANK), lambda i, a, b: (i, 0)),
        pl.BlockSpec((tb, LEAF, RHS), lambda i, a, b: (i, 0, 0)),
    ]

    def gather_sum(idx_ref, pool_ref, mats, base, pairs):
        blocks = [pool_ref[idx_ref[base + k]] for k in range(pairs)]
        return jnp.dot(mats, jnp.concatenate(blocks, axis=0), preferred_element_type=jnp.float32)

    def kernel(ci_ref, fi_ref, cm_hbm, fm_ref, *refs):
        seg_refs = refs[:n_seg]
        e_ref, v_ref, near_ref, out_ref = refs[n_seg:n_seg + 4]
        c_pool, f_pool, c_mats_v, cr_ref, acc_ref, sem = refs[n_seg + 4:]
        blk = pl.program_id(0)

        @pl.when(blk == 0)
        def _():
            seg_copies = []
            for j, (ref, (_, lo, cnt, row)) in enumerate(zip(seg_refs, segs)):
                pool = c_pool if j < n_c else f_pool
                seg_copies.append(
                    pltpu.make_async_copy(ref.at[pl.ds(row, cnt)], pool.at[pl.ds(lo, cnt)], sem.at[j])
                )
            for cp in seg_copies[:n_c]:
                cp.start()
            mat_copies = []
            for h in range(halves):
                cp = pltpu.make_async_copy(
                    cm_hbm.at[pl.ds(h * c_rows, c_rows)], c_mats_v.at[pl.ds(h * c_rows, c_rows)], sem.at[n_seg + h]
                )
                cp.start()
                mat_copies.append(cp)
            for cp in seg_copies[:n_c]:
                cp.wait()
            per_half = parents // halves
            for h in range(halves):
                mat_copies[h].wait()
                if h == 0:
                    for cp in seg_copies[n_c:]:
                        cp.start()
                for p in range(h * per_half, (h + 1) * per_half):
                    acc = gather_sum(ci_ref, c_pool, c_mats_v[p * RANK:(p + 1) * RANK, :], p * c_pairs, c_pairs)
                    cr_ref[p] = acc.astype(jnp.bfloat16)
            for cp in seg_copies[n_c:]:
                cp.wait()

        for tt in range(tb):
            base = (blk * tb + tt) * f_pairs
            acc_ref[tt] = gather_sum(fi_ref, f_pool, fm_ref[tt * LEAF:(tt + 1) * LEAF, :], base, f_pairs)
        rounded = []
        for j in range(tb // 2):
            e = e_ref[2 * j * RANK:(2 * j + 2) * RANK, :]
            down = jnp.dot(e, cr_ref[blk * (tb // 2) + j], preferred_element_type=jnp.float32)
            for h in range(2):
                rounded.append((acc_ref[2 * j + h] + down[h * RANK:(h + 1) * RANK]).astype(jnp.bfloat16))
        for tt in range(tb):
            v = v_ref[tt * LEAF:(tt + 1) * LEAF, :]
            far = jnp.dot(v, rounded[tt], preferred_element_type=jnp.float32)
            out_ref[tt] = (far + near_ref[tt]).astype(jnp.bfloat16)

    grid_spec = pltpu.PrefetchScalarGridSpec(
        num_scalar_prefetch=2,
        grid=(steps,),
        in_specs=in_specs,
        out_specs=pl.BlockSpec((tb, LEAF, RHS), lambda i, a, b: (i, 0, 0)),
        scratch_shapes=[
            pltpu.VMEM((c_total, width, RHS), jnp.bfloat16),
            pltpu.VMEM((f_total, width, RHS), jnp.bfloat16),
            pltpu.VMEM(c_mats.shape, jnp.bfloat16),
            pltpu.VMEM((parents, RANK, RHS), jnp.bfloat16),
            pltpu.VMEM((tb, LEAF, RHS), jnp.float32),
            pltpu.SemaphoreType.DMA((n_seg + halves,)),
        ],
    )
    flops = 2 * (c_mats.size + f_mats.size) * RHS
    bytes_accessed = (c_mats.size + f_mats.size) * 2 + (c_total + f_total) * width * RHS * 2
    return pl.pallas_call(
        kernel,
        grid_spec=grid_spec,
        out_shape=jax.ShapeDtypeStruct((leaves, LEAF, RHS), jnp.bfloat16),
        compiler_params=pltpu.CompilerParams(dimension_semantics=("arbitrary",)),
        cost_estimate=pl.CostEstimate(flops=flops, transcendentals=0, bytes_accessed=bytes_accessed),
    )(c_idx, f_idx, c_mats, f_mats, *[s[0] for s in segs], transfer, leaf_basis, near_field)


def on_device(
    charges,
    leaf_basis,
    transfer,
    near_blocks,
    near_source,
    couple_fine,
    source_fine,
    couple_coarse,
    source_coarse,
    send_fine,
    send_coarse,
):
    leaves = charges.shape[0]
    parents = leaves // 2
    fine_each = send_fine.shape[1] // (2 * REACH)
    coarse_each = send_coarse.shape[1] // (2 * REACH)
    axis = ("leaf", "couple")
    basis_t = leaf_basis.T
    transfer_t = transfer.T
    packets = upward(
        charges, basis_t, transfer_t, send_fine[0], send_coarse[0], fine_each, coarse_each, True
    )
    fine_coeffs, coarse_coeffs = upward(
        charges, basis_t, transfer_t, send_fine[0], send_coarse[0], fine_each, coarse_each, False
    )
    incoming = []
    for slot, offset in enumerate(offset_list()):
        incoming.append(from_behind(packets[slot], axis, offset))

    each = fine_each + coarse_each
    near_field = gather_dot(
        near_source,
        near_blocks,
        [(incoming[0], 0, HALO, each), (charges, HALO, leaves, 0), (incoming[1], HALO + leaves, HALO, each)],
        near_source.shape[0] // leaves,
    )

    coarse_segments = [(coarse_coeffs, 0, parents, 0)]
    for slot in range(2 * REACH):
        coarse_segments.append((incoming[slot], parents + slot * coarse_each, coarse_each, fine_each))
    fine_segments = [(fine_coeffs, 0, leaves, 0)]
    for slot in range(2 * REACH):
        fine_segments.append((incoming[slot], leaves + slot * fine_each, fine_each, 0))
    return coupled_product(
        (source_coarse, couple_coarse, coarse_segments, source_coarse.shape[0] // parents),
        (source_fine, couple_fine, fine_segments, source_fine.shape[0] // leaves),
        transfer,
        leaf_basis,
        near_field,
    )


def solution(mesh):
    return jax.shard_map(
        on_device,
        mesh=mesh,
        in_specs=(
            P(("leaf", "couple"), None, None),
            P(("leaf", "couple"), None),
            P(("leaf", "couple"), None),
            P(("leaf", "couple"), None),
            P(("leaf", "couple")),
            P(("leaf", "couple"), None),
            P(("leaf", "couple")),
            P(("leaf", "couple"), None),
            P(("leaf", "couple")),
            P(("leaf", "couple"), None),
            P(("leaf", "couple"), None),
        ),
        out_specs=P(("leaf", "couple"), None, None),
        check_vma=False,
    )
```

```python
import functools

import jax
import jax.numpy as jnp
from jax import lax
from jax.experimental import pallas as pl
from jax.experimental.pallas import tpu as pltpu
from jax.sharding import PartitionSpec as P

LEAF = 64
RANK = 64
RHS = 128
HALO = 4
REACH = 3
BLOCK_TARGETS = 16


def from_behind(value, axis, steps):
    count = lax.axis_size(axis)
    first, last = (max(0, -steps), min(count, count - steps))
    return lax.ppermute(value, axis, [(source, source + steps) for source in range(first, last)])


def halo_pieces(block, axis, width):
    count = lax.axis_size(axis)
    forward = [(i, i + 1) for i in range(count - 1)]
    backward = [(target, source) for source, target in forward]
    low = lax.ppermute(lax.slice_in_dim(block, block.shape[0] - width, None, axis=0), axis, forward)
    high = lax.ppermute(lax.slice_in_dim(block, 0, width, axis=0), axis, backward)
    return low, high


def offset_list():
    values = []
    for step in range(REACH):
        values.append(step + 1)
        values.append(-(step + 1))
    return values


def gather_dot(idx, mats, segments, pairs, epilogue=None, out_dtype=jnp.float32):
    rows = mats.shape[0]
    width = mats.shape[1] // pairs
    targets = rows // LEAF
    tb = min(BLOCK_TARGETS, targets)
    steps = targets // tb
    n_seg = len(segments)
    seg_arrays = [s[0] for s in segments]
    seg_meta = [(s[1], s[2], s[3]) for s in segments]
    total = sum(s[2] for s in segments)

    in_specs = [pl.BlockSpec((tb * LEAF, pairs * width), lambda i, ix: (i, 0))]
    for arr in seg_arrays:
        in_specs.append(pl.BlockSpec(memory_space=pl.ANY))
    extra = []
    if epilogue is not None:
        extra, extra_specs, _, out_dtype = epilogue
        in_specs.extend(extra_specs)

    def kernel(idx_ref, mats_ref, *refs):
        seg_refs = refs[:n_seg]
        extra_refs = refs[n_seg:len(refs) - 4]
        out_ref, pool_ref, sem, acc_ref = refs[len(refs) - 4:]
        blk = pl.program_id(0)

        @pl.when(blk == 0)
        def _():
            copies = []
            for j, (ref, (lo, cnt, row)) in enumerate(zip(seg_refs, seg_meta)):
                cp = pltpu.make_async_copy(ref.at[pl.ds(row, cnt)], pool_ref.at[pl.ds(lo, cnt)], sem.at[j])
                cp.start()
                copies.append(cp)
            for cp in copies:
                cp.wait()

        for tt in range(tb):
            base = (blk * tb + tt) * pairs
            blocks = [pool_ref[idx_ref[base + k]] for k in range(pairs)]
            rhs = jnp.concatenate(blocks, axis=0)
            acc = jnp.dot(mats_ref[tt * LEAF:(tt + 1) * LEAF, :], rhs, preferred_element_type=jnp.float32)
            if epilogue is None:
                out_ref[tt] = acc.astype(out_dtype)
            else:
                acc_ref[tt] = acc
        if epilogue is not None:
            epilogue[2](tb, acc_ref, extra_refs, out_ref)

    grid_spec = pltpu.PrefetchScalarGridSpec(
        num_scalar_prefetch=1,
        grid=(steps,),
        in_specs=in_specs,
        out_specs=pl.BlockSpec((tb, LEAF, RHS), lambda i, ix: (i, 0, 0)),
        scratch_shapes=[
            pltpu.VMEM((total, width, RHS), jnp.bfloat16),
            pltpu.SemaphoreType.DMA((n_seg,)),
            pltpu.VMEM((tb if epilogue is not None else 1, LEAF, RHS), jnp.float32),
        ],
    )
    flops = 2 * rows * pairs * width * RHS
    bytes_accessed = mats.size * 2 + total * width * RHS * 2 + targets * LEAF * RHS * 4
    return pl.pallas_call(
        kernel,
        grid_spec=grid_spec,
        out_shape=jax.ShapeDtypeStruct((targets, LEAF, RHS), out_dtype),
        compiler_params=pltpu.CompilerParams(dimension_semantics=("arbitrary",)),
        cost_estimate=pl.CostEstimate(flops=flops, transcendentals=0, bytes_accessed=bytes_accessed),
    )(idx, mats, *seg_arrays, *extra)


def upward(charges, basis_t, transfer_t, send_fine, send_coarse, fine_each, coarse_each, packets):
    leaves = charges.shape[0]
    parents = leaves // 2
    slots = 2 * REACH
    each = fine_each + coarse_each
    sizes = [each + (HALO if q < 2 else 0) for q in range(slots)]
    chunks = 4 if parents % 4 == 0 else 1
    per = parents // chunks

    def kernel(sf_ref, sc_ref, x_ref, v_ref, e_ref, *rest):
        n_out = slots if packets else 2
        outs = rest[:n_out]
        fine_v, coarse_v = rest[n_out:n_out + 2]
        bufs = rest[n_out + 2:len(rest) - 1]
        sem = rest[len(rest) - 1]
        for c in range(chunks):
            for j in range(c * per, (c + 1) * per):
                col = j * 2 * RANK
                f0 = jnp.dot(v_ref[:, col:col + RANK], x_ref[2 * j], preferred_element_type=jnp.float32)
                f1 = jnp.dot(v_ref[:, col + RANK:col + 2 * RANK], x_ref[2 * j + 1], preferred_element_type=jnp.float32)
                pair = jnp.concatenate([f0.astype(jnp.bfloat16), f1.astype(jnp.bfloat16)], axis=0)
                fine_v[2 * j] = pair[:RANK]
                fine_v[2 * j + 1] = pair[RANK:]
                e = e_ref[:, col:col + 2 * RANK]
                coarse_v[j] = jnp.dot(e, pair, preferred_element_type=jnp.float32).astype(jnp.bfloat16)

        copies = []
        if not packets:
            copies = [
                pltpu.make_async_copy(fine_v, outs[0], sem.at[0]),
                pltpu.make_async_copy(coarse_v, outs[1], sem.at[1]),
            ]
            for cp in copies:
                cp.start()
        else:
            for q in range(slots):
                buf = bufs[q]
                for m in range(fine_each):
                    buf[m] = fine_v[sf_ref[q * fine_each + m]]
                for m in range(coarse_each):
                    buf[fine_each + m] = coarse_v[sc_ref[q * coarse_each + m]]
                if q == 0:
                    buf[each:each + HALO] = x_ref[leaves - HALO:leaves]
                elif q == 1:
                    buf[each:each + HALO] = x_ref[0:HALO]
                cp = pltpu.make_async_copy(buf, outs[q], sem.at[q])
                cp.start()
                copies.append(cp)
        for cp in copies:
            cp.wait()

    smem = pl.BlockSpec(memory_space=pltpu.SMEM)
    vmem = pl.BlockSpec(memory_space=pltpu.VMEM)
    hbm = pl.BlockSpec(memory_space=pl.ANY)
    block = jax.ShapeDtypeStruct
    if packets:
        out_shape = [block((n, RANK, RHS), jnp.bfloat16) for n in sizes]
        bufs = [pltpu.VMEM((n, RANK, RHS), jnp.bfloat16) for n in sizes]
    else:
        out_shape = [block((leaves, RANK, RHS), jnp.bfloat16), block((parents, RANK, RHS), jnp.bfloat16)]
        bufs = []
    return pl.pallas_call(
        kernel,
        in_specs=[smem, smem, vmem, vmem, vmem],
        out_specs=[hbm] * len(out_shape),
        out_shape=out_shape,
        scratch_shapes=[
            pltpu.VMEM((leaves, RANK, RHS), jnp.bfloat16),
            pltpu.VMEM((parents, RANK, RHS), jnp.bfloat16),
        ]
        + bufs
        + [pltpu.SemaphoreType.DMA((len(out_shape),))],
        cost_estimate=pl.CostEstimate(
            flops=2 * leaves * LEAF * RANK * RHS * 2, transcendentals=0, bytes_accessed=8 * 2 ** 20
        ),
    )(send_fine, send_coarse, charges, basis_t, transfer_t)


def coupled_product(coarse_part, fine_part, transfer, leaf_basis, near_field):
    c_idx, c_mats, c_segs, c_pairs = coarse_part
    f_idx, f_mats, f_segs, f_pairs = fine_part
    width = RANK
    parents = c_mats.shape[0] // RANK
    leaves = f_mats.shape[0] // LEAF
    tb = min(BLOCK_TARGETS, leaves)
    steps = leaves // tb
    halves = 4 if parents % 4 == 0 else 1
    c_rows = parents * RANK // halves
    c_total = sum(s[2] for s in c_segs)
    f_total = sum(s[2] for s in f_segs)
    segs = c_segs + f_segs
    n_c = len(c_segs)
    n_seg = len(segs)

    hbm = pl.BlockSpec(memory_space=pl.ANY)
    in_specs = [hbm] + [pl.BlockSpec((tb * LEAF, f_pairs * width), lambda i, a, b: (i, 0))]
    in_specs += [hbm] * n_seg
    in_specs += [
        pl.BlockSpec((tb * RANK, RANK), lambda i, a, b: (i, 0)),
        pl.BlockSpec((tb * LEAF, RANK), lambda i, a, b: (i, 0)),
        pl.BlockSpec((tb, LEAF, RHS), lambda i, a, b: (i, 0, 0)),
    ]

    def gather_sum(idx_ref, pool_ref, mats, base, pairs):
        blocks = [pool_ref[idx_ref[base + k]] for k in range(pairs)]
        return jnp.dot(mats, jnp.concatenate(blocks, axis=0), preferred_element_type=jnp.float32)

    def kernel(ci_ref, fi_ref, cm_hbm, fm_ref, *refs):
        seg_refs = refs[:n_seg]
        e_ref, v_ref, near_ref, out_ref = refs[n_seg:n_seg + 4]
        c_pool, f_pool, c_mats_v, cr_ref, acc_ref, sem = refs[n_seg + 4:]
        blk = pl.program_id(0)

        @pl.when(blk == 0)
        def _():
            seg_copies = []
            for j, (ref, (_, lo, cnt, row)) in enumerate(zip(seg_refs, segs)):
                pool = c_pool if j < n_c else f_pool
                seg_copies.append(
                    pltpu.make_async_copy(ref.at[pl.ds(row, cnt)], pool.at[pl.ds(lo, cnt)], sem.at[j])
                )
            for cp in seg_copies[:n_c]:
                cp.start()
            mat_copies = []
            for h in range(halves):
                cp = pltpu.make_async_copy(
                    cm_hbm.at[pl.ds(h * c_rows, c_rows)], c_mats_v.at[pl.ds(h * c_rows, c_rows)], sem.at[n_seg + h]
                )
                cp.start()
                mat_copies.append(cp)
            for cp in seg_copies[:n_c]:
                cp.wait()
            per_half = parents // halves
            for h in range(halves):
                mat_copies[h].wait()
                if h == min(1, halves - 1):
                    for cp in seg_copies[n_c:]:
                        cp.start()
                for p in range(h * per_half, (h + 1) * per_half):
                    acc = gather_sum(ci_ref, c_pool, c_mats_v[p * RANK:(p + 1) * RANK, :], p * c_pairs, c_pairs)
                    cr_ref[p] = acc.astype(jnp.bfloat16)
            for cp in seg_copies[n_c:]:
                cp.wait()

        for tt in range(tb):
            base = (blk * tb + tt) * f_pairs
            acc_ref[tt] = gather_sum(fi_ref, f_pool, fm_ref[tt * LEAF:(tt + 1) * LEAF, :], base, f_pairs)
        rounded = []
        for j in range(tb // 2):
            e = e_ref[2 * j * RANK:(2 * j + 2) * RANK, :]
            down = jnp.dot(e, cr_ref[blk * (tb // 2) + j], preferred_element_type=jnp.float32)
            for h in range(2):
                rounded.append((acc_ref[2 * j + h] + down[h * RANK:(h + 1) * RANK]).astype(jnp.bfloat16))
        for tt in range(tb):
            v = v_ref[tt * LEAF:(tt + 1) * LEAF, :]
            far = jnp.dot(v, rounded[tt], preferred_element_type=jnp.float32)
            out_ref[tt] = (far + near_ref[tt]).astype(jnp.bfloat16)

    grid_spec = pltpu.PrefetchScalarGridSpec(
        num_scalar_prefetch=2,
        grid=(steps,),
        in_specs=in_specs,
        out_specs=pl.BlockSpec((tb, LEAF, RHS), lambda i, a, b: (i, 0, 0)),
        scratch_shapes=[
            pltpu.VMEM((c_total, width, RHS), jnp.bfloat16),
            pltpu.VMEM((f_total, width, RHS), jnp.bfloat16),
            pltpu.VMEM(c_mats.shape, jnp.bfloat16),
            pltpu.VMEM((parents, RANK, RHS), jnp.bfloat16),
            pltpu.VMEM((tb, LEAF, RHS), jnp.float32),
            pltpu.SemaphoreType.DMA((n_seg + halves,)),
        ],
    )
    flops = 2 * (c_mats.size + f_mats.size) * RHS
    bytes_accessed = (c_mats.size + f_mats.size) * 2 + (c_total + f_total) * width * RHS * 2
    return pl.pallas_call(
        kernel,
        grid_spec=grid_spec,
        out_shape=jax.ShapeDtypeStruct((leaves, LEAF, RHS), jnp.bfloat16),
        compiler_params=pltpu.CompilerParams(dimension_semantics=("arbitrary",)),
        cost_estimate=pl.CostEstimate(flops=flops, transcendentals=0, bytes_accessed=bytes_accessed),
    )(c_idx, f_idx, c_mats, f_mats, *[s[0] for s in segs], transfer, leaf_basis, near_field)


def on_device(
    charges,
    leaf_basis,
    transfer,
    near_blocks,
    near_source,
    couple_fine,
    source_fine,
    couple_coarse,
    source_coarse,
    send_fine,
    send_coarse,
):
    leaves = charges.shape[0]
    parents = leaves // 2
    fine_each = send_fine.shape[1] // (2 * REACH)
    coarse_each = send_coarse.shape[1] // (2 * REACH)
    axis = ("leaf", "couple")
    basis_t = leaf_basis.T
    transfer_t = transfer.T
    packets = upward(
        charges, basis_t, transfer_t, send_fine[0], send_coarse[0], fine_each, coarse_each, True
    )
    fine_coeffs, coarse_coeffs = upward(
        charges, basis_t, transfer_t, send_fine[0], send_coarse[0], fine_each, coarse_each, False
    )
    incoming = []
    for slot, offset in enumerate(offset_list()):
        incoming.append(from_behind(packets[slot], axis, offset))

    each = fine_each + coarse_each
    near_field = gather_dot(
        near_source,
        near_blocks,
        [(incoming[0], 0, HALO, each), (charges, HALO, leaves, 0), (incoming[1], HALO + leaves, HALO, each)],
        near_source.shape[0] // leaves,
    )

    coarse_segments = [(coarse_coeffs, 0, parents, 0)]
    for slot in range(2 * REACH):
        coarse_segments.append((incoming[slot], parents + slot * coarse_each, coarse_each, fine_each))
    fine_segments = [(fine_coeffs, 0, leaves, 0)]
    for slot in range(2 * REACH):
        fine_segments.append((incoming[slot], leaves + slot * fine_each, fine_each, 0))
    return coupled_product(
        (source_coarse, couple_coarse, coarse_segments, source_coarse.shape[0] // parents),
        (source_fine, couple_fine, fine_segments, source_fine.shape[0] // leaves),
        transfer,
        leaf_basis,
        near_field,
    )


def solution(mesh):
    return jax.shard_map(
        on_device,
        mesh=mesh,
        in_specs=(
            P(("leaf", "couple"), None, None),
            P(("leaf", "couple"), None),
            P(("leaf", "couple"), None),
            P(("leaf", "couple"), None),
            P(("leaf", "couple")),
            P(("leaf", "couple"), None),
            P(("leaf", "couple")),
            P(("leaf", "couple"), None),
            P(("leaf", "couple")),
            P(("leaf", "couple"), None),
            P(("leaf", "couple"), None),
        ),
        out_specs=P(("leaf", "couple"), None, None),
        check_vma=False,
    )
```
